32 devices in a mesh: gx: 4 (over y, x), gz: 8 (over z, core).
Axes of the slice: x: 2, y: 2, z: 4, core: 2. Of those that a mesh axis runs over, the one named last changes fastest.
Arguments:
- theta: float32 [152, 256, 512], P(None, 'gz', 'gx'), may hold values from -5 to 5
- section_store: float32 [152, 256, 512], P(None, 'gz', 'gx'), may hold values from -3 to 3
- stream_speed: bfloat16 [152, 256, 512], P(None, 'gz', 'gx'), may hold values from 0.19921875 to 1.1953125
- span_speed: bfloat16 [152, 256, 512], P(None, 'gz', 'gx'), may hold values from -2.5 to 2.5
- conductivity: float32 [2, 152], replicated, may hold values from 0.05 to 0.5
- wall_layers: int32 [256], P('gz'), may hold values from 32 to 47
- contact: int32 [512], P('gx'), may hold values 0 or 1
- spanwise_number: float32 [32], replicated, may hold values from 3072 to 6144
- block_inverse: float32 [32, 31, 31], replicated, may hold values from 0 to 1, as said below
Outputs:
- theta_new: float32 [152, 256, 512], P(None, 'gz', 'gx')
- section_new: float32 [152, 256, 512], P(None, 'gz', 'gx')
The draws below stay inside these ranges and needn't reach their ends.
Inputs may be any that keep to these rules, and one draw needn't show every extreme that they name: block_inverse[l] is the symmetric inverse of the 31-square tridiagonal matrix with 1 + 2 spanwise_number[l] on its diagonal and -spanwise_number[l] beside it.
All inputs are finite; a program needn't handle non-finite values. No bound on the sum of `contact` on one device may be relied on, other than what follows from the above.
Results may differ from the reference program's by a relative error of at most 0.0003.
Values sent between devices are 32-bit elements; how exact they have to be, the bound alone decides.
No kernel may reach another device: no remote copies, remote signals or barrier semaphores. Data moves between devices by JAX's collectives and lax.ppermute only.
A program may use at most 64 MiB of HBM per device.

```python
import math
import jax
import jax.numpy as jnp
from jax import lax

NF = 120
NS = 32
CZ = 32
NY = 152
NX = 512
NZ = 256


def spanwise_law(key):
    law_key = jax.random.fold_in(key, 11)
    uniform_draw = jax.random.uniform(law_key, (NS,), jnp.float32)
    return 3.0 * CZ * CZ * jnp.exp(uniform_draw * math.log(2.0))


def draw_spanwise_number(key, part):
    return spanwise_law(key)


def inverse_sinh(value):
    squared = value * value
    return jnp.log1p(value + squared / (1.0 + jnp.sqrt(1.0 + squared)))


def draw_block_inverse(key, part):
    number = spanwise_law(key)
    angle = 2.0 * inverse_sinh(0.5 / jnp.sqrt(number))
    order = CZ - 1
    positions = jnp.arange(1, order + 1, dtype=jnp.float32)
    low_index = jnp.minimum(positions[:, None], positions[None, :])
    high_index = jnp.maximum(positions[:, None], positions[None, :])
    angle = angle[:, None, None]
    numerator = jnp.sinh(low_index[None] * angle) * jnp.sinh((order + 1 - high_index[None]) * angle)
    return numerator / (number[:, None, None] * jnp.sinh(angle) * jnp.sinh((order + 1) * angle))


def draw_theta(key, part):
    full_shape = (NY, NZ, NX)
    return jnp.clip(jax.random.normal(key, full_shape, jnp.float32), -5.0, 5.0)


def touch_ends(values, own_key, least, largest):
    longest = values.shape.index(max(values.shape))
    spots = []
    for shift in (0, 1):
        where = [jax.random.randint(jax.random.fold_in(own_key, axis), (), 0, length) for axis, length in enumerate(values.shape)]
        where[longest] = (where[longest] + shift) % values.shape[longest]
        spots.append(tuple(where))
    return values.at[spots[0]].set(least).at[spots[1]].set(largest)


def shard_levels(stream_key, shape, cuts, smallest, largest):
    def one(axis_at, blocks):
        steps = jax.random.uniform(jax.random.fold_in(jax.random.fold_in(stream_key, 6), axis_at), (blocks,), jnp.float32, smallest / len(cuts), largest / len(cuts))
        return jnp.repeat(jnp.exp(steps), shape[axis_at] // blocks).reshape((-1,) + (1,) * (len(shape) - axis_at - 1))

    factor_of = one(*cuts[0])
    for cut in cuts[1:]:
        factor_of = factor_of * one(*cut)
    return factor_of


def normal_values(own_key, shape, scale, reach, cuts=(), held_as=jnp.bfloat16):
    gain = shard_levels(own_key, shape, cuts, -0.22, 0.18) if cuts else 1.0
    drawn = jax.random.normal(own_key, shape, jnp.float32) * scale * gain
    return jnp.minimum(jnp.maximum(drawn, -reach), reach).astype(held_as)


def setup_inputs(seed: int = 0) -> dict:
    arg_keys = jax.random.split(jax.random.key(seed), 10)
    return {
        "theta": draw_theta(jax.random.fold_in(arg_keys[9], 71), 0),
        "section_store": normal_values(arg_keys[1], (NY, NZ, NX), 0.5, 3.0, ((1, 8), (2, 4)), jnp.float32),
        "stream_speed": jnp.clip(0.19921875 + 0.99609375 * jax.random.uniform(arg_keys[2], (NY, NZ, NX), jnp.float32) ** shard_levels(arg_keys[2], (NY, NZ, NX), ((1, 8), (2, 4)), -0.2, 0.2), 0.19921875, 1.1953125).astype(jnp.bfloat16),
        "span_speed": normal_values(arg_keys[3], (NY, NZ, NX), 0.5, 2.5, ((1, 8), (2, 4))),
        "conductivity": jnp.clip(jnp.exp(jax.random.uniform(arg_keys[4], (2, NY), jnp.float32, math.log(0.05), math.log(0.5))), 0.05, 0.5),
        "wall_layers": touch_ends(jax.random.randint(arg_keys[5], (NZ,), NS, NS + NF // 8 + 1), jax.random.fold_in(arg_keys[5], 1), NS, (NS + NF // 8 + 1) - 1).astype(jnp.int32),
        "contact": touch_ends((jax.random.randint(arg_keys[6], (NX,), 0, 2) < 1).astype(jnp.int32), jax.random.fold_in(arg_keys[6], 1), 0, 1),
        "spanwise_number": draw_spanwise_number(jax.random.fold_in(arg_keys[9], 71), 0),
        "block_inverse": draw_block_inverse(jax.random.fold_in(arg_keys[9], 71), 0),
    }


keep_factor = -5.0 / 9.0
section_weight = 15.0 / 16.0
stream_courant = 0.4
span_courant = 0.4
damping = 1.0 / 256.0
slope_weights = (-1.0, 9.0, -45.0, 0.0, 45.0, -9.0, 1.0)
smooth_weights = (1.0, -8.0, 28.0, -56.0, 70.0, -56.0, 28.0, -8.0, 1.0)


def stencil(padded, along, length, weights, first_offset):
    running = jnp.zeros_like(lax.slice_in_dim(padded, 0, length, axis=along))
    for offset, weight in enumerate(weights):
        if weight != 0.0:
            begin = first_offset + offset
            running = running + weight * lax.slice_in_dim(padded, begin, begin + length, axis=along)
    return running


def horizontal_term(span_pad, stream_pad, stream_speed, span_speed):
    span_length = stream_pad.shape[1]
    stream_length = span_pad.shape[2]
    span_slope = stencil(span_pad, 1, span_length, slope_weights, 1) / 60.0
    stream_slope = stencil(stream_pad, 2, stream_length, slope_weights, 1) / 60.0
    smoothing = stencil(span_pad, 1, span_length, smooth_weights, 0) + stencil(stream_pad, 2, stream_length, smooth_weights, 0)
    return (-stream_courant * stream_speed.astype(jnp.float32) * stream_slope
            - span_courant * span_speed.astype(jnp.float32) * span_slope
            - damping * smoothing)


def normal_term(theta, conductivity, wall_layers, contact):
    layer_index = jnp.arange(theta.shape[0], dtype=jnp.int32)[:, None]
    solid_cell = layer_index < wall_layers[None, :]
    cell_cond = jnp.where(solid_cell, conductivity[0][:, None], conductivity[1][:, None])
    face_cond = 2.0 * cell_cond[:-1] * cell_cond[1:] / (cell_cond[:-1] + cell_cond[1:])
    at_wall = layer_index[:-1] == wall_layers[None, :] - 1
    contact_float = contact.astype(jnp.float32)
    face_full = jnp.where(at_wall[:, :, None], face_cond[:, :, None] * contact_float[None, None, :], face_cond[:, :, None])
    face_flux = face_full * (theta[1:] - theta[:-1])
    border = jnp.zeros((1,) + theta.shape[1:], jnp.float32)
    return jnp.concatenate([face_flux, border], 0) - jnp.concatenate([border, face_flux], 0)


def solve_substrate(advanced, number, inverse):
    layers, span_total, stream_total = advanced.shape
    block_width = inverse.shape[1] + 1
    group_count = span_total // block_width
    blocks = advanced.reshape(layers, group_count, block_width, stream_total)
    interior = jnp.einsum("lij,lkjx->lkix", inverse, blocks[:, :, 1:, :], precision=lax.Precision.HIGHEST)
    number_scale = number[:, None, None]
    target = blocks[:, :, 0, :] + number_scale * jnp.roll(interior[:, :, -1, :], 1, axis=1) + number_scale * interior[:, :, 0, :]
    square = number * number
    diagonal = 1.0 + 2.0 * number - square * (inverse[:, 0, 0] + inverse[:, -1, -1])
    beside = square * inverse[:, 0, -1]
    frequency = 2.0 * math.pi * jnp.arange(group_count // 2 + 1, dtype=jnp.float32) / group_count
    denominator = diagonal[:, None] - 2.0 * beside[:, None] * jnp.cos(frequency)[None, :]
    head_values = jnp.fft.irfft(jnp.fft.rfft(target, axis=1) / denominator[:, :, None], n=group_count, axis=1)
    following = jnp.roll(head_values, -1, axis=1)
    interior = interior + number_scale[..., None] * (inverse[:, None, :, 0, None] * head_values[:, :, None, :]
                                                     + inverse[:, None, :, -1, None] * following[:, :, None, :])
    whole_block = jnp.concatenate([head_values[:, :, None, :], interior], 2)
    return whole_block.reshape(layers, span_total, stream_total)


def expand(array):
    return array.reshape((array.shape[0], 1) + array.shape[1:])


def one_layer(pieces):
    layer_theta, layer_stream, layer_span = pieces
    span_pad = jnp.concatenate([layer_theta[:, -4:], layer_theta, layer_theta[:, :4]], 1)
    stream_pad = jnp.pad(layer_theta, ((0, 0), (0, 0), (4, 4)))
    return horizontal_term(span_pad, stream_pad, layer_stream, layer_span)


def reference(theta, section_store, stream_speed, span_speed, conductivity, wall_layers, contact, spanwise_number, block_inverse):
    solid_count = block_inverse.shape[0]
    fluid_theta = theta[solid_count:]
    across = lax.map(one_layer, (expand(fluid_theta), expand(stream_speed[solid_count:]), expand(span_speed[solid_count:])))
    across = across.reshape(fluid_theta.shape)
    layer_index = jnp.arange(solid_count, theta.shape[0], dtype=jnp.int32)[:, None, None]
    fluid_mask = layer_index >= wall_layers[None, :, None]
    across = jnp.where(fluid_mask, across, 0.0)
    section_rate = normal_term(theta, conductivity, wall_layers, contact) + jnp.concatenate([jnp.zeros_like(theta[:solid_count]), across], 0)
    section_new = keep_factor * section_store + section_rate
    advanced = theta + section_weight * section_new
    substrate = solve_substrate(advanced[:solid_count], spanwise_number, block_inverse)
    theta_new = jnp.concatenate([substrate, advanced[solid_count:]], 0)
    return theta_new, section_new
```

```python
import math

import jax
import jax.numpy as jnp
from jax import lax
from jax.experimental import pallas as pl
from jax.experimental.pallas import tpu as pltpu
from jax.sharding import PartitionSpec as P

keep_factor = -5.0 / 9.0
section_weight = 15.0 / 16.0
stream_courant = 0.4
span_courant = 0.4
damping = 1.0 / 256.0

LB = 8


def pack_kernel(th_ref, xl_ref, xr_ref, zl_ref, zr_ref):
    _, cz, w = th_ref.shape
    i = pl.program_id(0)
    lane = lax.broadcasted_iota(jnp.int32, (cz, w), 1)
    sub8 = lax.broadcasted_iota(jnp.int32, (8, w), 0)

    @pl.when(i % 4 == 0)
    def _():
        xl_ref[...] = jnp.zeros_like(xl_ref)
        xr_ref[...] = jnp.zeros_like(xr_ref)

    acc_l = xl_ref[0]
    acc_r = xr_ref[0]
    for s in range(LB):
        t = th_ref[s]
        slot = (i % 4) * LB + s
        pick = (lane // 4) == slot
        acc_l = jnp.where(pick, pltpu.roll(t, (4 * slot) % w, 1), acc_l)
        acc_r = jnp.where(pick, pltpu.roll(t, (4 * slot + 4) % w, 1), acc_r)
    xl_ref[0] = acc_l
    xr_ref[0] = acc_r
    for p in range(LB // 2):
        a_hi = th_ref[2 * p, cz - 8:cz, :]
        b_hi = th_ref[2 * p + 1, cz - 8:cz, :]
        zl_ref[p] = jnp.where(sub8 < 4, pltpu.roll(a_hi, 4, 0), b_hi)
        a_lo = th_ref[2 * p, 0:8, :]
        b_lo = th_ref[2 * p + 1, 0:8, :]
        zr_ref[p] = jnp.where(sub8 < 4, a_lo, pltpu.roll(b_lo, 4, 0))


def layer_kernel(fluid, block_offset, ny, *refs):
    if fluid:
        (cond_ref, th_ref, prev_ref, next_ref, st_ref, wall_ref, contact_ref,
         u_ref, v_ref, zb_ref, za_ref, xb_ref, xa_ref, _alias_ref,
         sn_ref, tn_ref) = refs
    else:
        (cond_ref, th_ref, prev_ref, next_ref, st_ref, wall_ref, contact_ref,
         bs_ref, sn_ref, int_ref, head_ref) = refs
    _, cz, w = th_ref.shape
    base = (pl.program_id(0) + block_offset) * LB
    wall = wall_ref[...]
    contact = contact_ref[...]

    def cell(y):
        return jnp.where(y < wall, cond_ref[0, y], cond_ref[1, y])

    def face(y):
        yc = jnp.clip(y, 0, ny - 2)
        a = cell(yc)
        b = cell(yc + 1)
        f = 2.0 * a * b / (a + b)
        f = jnp.where(yc == wall - 1, f * contact, f)
        valid = jnp.logical_and(y >= 0, y <= ny - 2)
        return jnp.where(valid, f, 0.0)

    if fluid:
        lane = lax.broadcasted_iota(jnp.int32, (cz, w), 1)
        sub8 = lax.broadcasted_iota(jnp.int32, (8, w), 0)

    heads = []
    face_dn = face(base - 1)
    for s in range(LB):
        y = base + s
        t = th_ref[s]
        tp = th_ref[s - 1] if s > 0 else prev_ref[0]
        tn = th_ref[s + 1] if s < LB - 1 else next_ref[0]
        face_up = face(y)
        normal = face_up * (tn - t) - face_dn * (t - tp)
        face_dn = face_up
        if fluid:
            u = u_ref[s].astype(jnp.float32)
            v = v_ref[s].astype(jnp.float32)
            slot = (pl.program_id(0) % 4) * LB + s
            edge_b = xb_ref[0]
            edge_a = xa_ref[0]
            xm = [None]
            xp = [None]
            for j in range(1, 5):
                xm.append(jnp.where(lane < j, pltpu.roll(edge_b, (w - 4 - 4 * slot + j) % w, 1),
                                    pltpu.roll(t, j, 1)))
                xp.append(jnp.where(lane >= w - j, pltpu.roll(edge_a, (w - j - 4 * slot) % w, 1),
                                    pltpu.roll(t, w - j, 1)))
            packed_b = zb_ref[s // 2]
            packed_a = za_ref[s // 2]
            if s % 2 == 0:
                zb8 = pltpu.roll(packed_b, 4, 0)
                za8 = packed_a
            else:
                zb8 = packed_b
                za8 = pltpu.roll(packed_a, 4, 0)
            zm = [None]
            zp = [None]
            for j in range(1, 5):
                r = pltpu.roll(t, j, 0)
                first = jnp.where(sub8 < j, pltpu.roll(zb8, j, 0), r[0:8])
                zm.append(jnp.concatenate([first, r[8:]], axis=0))
                r = pltpu.roll(t, cz - j, 0)
                last = jnp.where(sub8 >= 8 - j, pltpu.roll(za8, 8 - j, 0), r[cz - 8:])
                zp.append(jnp.concatenate([r[:cz - 8], last], axis=0))

            def slope(m, p):
                acc = -1.0 * m[3] + 9.0 * m[2]
                acc = acc + -45.0 * m[1]
                acc = acc + 45.0 * p[1]
                acc = acc + -9.0 * p[2]
                acc = acc + p[3]
                return acc / 60.0

            def smooth(m, p):
                acc = m[4] + -8.0 * m[3]
                acc = acc + 28.0 * m[2]
                acc = acc + -56.0 * m[1]
                acc = acc + 70.0 * t
                acc = acc + -56.0 * p[1]
                acc = acc + 28.0 * p[2]
                acc = acc + -8.0 * p[3]
                acc = acc + p[4]
                return acc

            span_slope = slope(zm, zp)
            stream_slope = slope(xm, xp)
            smoothing = smooth(zm, zp) + smooth(xm, xp)
            horiz = (-stream_courant * u * stream_slope
                     - span_courant * v * span_slope
                     - damping * smoothing)
            across = jnp.where(y >= wall, horiz, 0.0)
            rate = normal + across
        else:
            rate = normal
        sn = keep_factor * st_ref[s] + rate
        adv = t + section_weight * sn
        sn_ref[s] = sn
        if fluid:
            tn_ref[s] = adv
        else:
            int_ref[s] = jnp.dot(bs_ref[s], adv, precision=lax.Precision.HIGHEST,
                                 preferred_element_type=jnp.float32)
            heads.append(adv[0:1, :])
    if not fluid:
        head_ref[...] = jnp.concatenate(heads, axis=0)


def local(theta, section_store, stream_speed, span_speed, conductivity, wall_layers,
          contact, spanwise_number, block_inverse):
    f32 = jnp.float32
    ny, cz, w = theta.shape
    ns = block_inverse.shape[0]
    nf = ny - ns
    nsb = ns // LB
    nfb = nf // LB
    groups = (nfb + 3) // 4
    ngz = lax.axis_size("gz")
    ngx = lax.axis_size("gx")
    k = lax.axis_index("gz")

    wall2 = jnp.broadcast_to(wall_layers[:, None], (cz, w)).astype(jnp.int32)
    contact2 = jnp.broadcast_to(contact.astype(f32)[None, :], (cz, w))

    smem = pl.BlockSpec(memory_space=pltpu.SMEM)
    blk = lambda off: pl.BlockSpec((LB, cz, w), lambda i: (i + off, 0, 0))
    prev_spec = lambda off: pl.BlockSpec((1, cz, w), lambda i: (jnp.maximum((i + off) * LB - 1, 0), 0, 0))
    next_spec = lambda off: pl.BlockSpec((1, cz, w), lambda i: (jnp.minimum((i + off) * LB + LB, ny - 1), 0, 0))
    full2 = pl.BlockSpec((cz, w), lambda i: (0, 0))

    xl, xr, zl, zr = pl.pallas_call(
        pack_kernel,
        grid=(nfb,),
        in_specs=[blk(nsb)],
        out_specs=[
            pl.BlockSpec((1, cz, w), lambda i: (i // 4, 0, 0)),
            pl.BlockSpec((1, cz, w), lambda i: (i // 4, 0, 0)),
            pl.BlockSpec((LB // 2, 8, w), lambda i: (i, 0, 0)),
            pl.BlockSpec((LB // 2, 8, w), lambda i: (i, 0, 0)),
        ],
        out_shape=[
            jax.ShapeDtypeStruct((groups, cz, w), f32),
            jax.ShapeDtypeStruct((groups, cz, w), f32),
            jax.ShapeDtypeStruct((nf // 2, 8, w), f32),
            jax.ShapeDtypeStruct((nf // 2, 8, w), f32),
        ],
    )(theta)

    xb = lax.ppermute(xr, "gx", [(i, i + 1) for i in range(ngx - 1)])
    xa = lax.ppermute(xl, "gx", [(i + 1, i) for i in range(ngx - 1)])
    zb = lax.ppermute(zl, "gz", [(i, (i + 1) % ngz) for i in range(ngz)])
    za = lax.ppermute(zr, "gz", [((i + 1) % ngz, i) for i in range(ngz)])

    shifted_inverse = jnp.zeros((ns, cz, cz), f32).at[:, 1:, 1:].set(block_inverse)

    sn_part, interior, head = pl.pallas_call(
        lambda *refs: layer_kernel(False, 0, ny, *refs),
        grid=(nsb,),
        in_specs=[smem, blk(0), prev_spec(0), next_spec(0), blk(0), full2, full2,
                  pl.BlockSpec((LB, cz, cz), lambda i: (i, 0, 0))],
        out_specs=[blk(0), blk(0), pl.BlockSpec((LB, w), lambda i: (i, 0))],
        out_shape=[
            jax.ShapeDtypeStruct((ny, cz, w), f32),
            jax.ShapeDtypeStruct((ns, cz, w), f32),
            jax.ShapeDtypeStruct((ns, w), f32),
        ],
    )(conductivity, theta, theta, theta, section_store, wall2, contact2, shifted_inverse)

    number = spanwise_number
    from_left = lax.ppermute(interior[:, cz - 1, :], "gz", [(i, (i + 1) % ngz) for i in range(ngz)])
    target = head + number[:, None] * from_left + number[:, None] * interior[:, 1, :]
    all_targets = lax.all_gather(target, "gz", axis=1, tiled=False)

    square = number * number
    diagonal = 1.0 + 2.0 * number - square * (block_inverse[:, 0, 0] + block_inverse[:, -1, -1])
    beside = square * block_inverse[:, 0, -1]
    q = jnp.arange(ngz, dtype=jnp.int32)
    angle = (2.0 * math.pi / ngz) * q.astype(f32)
    denominator = diagonal[:, None] - 2.0 * beside[:, None] * jnp.cos(angle)[None, :]
    phase = (2.0 * math.pi / ngz) * ((q[:, None] * q[None, :]) % ngz).astype(f32)
    coeff = jnp.sum(jnp.cos(phase)[None, :, :] / denominator[:, :, None], axis=1) / ngz
    own = jnp.take(coeff, (q - k) % ngz, axis=1)
    nxt = jnp.take(coeff, (q - k - 1) % ngz, axis=1)
    head_values = jnp.sum(own[:, :, None] * all_targets, axis=1)
    following = jnp.sum(nxt[:, :, None] * all_targets, axis=1)

    fluid_sn, fluid_tn = pl.pallas_call(
        lambda *refs: layer_kernel(True, nsb, ny, *refs),
        grid=(nfb,),
        in_specs=[smem, blk(nsb), prev_spec(nsb), next_spec(nsb), blk(nsb), full2, full2,
                  blk(nsb), blk(nsb),
                  pl.BlockSpec((LB // 2, 8, w), lambda i: (i, 0, 0)),
                  pl.BlockSpec((LB // 2, 8, w), lambda i: (i, 0, 0)),
                  pl.BlockSpec((1, cz, w), lambda i: (i // 4, 0, 0)),
                  pl.BlockSpec((1, cz, w), lambda i: (i // 4, 0, 0)),
                  pl.BlockSpec(memory_space=pl.ANY)],
        out_specs=[blk(nsb), blk(nsb)],
        out_shape=[
            jax.ShapeDtypeStruct((ny, cz, w), f32),
            jax.ShapeDtypeStruct((ny, cz, w), f32),
        ],
        input_output_aliases={13: 0},
    )(conductivity, theta, theta, theta, section_store, wall2, contact2,
      stream_speed, span_speed, zb, za, xb, xa, sn_part)

    row = jnp.arange(cz, dtype=jnp.int32)
    col0 = jnp.zeros((ns, cz), f32).at[:, 1:].set(block_inverse[:, :, 0])
    col_last = jnp.zeros((ns, cz), f32).at[:, 1:].set(block_inverse[:, :, -1])
    scale = number[:, None, None]
    solved = interior + scale * (col0[:, :, None] * head_values[:, None, :]
                                 + col_last[:, :, None] * following[:, None, :])
    solved = jnp.where((row == 0)[None, :, None], head_values[:, None, :], solved)
    theta_new = lax.dynamic_update_slice_in_dim(fluid_tn, solved, 0, 0)
    return (theta_new, fluid_sn)


def solution(mesh):
    return jax.shard_map(
        local,
        mesh=mesh,
        in_specs=(
            P(None, "gz", "gx"),
            P(None, "gz", "gx"),
            P(None, "gz", "gx"),
            P(None, "gz", "gx"),
            P(),
            P("gz"),
            P("gx"),
            P(),
            P(),
        ),
        out_specs=(P(None, "gz", "gx"), P(None, "gz", "gx")),
        check_vma=False,
    )
```

```python
import math

import jax
import jax.numpy as jnp
from jax import lax
from jax.experimental import pallas as pl
from jax.experimental.pallas import tpu as pltpu
from jax.sharding import PartitionSpec as P

keep_factor = -5.0 / 9.0
section_weight = 15.0 / 16.0
stream_courant = 0.4
span_courant = 0.4
damping = 1.0 / 256.0

LB = 8


def pack_kernel(th_ref, xl_ref, xr_ref, zl_ref, zr_ref):
    _, cz, w = th_ref.shape
    lane8 = lax.broadcasted_iota(jnp.int32, (8, w), 1)
    sub8 = lax.broadcasted_iota(jnp.int32, (8, w), 0)
    acc_l = jnp.zeros((8, w), jnp.float32)
    acc_r = jnp.zeros((8, w), jnp.float32)
    for s in range(LB):
        for v in range(cz // 8):
            t = th_ref[s, 8 * v:8 * v + 8, :]
            pos = 4 * LB * v + 4 * s
            pick = jnp.logical_and(lane8 >= pos, lane8 < pos + 4)
            acc_l = jnp.where(pick, pltpu.roll(t, pos % w, 1), acc_l)
            acc_r = jnp.where(pick, pltpu.roll(t, (pos + 4) % w, 1), acc_r)
    xl_ref[0] = acc_l
    xr_ref[0] = acc_r
    for p in range(LB // 2):
        a_hi = th_ref[2 * p, cz - 8:cz, :]
        b_hi = th_ref[2 * p + 1, cz - 8:cz, :]
        zl_ref[p] = jnp.where(sub8 < 4, pltpu.roll(a_hi, 4, 0), b_hi)
        a_lo = th_ref[2 * p, 0:8, :]
        b_lo = th_ref[2 * p + 1, 0:8, :]
        zr_ref[p] = jnp.where(sub8 < 4, a_lo, pltpu.roll(b_lo, 4, 0))


def layer_kernel(fluid, block_offset, *refs):
    if fluid:
        (face_ref, th_ref, prev_ref, next_ref, st_ref, wall_ref, contact_ref,
         u_ref, v_ref, zb_ref, za_ref, xb_ref, xa_ref, _alias_ref,
         sn_ref, tn_ref, ext_ref) = refs
    else:
        (face_ref, th_ref, prev_ref, next_ref, st_ref, wall_ref, contact_ref,
         bs_ref, sn_ref, int_ref, head_ref) = refs
    _, cz, w = th_ref.shape
    base = (pl.program_id(0) + block_offset) * LB
    wall = wall_ref[...]
    contact = contact_ref[...]

    def face(y):
        both_solid = face_ref[0, y + 1]
        both_fluid = face_ref[2, y + 1]
        at_wall = face_ref[1, y + 1] * contact
        return jnp.where(y + 1 < wall, both_solid, jnp.where(y >= wall, both_fluid, at_wall))

    if fluid:
        lane = lax.broadcasted_iota(jnp.int32, (8, w), 1)
        nv = cz // 8
        slope_scale = -stream_courant / 60.0

    heads = []
    face_dn = face(base - 1)
    for s in range(LB):
        y = base + s
        t = th_ref[s]
        tp = th_ref[s - 1] if s > 0 else prev_ref[0]
        tn = th_ref[s + 1] if s < LB - 1 else next_ref[0]
        face_up = face(y)
        normal = face_up * (tn - t) - face_dn * (t - tp)
        face_dn = face_up
        if fluid:
            u = u_ref[s].astype(jnp.float32)
            v = v_ref[s].astype(jnp.float32)
            edge_b = xb_ref[0]
            edge_a = xa_ref[0]
            xm = [[None] * nv for _ in range(5)]
            xp = [[None] * nv for _ in range(5)]
            for g in range(nv):
                tg = t[8 * g:8 * g + 8]
                pos = 4 * LB * g + 4 * s
                for j in range(1, 5):
                    xm[j][g] = jnp.where(lane < j, pltpu.roll(edge_b, (j - 4 - pos) % w, 1),
                                         pltpu.roll(tg, j, 1))
                    xp[j][g] = jnp.where(lane >= w - j, pltpu.roll(edge_a, (w - j - pos) % w, 1),
                                         pltpu.roll(tg, w - j, 1))
            xm = [None] + [jnp.concatenate(xm[j], axis=0) for j in range(1, 5)]
            xp = [None] + [jnp.concatenate(xp[j], axis=0) for j in range(1, 5)]
            packed_b = zb_ref[s // 2]
            packed_a = za_ref[s // 2]
            if s % 2 == 0:
                packed_b = pltpu.roll(packed_b, 4, 0)
            else:
                packed_a = pltpu.roll(packed_a, 4, 0)
            ext_ref[0:8, :] = packed_b
            ext_ref[8:8 + cz, :] = t
            ext_ref[8 + cz:16 + cz, :] = packed_a
            zm = [None] + [ext_ref[8 - j:8 - j + cz, :] for j in range(1, 5)]
            zp = [None] + [ext_ref[8 + j:8 + j + cz, :] for j in range(1, 5)]

            def slope(m, p):
                return 45.0 * (p[1] - m[1]) - 9.0 * (p[2] - m[2]) + (p[3] - m[3])

            def smooth(m, p):
                return ((p[4] + m[4]) - 8.0 * (p[3] + m[3]) + 28.0 * (p[2] + m[2])
                        - 56.0 * (p[1] + m[1]))

            smoothing = smooth(zm, zp) + smooth(xm, xp) + 140.0 * t
            horiz = (slope_scale * (u * slope(xm, xp) + v * slope(zm, zp))
                     - damping * smoothing)
            across = jnp.where(y >= wall, horiz, 0.0)
            rate = normal + across
        else:
            rate = normal
        sn = keep_factor * st_ref[s] + rate
        adv = t + section_weight * sn
        sn_ref[s] = sn
        if fluid:
            tn_ref[s] = adv
        else:
            int_ref[s] = jnp.dot(bs_ref[s], adv, precision=lax.Precision.HIGHEST,
                                 preferred_element_type=jnp.float32)
            heads.append(adv[0:1, :])
    if not fluid:
        head_ref[...] = jnp.concatenate(heads, axis=0)


def local(theta, section_store, stream_speed, span_speed, conductivity, wall_layers,
          contact, spanwise_number, block_inverse):
    f32 = jnp.float32
    ny, cz, w = theta.shape
    ns = block_inverse.shape[0]
    nf = ny - ns
    nsb = ns // LB
    nfb = nf // LB
    ngz = lax.axis_size("gz")
    ngx = lax.axis_size("gx")

    wall2 = jnp.broadcast_to(wall_layers[:, None], (cz, w)).astype(jnp.int32)
    contact2 = jnp.broadcast_to(contact.astype(f32)[None, :], (cz, w))

    solid_c = conductivity[0]
    fluid_c = conductivity[1]

    def harmonic(a, b):
        return 2.0 * a * b / (a + b)

    zero = jnp.zeros((1,), f32)
    faces = jnp.stack([
        jnp.concatenate([zero, harmonic(solid_c[:-1], solid_c[1:]), zero]),
        jnp.concatenate([zero, harmonic(solid_c[:-1], fluid_c[1:]), zero]),
        jnp.concatenate([zero, harmonic(fluid_c[:-1], fluid_c[1:]), zero]),
    ])

    smem = pl.BlockSpec(memory_space=pltpu.SMEM)
    blk = lambda off: pl.BlockSpec((LB, cz, w), lambda i: (i + off, 0, 0))
    prev_spec = lambda off: pl.BlockSpec((1, cz, w), lambda i: (jnp.maximum((i + off) * LB - 1, 0), 0, 0))
    next_spec = lambda off: pl.BlockSpec((1, cz, w), lambda i: (jnp.minimum((i + off) * LB + LB, ny - 1), 0, 0))
    full2 = pl.BlockSpec((cz, w), lambda i: (0, 0))
    edge_spec = pl.BlockSpec((1, 8, w), lambda i: (i, 0, 0))
    rows_spec = pl.BlockSpec((LB // 2, 8, w), lambda i: (i, 0, 0))

    xl, xr, zl, zr = pl.pallas_call(
        pack_kernel,
        grid=(nfb,),
        in_specs=[blk(nsb)],
        out_specs=[edge_spec, edge_spec, rows_spec, rows_spec],
        out_shape=[
            jax.ShapeDtypeStruct((nfb, 8, w), f32),
            jax.ShapeDtypeStruct((nfb, 8, w), f32),
            jax.ShapeDtypeStruct((nf // 2, 8, w), f32),
            jax.ShapeDtypeStruct((nf // 2, 8, w), f32),
        ],
    )(theta)

    xb = lax.ppermute(xr, "gx", [(i, i + 1) for i in range(ngx - 1)])
    xa = lax.ppermute(xl, "gx", [(i + 1, i) for i in range(ngx - 1)])
    zb = lax.ppermute(zl, "gz", [(i, (i + 1) % ngz) for i in range(ngz)])
    za = lax.ppermute(zr, "gz", [((i + 1) % ngz, i) for i in range(ngz)])

    shifted_inverse = jnp.zeros((ns, cz, cz), f32).at[:, 1:, 1:].set(block_inverse)

    sn_part, interior, head = pl.pallas_call(
        lambda *refs: layer_kernel(False, 0, *refs),
        grid=(nsb,),
        in_specs=[smem, blk(0), prev_spec(0), next_spec(0), blk(0), full2, full2,
                  pl.BlockSpec((LB, cz, cz), lambda i: (i, 0, 0))],
        out_specs=[blk(0), blk(0), pl.BlockSpec((LB, w), lambda i: (i, 0))],
        out_shape=[
            jax.ShapeDtypeStruct((ny, cz, w), f32),
            jax.ShapeDtypeStruct((ns, cz, w), f32),
            jax.ShapeDtypeStruct((ns, w), f32),
        ],
    )(faces, theta, theta, theta, section_store, wall2, contact2, shifted_inverse)

    number = spanwise_number
    mine = jnp.stack([head, interior[:, 1, :], interior[:, cz - 1, :]])
    gathered = [mine]
    for d in range(1, ngz):
        gathered.append(lax.ppermute(mine, "gz", [(i, (i + d) % ngz) for i in range(ngz)]))
    targets = []
    for d in range(ngz):
        left = gathered[(d + 1) % ngz][2]
        targets.append(gathered[d][0] + number[:, None] * left + number[:, None] * gathered[d][1])

    square = number * number
    diagonal = 1.0 + 2.0 * number - square * (block_inverse[:, 0, 0] + block_inverse[:, -1, -1])
    beside = square * block_inverse[:, 0, -1]
    q = jnp.arange(ngz, dtype=jnp.int32)
    angle = (2.0 * math.pi / ngz) * q.astype(f32)
    denominator = diagonal[:, None] - 2.0 * beside[:, None] * jnp.cos(angle)[None, :]
    phase = (2.0 * math.pi / ngz) * ((q[:, None] * q[None, :]) % ngz).astype(f32)
    coeff = jnp.sum(jnp.cos(phase)[None, :, :] / denominator[:, :, None], axis=1) / ngz
    head_values = sum(coeff[:, (-d) % ngz, None] * targets[d] for d in range(ngz))
    following = sum(coeff[:, (-d - 1) % ngz, None] * targets[d] for d in range(ngz))

    fluid_sn, fluid_tn = pl.pallas_call(
        lambda *refs: layer_kernel(True, nsb, *refs),
        grid=(nfb,),
        in_specs=[smem, blk(nsb), prev_spec(nsb), next_spec(nsb), blk(nsb), full2, full2,
                  blk(nsb), blk(nsb), rows_spec, rows_spec, edge_spec, edge_spec,
                  pl.BlockSpec(memory_space=pl.ANY)],
        out_specs=[blk(nsb), blk(nsb)],
        out_shape=[
            jax.ShapeDtypeStruct((ny, cz, w), f32),
            jax.ShapeDtypeStruct((ny, cz, w), f32),
        ],
        scratch_shapes=[pltpu.VMEM((cz + 16, w), f32)],
        input_output_aliases={13: 0},
    )(faces, theta, theta, theta, section_store, wall2, contact2,
      stream_speed, span_speed, zb, za, xb, xa, sn_part)

    row = jnp.arange(cz, dtype=jnp.int32)
    col0 = jnp.zeros((ns, cz), f32).at[:, 1:].set(block_inverse[:, :, 0])
    col_last = jnp.zeros((ns, cz), f32).at[:, 1:].set(block_inverse[:, :, -1])
    scale = number[:, None, None]
    solved = interior + scale * (col0[:, :, None] * head_values[:, None, :]
                                 + col_last[:, :, None] * following[:, None, :])
    solved = jnp.where((row == 0)[None, :, None], head_values[:, None, :], solved)
    theta_new = lax.dynamic_update_slice_in_dim(fluid_tn, solved, 0, 0)
    return (theta_new, fluid_sn)


def solution(mesh):
    return jax.shard_map(
        local,
        mesh=mesh,
        in_specs=(
            P(None, "gz", "gx"),
            P(None, "gz", "gx"),
            P(None, "gz", "gx"),
            P(None, "gz", "gx"),
            P(),
            P("gz"),
            P("gx"),
            P(),
            P(),
        ),
        out_specs=(P(None, "gz", "gx"), P(None, "gz", "gx")),
        check_vma=False,
    )
```

```python
import math

import jax
import jax.numpy as jnp
from jax import lax
from jax.experimental import pallas as pl
from jax.experimental.pallas import tpu as pltpu
from jax.sharding import PartitionSpec as P

keep_factor = -5.0 / 9.0
section_weight = 15.0 / 16.0
stream_courant = 0.4
span_courant = 0.4
damping = 1.0 / 256.0

LB = 8


def pack_kernel(th_ref, xl_ref, xr_ref, zl_ref, zr_ref):
    ny, cz, w = th_ref.shape
    nblocks = xl_ref.shape[0]
    skip = ny - nblocks * LB
    lane8 = lax.broadcasted_iota(jnp.int32, (8, w), 1)
    sub8 = lax.broadcasted_iota(jnp.int32, (8, w), 0)

    def block(b, carry):
        first = skip + b * LB
        acc_l = jnp.zeros((8, w), jnp.float32)
        acc_r = jnp.zeros((8, w), jnp.float32)
        for s in range(LB):
            for v in range(cz // 8):
                t = th_ref[first + s, 8 * v:8 * v + 8, :]
                pos = 4 * LB * v + 4 * s
                pick = jnp.logical_and(lane8 >= pos, lane8 < pos + 4)
                acc_l = jnp.where(pick, pltpu.roll(t, pos % w, 1), acc_l)
                acc_r = jnp.where(pick, pltpu.roll(t, (pos + 4) % w, 1), acc_r)
        xl_ref[b] = acc_l
        xr_ref[b] = acc_r
        for p in range(LB // 2):
            a_hi = th_ref[first + 2 * p, cz - 8:cz, :]
            b_hi = th_ref[first + 2 * p + 1, cz - 8:cz, :]
            zl_ref[b * (LB // 2) + p] = jnp.where(sub8 < 4, pltpu.roll(a_hi, 4, 0), b_hi)
            a_lo = th_ref[first + 2 * p, 0:8, :]
            b_lo = th_ref[first + 2 * p + 1, 0:8, :]
            zr_ref[b * (LB // 2) + p] = jnp.where(sub8 < 4, a_lo, pltpu.roll(b_lo, 4, 0))
        return carry

    lax.fori_loop(0, nblocks, block, 0)


def layer_kernel(fluid, block_offset, *refs):
    if fluid:
        (face_ref, wall_ref, contact_ref, th_ref, prev_ref, next_ref, st_ref,
         u_ref, v_ref, zb_ref, za_ref, xb_ref, xa_ref, _alias_ref,
         sn_ref, tn_ref, wallv_ref, contv_ref, ext_ref) = refs
    else:
        (face_ref, wall_ref, contact_ref, th_ref, prev_ref, next_ref, st_ref,
         bs_ref, sn_ref, int_ref, mine_ref, wallv_ref, contv_ref) = refs
    _, cz, w = th_ref.shape
    base = (pl.program_id(0) + block_offset) * LB

    @pl.when(pl.program_id(0) == 0)
    def _():
        sub = lax.broadcasted_iota(jnp.int32, (cz, w), 0)
        acc = jnp.zeros((cz, w), jnp.int32)
        for z in range(cz):
            acc = jnp.where(sub == z, wall_ref[z], acc)
        wallv_ref[...] = acc
        lane = lax.broadcasted_iota(jnp.int32, (cz, w), 1)
        cacc = jnp.zeros((cz, w), jnp.float32)
        for x in range(w):
            cacc = jnp.where(lane == x, contact_ref[x].astype(jnp.float32), cacc)
        contv_ref[...] = cacc

    wall = wallv_ref[...]
    contact = contv_ref[...]

    def face(y):
        both_solid = face_ref[0, y + 1]
        both_fluid = face_ref[2, y + 1]
        at_wall = face_ref[1, y + 1] * contact
        return jnp.where(y + 1 < wall, both_solid, jnp.where(y >= wall, both_fluid, at_wall))

    if fluid:
        lane = lax.broadcasted_iota(jnp.int32, (8, w), 1)
        nv = cz // 8
        slope_scale = -stream_courant / 60.0

    heads = []
    face_dn = face(base - 1)
    for s in range(LB):
        y = base + s
        t = th_ref[s]
        tp = th_ref[s - 1] if s > 0 else prev_ref[0]
        tn = th_ref[s + 1] if s < LB - 1 else next_ref[0]
        face_up = face(y)
        normal = face_up * (tn - t) - face_dn * (t - tp)
        face_dn = face_up
        if fluid:
            u = u_ref[s].astype(jnp.float32)
            v = v_ref[s].astype(jnp.float32)
            edge_b = xb_ref[0]
            edge_a = xa_ref[0]
            xm = [[None] * nv for _ in range(5)]
            xp = [[None] * nv for _ in range(5)]
            for g in range(nv):
                tg = t[8 * g:8 * g + 8]
                pos = 4 * LB * g + 4 * s
                for j in range(1, 5):
                    xm[j][g] = jnp.where(lane < j, pltpu.roll(edge_b, (j - 4 - pos) % w, 1),
                                         pltpu.roll(tg, j, 1))
                    xp[j][g] = jnp.where(lane >= w - j, pltpu.roll(edge_a, (w - j - pos) % w, 1),
                                         pltpu.roll(tg, w - j, 1))
            xm = [None] + [jnp.concatenate(xm[j], axis=0) for j in range(1, 5)]
            xp = [None] + [jnp.concatenate(xp[j], axis=0) for j in range(1, 5)]
            packed_b = zb_ref[s // 2]
            packed_a = za_ref[s // 2]
            if s % 2 == 0:
                packed_b = pltpu.roll(packed_b, 4, 0)
            else:
                packed_a = pltpu.roll(packed_a, 4, 0)
            ext_ref[0:8, :] = packed_b
            ext_ref[8:8 + cz, :] = t
            ext_ref[8 + cz:16 + cz, :] = packed_a
            zm = [None] + [ext_ref[8 - j:8 - j + cz, :] for j in range(1, 5)]
            zp = [None] + [ext_ref[8 + j:8 + j + cz, :] for j in range(1, 5)]

            def slope(m, p):
                return 45.0 * (p[1] - m[1]) - 9.0 * (p[2] - m[2]) + (p[3] - m[3])

            def smooth(m, p):
                return ((p[4] + m[4]) - 8.0 * (p[3] + m[3]) + 28.0 * (p[2] + m[2])
                        - 56.0 * (p[1] + m[1]))

            smoothing = smooth(zm, zp) + smooth(xm, xp) + 140.0 * t
            horiz = (slope_scale * (u * slope(xm, xp) + v * slope(zm, zp))
                     - damping * smoothing)
            across = jnp.where(y >= wall, horiz, 0.0)
            rate = normal + across
        else:
            rate = normal
        sn = keep_factor * st_ref[s] + rate
        adv = t + section_weight * sn
        sn_ref[s] = sn
        if fluid:
            tn_ref[s] = adv
        else:
            inner = jnp.dot(bs_ref[s], adv, precision=lax.Precision.HIGHEST,
                            preferred_element_type=jnp.float32)
            int_ref[s] = inner
            heads.append((adv[0:1, :], inner[1:2, :], inner[cz - 1:cz, :]))
    if not fluid:
        for part in range(3):
            mine_ref[part] = jnp.concatenate([h[part] for h in heads], axis=0)


def local(theta, section_store, stream_speed, span_speed, conductivity, wall_layers,
          contact, spanwise_number, block_inverse):
    f32 = jnp.float32
    ny, cz, w = theta.shape
    ns = block_inverse.shape[0]
    nf = ny - ns
    nsb = ns // LB
    nfb = nf // LB
    ngz = lax.axis_size("gz")
    ngx = lax.axis_size("gx")


    solid_c = conductivity[0]
    fluid_c = conductivity[1]

    def harmonic(a, b):
        return 2.0 * a * b / (a + b)

    zero = jnp.zeros((1,), f32)
    faces = jnp.stack([
        jnp.concatenate([zero, harmonic(solid_c[:-1], solid_c[1:]), zero]),
        jnp.concatenate([zero, harmonic(solid_c[:-1], fluid_c[1:]), zero]),
        jnp.concatenate([zero, harmonic(fluid_c[:-1], fluid_c[1:]), zero]),
    ])

    smem = pl.BlockSpec(memory_space=pltpu.SMEM)
    blk = lambda off: pl.BlockSpec((LB, cz, w), lambda i: (i + off, 0, 0))
    prev_spec = lambda off: pl.BlockSpec((1, cz, w), lambda i: (jnp.maximum((i + off) * LB - 1, 0), 0, 0))
    next_spec = lambda off: pl.BlockSpec((1, cz, w), lambda i: (jnp.minimum((i + off) * LB + LB, ny - 1), 0, 0))
    edge_spec = pl.BlockSpec((1, 8, w), lambda i: (i, 0, 0))
    rows_spec = pl.BlockSpec((LB // 2, 8, w), lambda i: (i, 0, 0))

    xl, xr, zl, zr = pl.pallas_call(
        pack_kernel,
        grid=(1,),
        in_specs=[pl.BlockSpec((ny, cz, w), lambda i: (0, 0, 0))],
        out_specs=[pl.BlockSpec((nfb, 8, w), lambda i: (0, 0, 0)),
                   pl.BlockSpec((nfb, 8, w), lambda i: (0, 0, 0)),
                   pl.BlockSpec((nf // 2, 8, w), lambda i: (0, 0, 0)),
                   pl.BlockSpec((nf // 2, 8, w), lambda i: (0, 0, 0))],
        out_shape=[
            jax.ShapeDtypeStruct((nfb, 8, w), f32),
            jax.ShapeDtypeStruct((nfb, 8, w), f32),
            jax.ShapeDtypeStruct((nf // 2, 8, w), f32),
            jax.ShapeDtypeStruct((nf // 2, 8, w), f32),
        ],
    )(theta)

    xb = lax.ppermute(xr, "gx", [(i, i + 1) for i in range(ngx - 1)])
    xa = lax.ppermute(xl, "gx", [(i + 1, i) for i in range(ngx - 1)])
    zb = lax.ppermute(zl, "gz", [(i, (i + 1) % ngz) for i in range(ngz)])
    za = lax.ppermute(zr, "gz", [((i + 1) % ngz, i) for i in range(ngz)])

    shifted_inverse = jnp.pad(block_inverse, ((0, 0), (1, 0), (1, 0)))

    sn_part, interior, mine = pl.pallas_call(
        lambda *refs: layer_kernel(False, 0, *refs),
        grid=(nsb,),
        in_specs=[smem, smem, smem, blk(0), prev_spec(0), next_spec(0), blk(0),
                  pl.BlockSpec((LB, cz, cz), lambda i: (i, 0, 0))],
        out_specs=[blk(0), blk(0), pl.BlockSpec((3, LB, w), lambda i: (0, i, 0))],
        out_shape=[
            jax.ShapeDtypeStruct((ny, cz, w), f32),
            jax.ShapeDtypeStruct((ns, cz, w), f32),
            jax.ShapeDtypeStruct((3, ns, w), f32),
        ],
        scratch_shapes=[pltpu.VMEM((cz, w), jnp.int32), pltpu.VMEM((cz, w), f32)],
    )(faces, wall_layers, contact, theta, theta, theta, section_store, shifted_inverse)

    number = spanwise_number
    gathered = [mine]
    for d in range(1, ngz):
        gathered.append(lax.ppermute(mine, "gz", [(i, (i + d) % ngz) for i in range(ngz)]))
    targets = []
    for d in range(ngz):
        left = gathered[(d + 1) % ngz][2]
        targets.append(gathered[d][0] + number[:, None] * left + number[:, None] * gathered[d][1])

    square = number * number
    diagonal = 1.0 + 2.0 * number - square * (block_inverse[:, 0, 0] + block_inverse[:, -1, -1])
    beside = square * block_inverse[:, 0, -1]
    q = jnp.arange(ngz, dtype=jnp.int32)
    angle = (2.0 * math.pi / ngz) * q.astype(f32)
    denominator = diagonal[:, None] - 2.0 * beside[:, None] * jnp.cos(angle)[None, :]
    phase = (2.0 * math.pi / ngz) * ((q[:, None] * q[None, :]) % ngz).astype(f32)
    coeff = jnp.sum(jnp.cos(phase)[None, :, :] / denominator[:, :, None], axis=1) / ngz
    head_values = sum(coeff[:, (-d) % ngz, None] * targets[d] for d in range(ngz))
    following = sum(coeff[:, (-d - 1) % ngz, None] * targets[d] for d in range(ngz))

    fluid_sn, fluid_tn = pl.pallas_call(
        lambda *refs: layer_kernel(True, nsb, *refs),
        grid=(nfb,),
        in_specs=[smem, smem, smem, blk(nsb), prev_spec(nsb), next_spec(nsb), blk(nsb),
                  blk(nsb), blk(nsb), rows_spec, rows_spec, edge_spec, edge_spec,
                  pl.BlockSpec(memory_space=pl.ANY)],
        out_specs=[blk(nsb), blk(nsb)],
        out_shape=[
            jax.ShapeDtypeStruct((ny, cz, w), f32),
            jax.ShapeDtypeStruct((ny, cz, w), f32),
        ],
        scratch_shapes=[pltpu.VMEM((cz, w), jnp.int32), pltpu.VMEM((cz, w), f32),
                        pltpu.VMEM((cz + 16, w), f32)],
        input_output_aliases={13: 0},
    )(faces, wall_layers, contact, theta, theta, theta, section_store,
      stream_speed, span_speed, zb, za, xb, xa, sn_part)

    row = jnp.arange(cz, dtype=jnp.int32)
    col0 = jnp.zeros((ns, cz), f32).at[:, 1:].set(block_inverse[:, :, 0])
    col_last = jnp.zeros((ns, cz), f32).at[:, 1:].set(block_inverse[:, :, -1])
    scale = number[:, None, None]
    solved = interior + scale * (col0[:, :, None] * head_values[:, None, :]
                                 + col_last[:, :, None] * following[:, None, :])
    solved = jnp.where((row == 0)[None, :, None], head_values[:, None, :], solved)
    theta_new = lax.dynamic_update_slice_in_dim(fluid_tn, solved, 0, 0)
    return (theta_new, fluid_sn)


def solution(mesh):
    return jax.shard_map(
        local,
        mesh=mesh,
        in_specs=(
            P(None, "gz", "gx"),
            P(None, "gz", "gx"),
            P(None, "gz", "gx"),
            P(None, "gz", "gx"),
            P(),
            P("gz"),
            P("gx"),
            P(),
            P(),
        ),
        out_specs=(P(None, "gz", "gx"), P(None, "gz", "gx")),
        check_vma=False,
    )
```

```python
import math

import jax
import jax.numpy as jnp
from jax import lax
from jax.experimental import pallas as pl
from jax.experimental.pallas import tpu as pltpu
from jax.sharding import PartitionSpec as P

keep_factor = -5.0 / 9.0
section_weight = 15.0 / 16.0
stream_courant = 0.4
span_courant = 0.4
damping = 1.0 / 256.0

LB = 8


def pack_kernel(th_ref, xl_ref, xr_ref, zl_ref, zr_ref):
    ny, cz, w = th_ref.shape
    nblocks = xl_ref.shape[0]
    skip = ny - nblocks * LB
    lane8 = lax.broadcasted_iota(jnp.int32, (8, w), 1)
    sub8 = lax.broadcasted_iota(jnp.int32, (8, w), 0)

    def block(b, carry):
        first = skip + b * LB
        acc_l = jnp.zeros((8, w), jnp.float32)
        acc_r = jnp.zeros((8, w), jnp.float32)
        for s in range(LB):
            for v in range(cz // 8):
                t = th_ref[first + s, 8 * v:8 * v + 8, :]
                pos = 4 * LB * v + 4 * s
                pick = jnp.logical_and(lane8 >= pos, lane8 < pos + 4)
                acc_l = jnp.where(pick, pltpu.roll(t, pos % w, 1), acc_l)
                acc_r = jnp.where(pick, pltpu.roll(t, (pos + 4) % w, 1), acc_r)
        xl_ref[b] = acc_l
        xr_ref[b] = acc_r
        for p in range(LB // 2):
            a_hi = th_ref[first + 2 * p, cz - 8:cz, :]
            b_hi = th_ref[first + 2 * p + 1, cz - 8:cz, :]
            zl_ref[b * (LB // 2) + p] = jnp.where(sub8 < 4, pltpu.roll(a_hi, 4, 0), b_hi)
            a_lo = th_ref[first + 2 * p, 0:8, :]
            b_lo = th_ref[first + 2 * p + 1, 0:8, :]
            zr_ref[b * (LB // 2) + p] = jnp.where(sub8 < 4, a_lo, pltpu.roll(b_lo, 4, 0))
        return carry

    lax.fori_loop(0, nblocks, block, 0)


def layer_kernel(fluid, block_offset, *refs):
    if fluid:
        (face_ref, wall_ref, contact_ref, th_ref, prev_ref, next_ref, st_ref,
         u_ref, v_ref, zb_ref, za_ref, xb_ref, xa_ref, _alias_ref,
         sn_ref, tn_ref, wallv_ref, contv_ref, ext_ref) = refs
    else:
        (face_ref, wall_ref, contact_ref, th_ref, prev_ref, next_ref, st_ref,
         bs_ref, _order_ref, sn_ref, int_ref, mine_ref, wallv_ref, contv_ref) = refs
    _, cz, w = th_ref.shape
    base = (pl.program_id(0) + block_offset) * LB

    @pl.when(pl.program_id(0) == 0)
    def _():
        sub = lax.broadcasted_iota(jnp.int32, (cz, w), 0)
        acc = jnp.zeros((cz, w), jnp.int32)
        for z in range(cz):
            acc = jnp.where(sub == z, wall_ref[z], acc)
        wallv_ref[...] = acc
        lane = lax.broadcasted_iota(jnp.int32, (cz, w), 1)
        cacc = jnp.zeros((cz, w), jnp.float32)
        for x in range(w):
            cacc = jnp.where(lane == x, contact_ref[x].astype(jnp.float32), cacc)
        contv_ref[...] = cacc

    wall = wallv_ref[...]
    contact = contv_ref[...]

    def face(y):
        both_solid = face_ref[0, y + 1]
        both_fluid = face_ref[2, y + 1]
        at_wall = face_ref[1, y + 1] * contact
        return jnp.where(y + 1 < wall, both_solid, jnp.where(y >= wall, both_fluid, at_wall))

    if fluid:
        lane = lax.broadcasted_iota(jnp.int32, (8, w), 1)
        nv = cz // 8
        slope_scale = -stream_courant / 60.0

    heads = []
    face_dn = face(base - 1)
    for s in range(LB):
        y = base + s
        t = th_ref[s]
        tp = th_ref[s - 1] if s > 0 else prev_ref[0]
        tn = th_ref[s + 1] if s < LB - 1 else next_ref[0]
        face_up = face(y)
        normal = face_up * (tn - t) - face_dn * (t - tp)
        face_dn = face_up
        if fluid:
            u = u_ref[s].astype(jnp.float32)
            v = v_ref[s].astype(jnp.float32)
            edge_b = xb_ref[0]
            edge_a = xa_ref[0]
            xm = [[None] * nv for _ in range(5)]
            xp = [[None] * nv for _ in range(5)]
            for g in range(nv):
                tg = t[8 * g:8 * g + 8]
                pos = 4 * LB * g + 4 * s
                for j in range(1, 5):
                    xm[j][g] = jnp.where(lane < j, pltpu.roll(edge_b, (j - 4 - pos) % w, 1),
                                         pltpu.roll(tg, j, 1))
                    xp[j][g] = jnp.where(lane >= w - j, pltpu.roll(edge_a, (w - j - pos) % w, 1),
                                         pltpu.roll(tg, w - j, 1))
            xm = [None] + [jnp.concatenate(xm[j], axis=0) for j in range(1, 5)]
            xp = [None] + [jnp.concatenate(xp[j], axis=0) for j in range(1, 5)]
            packed_b = zb_ref[s // 2]
            packed_a = za_ref[s // 2]
            if s % 2 == 0:
                packed_b = pltpu.roll(packed_b, 4, 0)
            else:
                packed_a = pltpu.roll(packed_a, 4, 0)
            ext_ref[0:8, :] = packed_b
            ext_ref[8:8 + cz, :] = t
            ext_ref[8 + cz:16 + cz, :] = packed_a
            zm = [None] + [ext_ref[8 - j:8 - j + cz, :] for j in range(1, 5)]
            zp = [None] + [ext_ref[8 + j:8 + j + cz, :] for j in range(1, 5)]

            def slope(m, p):
                return 45.0 * (p[1] - m[1]) - 9.0 * (p[2] - m[2]) + (p[3] - m[3])

            def smooth(m, p):
                return ((p[4] + m[4]) - 8.0 * (p[3] + m[3]) + 28.0 * (p[2] + m[2])
                        - 56.0 * (p[1] + m[1]))

            smoothing = smooth(zm, zp) + smooth(xm, xp) + 140.0 * t
            horiz = (slope_scale * (u * slope(xm, xp) + v * slope(zm, zp))
                     - damping * smoothing)
            across = jnp.where(y >= wall, horiz, 0.0)
            rate = normal + across
        else:
            rate = normal
        sn = keep_factor * st_ref[s] + rate
        adv = t + section_weight * sn
        sn_ref[s] = sn
        if fluid:
            tn_ref[s] = adv
        else:
            inner = jnp.dot(bs_ref[s], adv, precision=lax.Precision.HIGHEST,
                            preferred_element_type=jnp.float32)
            int_ref[s] = inner
            heads.append((adv[0:1, :], inner[1:2, :], inner[cz - 1:cz, :]))
    if not fluid:
        for part in range(3):
            mine_ref[part] = jnp.concatenate([h[part] for h in heads], axis=0)


def local(theta, section_store, stream_speed, span_speed, conductivity, wall_layers,
          contact, spanwise_number, block_inverse):
    f32 = jnp.float32
    ny, cz, w = theta.shape
    ns = block_inverse.shape[0]
    nf = ny - ns
    nsb = ns // LB
    nfb = nf // LB
    ngz = lax.axis_size("gz")
    ngx = lax.axis_size("gx")


    solid_c = conductivity[0]
    fluid_c = conductivity[1]

    def harmonic(a, b):
        return 2.0 * a * b / (a + b)

    zero = jnp.zeros((1,), f32)
    faces = jnp.stack([
        jnp.concatenate([zero, harmonic(solid_c[:-1], solid_c[1:]), zero]),
        jnp.concatenate([zero, harmonic(solid_c[:-1], fluid_c[1:]), zero]),
        jnp.concatenate([zero, harmonic(fluid_c[:-1], fluid_c[1:]), zero]),
    ])

    smem = pl.BlockSpec(memory_space=pltpu.SMEM)
    blk = lambda off: pl.BlockSpec((LB, cz, w), lambda i: (i + off, 0, 0))
    prev_spec = lambda off: pl.BlockSpec((1, cz, w), lambda i: (jnp.maximum((i + off) * LB - 1, 0), 0, 0))
    next_spec = lambda off: pl.BlockSpec((1, cz, w), lambda i: (jnp.minimum((i + off) * LB + LB, ny - 1), 0, 0))
    edge_spec = pl.BlockSpec((1, 8, w), lambda i: (i, 0, 0))
    rows_spec = pl.BlockSpec((LB // 2, 8, w), lambda i: (i, 0, 0))

    xl, xr, zl, zr = pl.pallas_call(
        pack_kernel,
        grid=(1,),
        in_specs=[pl.BlockSpec((ny, cz, w), lambda i: (0, 0, 0))],
        out_specs=[pl.BlockSpec((nfb, 8, w), lambda i: (0, 0, 0)),
                   pl.BlockSpec((nfb, 8, w), lambda i: (0, 0, 0)),
                   pl.BlockSpec((nf // 2, 8, w), lambda i: (0, 0, 0)),
                   pl.BlockSpec((nf // 2, 8, w), lambda i: (0, 0, 0))],
        out_shape=[
            jax.ShapeDtypeStruct((nfb, 8, w), f32),
            jax.ShapeDtypeStruct((nfb, 8, w), f32),
            jax.ShapeDtypeStruct((nf // 2, 8, w), f32),
            jax.ShapeDtypeStruct((nf // 2, 8, w), f32),
        ],
    )(theta)

    xb = lax.ppermute(xr, "gx", [(i, i + 1) for i in range(ngx - 1)])
    xa = lax.ppermute(xl, "gx", [(i + 1, i) for i in range(ngx - 1)])
    zb = lax.ppermute(zl, "gz", [(i, (i + 1) % ngz) for i in range(ngz)])
    za = lax.ppermute(zr, "gz", [((i + 1) % ngz, i) for i in range(ngz)])

    shifted_inverse = jnp.pad(block_inverse, ((0, 0), (1, 0), (1, 0)))

    sn_part, interior, mine = pl.pallas_call(
        lambda *refs: layer_kernel(False, 0, *refs),
        grid=(nsb,),
        in_specs=[smem, smem, smem, blk(0), prev_spec(0), next_spec(0), blk(0),
                  pl.BlockSpec((LB, cz, cz), lambda i: (i, 0, 0)),
                  pl.BlockSpec(memory_space=pl.ANY)],
        out_specs=[blk(0), blk(0), pl.BlockSpec((3, LB, w), lambda i: (0, i, 0))],
        out_shape=[
            jax.ShapeDtypeStruct((ny, cz, w), f32),
            jax.ShapeDtypeStruct((ns, cz, w), f32),
            jax.ShapeDtypeStruct((3, ns, w), f32),
        ],
        scratch_shapes=[pltpu.VMEM((cz, w), jnp.int32), pltpu.VMEM((cz, w), f32)],
    )(faces, wall_layers, contact, theta, theta, theta, section_store, shifted_inverse, zr)

    number = spanwise_number
    spread = jnp.broadcast_to(mine[None], (ngz,) + mine.shape)
    blocks = lax.all_to_all(spread, "gz", 0, 0, tiled=True)
    left = jnp.roll(blocks[:, 2], 1, axis=0)
    targets = blocks[:, 0] + number[None, :, None] * left + number[None, :, None] * blocks[:, 1]

    square = number * number
    diagonal = 1.0 + 2.0 * number - square * (block_inverse[:, 0, 0] + block_inverse[:, -1, -1])
    beside = square * block_inverse[:, 0, -1]
    q = jnp.arange(ngz, dtype=jnp.int32)
    angle = (2.0 * math.pi / ngz) * q.astype(f32)
    denominator = diagonal[:, None] - 2.0 * beside[:, None] * jnp.cos(angle)[None, :]
    k = lax.axis_index("gz")

    def weights(shift):
        m = (q - shift) % ngz
        phase = (2.0 * math.pi / ngz) * ((q[:, None] * m[None, :]) % ngz).astype(f32)
        return jnp.sum(jnp.cos(phase)[None, :, :] / denominator[:, :, None], axis=1) / ngz

    head_values = jnp.sum(weights(k).T[:, :, None] * targets, axis=0)
    following = jnp.sum(weights(k + 1).T[:, :, None] * targets, axis=0)

    fluid_sn, fluid_tn = pl.pallas_call(
        lambda *refs: layer_kernel(True, nsb, *refs),
        grid=(nfb,),
        in_specs=[smem, smem, smem, blk(nsb), prev_spec(nsb), next_spec(nsb), blk(nsb),
                  blk(nsb), blk(nsb), rows_spec, rows_spec, edge_spec, edge_spec,
                  pl.BlockSpec(memory_space=pl.ANY)],
        out_specs=[blk(nsb), blk(nsb)],
        out_shape=[
            jax.ShapeDtypeStruct((ny, cz, w), f32),
            jax.ShapeDtypeStruct((ny, cz, w), f32),
        ],
        scratch_shapes=[pltpu.VMEM((cz, w), jnp.int32), pltpu.VMEM((cz, w), f32),
                        pltpu.VMEM((cz + 16, w), f32)],
        input_output_aliases={13: 0},
    )(faces, wall_layers, contact, theta, theta, theta, section_store,
      stream_speed, span_speed, zb, za, xb, xa, sn_part)

    row = jnp.arange(cz, dtype=jnp.int32)
    col0 = jnp.zeros((ns, cz), f32).at[:, 1:].set(block_inverse[:, :, 0])
    col_last = jnp.zeros((ns, cz), f32).at[:, 1:].set(block_inverse[:, :, -1])
    scale = number[:, None, None]
    solved = interior + scale * (col0[:, :, None] * head_values[:, None, :]
                                 + col_last[:, :, None] * following[:, None, :])
    solved = jnp.where((row == 0)[None, :, None], head_values[:, None, :], solved)
    theta_new = lax.dynamic_update_slice_in_dim(fluid_tn, solved, 0, 0)
    return (theta_new, fluid_sn)


def solution(mesh):
    return jax.shard_map(
        local,
        mesh=mesh,
        in_specs=(
            P(None, "gz", "gx"),
            P(None, "gz", "gx"),
            P(None, "gz", "gx"),
            P(None, "gz", "gx"),
            P(),
            P("gz"),
            P("gx"),
            P(),
            P(),
        ),
        out_specs=(P(None, "gz", "gx"), P(None, "gz", "gx")),
        check_vma=False,
    )
```

```python
import math

import jax
import jax.numpy as jnp
from jax import lax
from jax.experimental import pallas as pl
from jax.experimental.pallas import tpu as pltpu
from jax.sharding import PartitionSpec as P

keep_factor = -5.0 / 9.0
section_weight = 15.0 / 16.0
stream_courant = 0.4
span_courant = 0.4
damping = 1.0 / 256.0

LB = 8


def pack_kernel(th_ref, u_ref, xl_ref, xr_ref, ul_ref, ur_ref, zl_ref, zr_ref):
    ny, cz, w = th_ref.shape
    nblocks = xl_ref.shape[0]
    skip = ny - nblocks * LB
    lane8 = lax.broadcasted_iota(jnp.int32, (8, w), 1)
    sub8 = lax.broadcasted_iota(jnp.int32, (8, w), 0)

    def block(b, carry):
        first = skip + b * LB
        acc_l = jnp.zeros((8, w), jnp.float32)
        acc_r = jnp.zeros((8, w), jnp.float32)
        uacc_l = jnp.zeros((8, w), jnp.float32)
        uacc_r = jnp.zeros((8, w), jnp.float32)
        for s in range(LB):
            speed = u_ref[first + s].astype(jnp.float32)
            for v in range(cz // 8):
                t = th_ref[first + s, 8 * v:8 * v + 8, :]
                pos = 4 * LB * v + 4 * s
                moved = pltpu.roll(t, pos % w, 1)
                umoved = pltpu.roll(speed[8 * v:8 * v + 8], pos % w, 1)
                pick_l = jnp.logical_and(lane8 >= pos, lane8 < pos + 4)
                pick_r = jnp.logical_and(lane8 >= (pos - 4) % w, lane8 < (pos - 4) % w + 4)
                acc_l = jnp.where(pick_l, moved, acc_l)
                acc_r = jnp.where(pick_r, moved, acc_r)
                uacc_l = jnp.where(pick_l, umoved, uacc_l)
                uacc_r = jnp.where(pick_r, umoved, uacc_r)
        xl_ref[b] = acc_l
        xr_ref[b] = acc_r
        ul_ref[b] = uacc_l
        ur_ref[b] = uacc_r
        for p in range(LB // 2):
            a_hi = th_ref[first + 2 * p, cz - 8:cz, :]
            b_hi = th_ref[first + 2 * p + 1, cz - 8:cz, :]
            zl_ref[b * (LB // 2) + p] = jnp.where(sub8 < 4, pltpu.roll(a_hi, 4, 0), b_hi)
            a_lo = th_ref[first + 2 * p, 0:8, :]
            b_lo = th_ref[first + 2 * p + 1, 0:8, :]
            zr_ref[b * (LB // 2) + p] = jnp.where(sub8 < 4, a_lo, pltpu.roll(b_lo, 4, 0))
        return carry

    lax.fori_loop(0, nblocks, block, 0)


def layer_kernel(fluid, block_offset, *refs):
    if fluid:
        (face_ref, wall_ref, contact_ref, th_ref, prev_ref, next_ref, st_ref,
         u_ref, v_ref, zb_ref, za_ref, xb_ref, xa_ref, xl_ref, xr_ref, ul_ref, ur_ref,
         _alias_ref, sn_ref, tn_ref, wallv_ref, contv_ref, ext_ref) = refs
    else:
        (face_ref, wall_ref, contact_ref, th_ref, prev_ref, next_ref, st_ref,
         bs_ref, _order_ref, sn_ref, int_ref, mine_ref, wallv_ref, contv_ref) = refs
    _, cz, w = th_ref.shape
    base = (pl.program_id(0) + block_offset) * LB

    @pl.when(pl.program_id(0) == 0)
    def _():
        sub = lax.broadcasted_iota(jnp.int32, (cz, w), 0)
        acc = jnp.zeros((cz, w), jnp.int32)
        for z in range(cz):
            acc = jnp.where(sub == z, wall_ref[z], acc)
        wallv_ref[...] = acc
        lane = lax.broadcasted_iota(jnp.int32, (cz, w), 1)
        cacc = jnp.zeros((cz, w), jnp.float32)
        for x in range(w):
            cacc = jnp.where(lane == x, contact_ref[x].astype(jnp.float32), cacc)
        contv_ref[...] = cacc

    wall = wallv_ref[...]
    contact = contv_ref[...]

    def face(y):
        both_solid = face_ref[0, y + 1]
        both_fluid = face_ref[2, y + 1]
        at_wall = face_ref[1, y + 1] * contact
        return jnp.where(y + 1 < wall, both_solid, jnp.where(y >= wall, both_fluid, at_wall))

    if fluid:
        lane = lax.broadcasted_iota(jnp.int32, (8, w), 1)
        nv = cz // 8
        slope_scale = -stream_courant / 60.0
        quarter = lane % 4
        miss_l = xb_ref[0] - xr_ref[0]
        miss_r = xa_ref[0] - xl_ref[0]

        def edge(miss, weights, left):
            acc = jnp.zeros((8, w), jnp.float32)
            for j, c in weights:
                if left:
                    term = jnp.where(quarter < j, pltpu.roll(miss, j, 1), 0.0)
                else:
                    term = jnp.where(quarter >= 4 - j, pltpu.roll(miss, w - j, 1), 0.0)
                acc = acc + c * term
            return acc

        fix_l = (slope_scale * ul_ref[0] * edge(miss_l, ((1, -45.0), (2, 9.0), (3, -1.0)), True)
                 - damping * edge(miss_l, ((1, -56.0), (2, 28.0), (3, -8.0), (4, 1.0)), True))
        fix_r = (slope_scale * ur_ref[0] * edge(miss_r, ((1, 45.0), (2, -9.0), (3, 1.0)), False)
                 - damping * edge(miss_r, ((1, -56.0), (2, 28.0), (3, -8.0), (4, 1.0)), False))

    heads = []
    face_dn = face(base - 1)
    for s in range(LB):
        y = base + s
        t = th_ref[s]
        tp = th_ref[s - 1] if s > 0 else prev_ref[0]
        tn = th_ref[s + 1] if s < LB - 1 else next_ref[0]
        face_up = face(y)
        normal = face_up * (tn - t) - face_dn * (t - tp)
        face_dn = face_up
        if fluid:
            u = u_ref[s].astype(jnp.float32)
            v = v_ref[s].astype(jnp.float32)
            xm = [None] + [pltpu.roll(t, j, 1) for j in range(1, 5)]
            xp = [None] + [pltpu.roll(t, w - j, 1) for j in range(1, 5)]
            fixes = []
            for g in range(nv):
                pos = 4 * LB * g + 4 * s
                at_l = jnp.logical_and(lane >= pos, lane < pos + 4)
                at_r = jnp.logical_and(lane >= (pos - 4) % w, lane < (pos - 4) % w + 4)
                picked = jnp.where(at_l, fix_l, jnp.where(at_r, fix_r, 0.0))
                fixes.append(pltpu.roll(picked, (w - pos) % w, 1))
            fix = jnp.concatenate(fixes, axis=0)
            packed_b = zb_ref[s // 2]
            packed_a = za_ref[s // 2]
            if s % 2 == 0:
                packed_b = pltpu.roll(packed_b, 4, 0)
            else:
                packed_a = pltpu.roll(packed_a, 4, 0)
            ext_ref[0:8, :] = packed_b
            ext_ref[8:8 + cz, :] = t
            ext_ref[8 + cz:16 + cz, :] = packed_a
            zm = [None] + [ext_ref[8 - j:8 - j + cz, :] for j in range(1, 5)]
            zp = [None] + [ext_ref[8 + j:8 + j + cz, :] for j in range(1, 5)]

            def slope(m, p):
                return 45.0 * (p[1] - m[1]) - 9.0 * (p[2] - m[2]) + (p[3] - m[3])

            def smooth(m, p):
                return ((p[4] + m[4]) - 8.0 * (p[3] + m[3]) + 28.0 * (p[2] + m[2])
                        - 56.0 * (p[1] + m[1]))

            smoothing = smooth(zm, zp) + smooth(xm, xp) + 140.0 * t
            horiz = (slope_scale * (u * slope(xm, xp) + v * slope(zm, zp))
                     - damping * smoothing) + fix
            across = jnp.where(y >= wall, horiz, 0.0)
            rate = normal + across
        else:
            rate = normal
        sn = keep_factor * st_ref[s] + rate
        adv = t + section_weight * sn
        sn_ref[s] = sn
        if fluid:
            tn_ref[s] = adv
        else:
            inner = jnp.dot(bs_ref[s], adv, precision=lax.Precision.HIGHEST,
                            preferred_element_type=jnp.float32)
            int_ref[s] = inner
            heads.append((adv[0:1, :], inner[1:2, :], inner[cz - 1:cz, :]))
    if not fluid:
        for part in range(3):
            mine_ref[part] = jnp.concatenate([h[part] for h in heads], axis=0)


def local(theta, section_store, stream_speed, span_speed, conductivity, wall_layers,
          contact, spanwise_number, block_inverse):
    f32 = jnp.float32
    ny, cz, w = theta.shape
    ns = block_inverse.shape[0]
    nf = ny - ns
    nsb = ns // LB
    nfb = nf // LB
    ngz = lax.axis_size("gz")
    ngx = lax.axis_size("gx")


    solid_c = conductivity[0]
    fluid_c = conductivity[1]

    def harmonic(a, b):
        return 2.0 * a * b / (a + b)

    zero = jnp.zeros((1,), f32)
    faces = jnp.stack([
        jnp.concatenate([zero, harmonic(solid_c[:-1], solid_c[1:]), zero]),
        jnp.concatenate([zero, harmonic(solid_c[:-1], fluid_c[1:]), zero]),
        jnp.concatenate([zero, harmonic(fluid_c[:-1], fluid_c[1:]), zero]),
    ])

    smem = pl.BlockSpec(memory_space=pltpu.SMEM)
    blk = lambda off: pl.BlockSpec((LB, cz, w), lambda i: (i + off, 0, 0))
    prev_spec = lambda off: pl.BlockSpec((1, cz, w), lambda i: (jnp.maximum((i + off) * LB - 1, 0), 0, 0))
    next_spec = lambda off: pl.BlockSpec((1, cz, w), lambda i: (jnp.minimum((i + off) * LB + LB, ny - 1), 0, 0))
    edge_spec = pl.BlockSpec((1, 8, w), lambda i: (i, 0, 0))
    rows_spec = pl.BlockSpec((LB // 2, 8, w), lambda i: (i, 0, 0))

    xl, xr, ul, ur, zl, zr = pl.pallas_call(
        pack_kernel,
        grid=(1,),
        in_specs=[pl.BlockSpec((ny, cz, w), lambda i: (0, 0, 0))] * 2,
        out_specs=[pl.BlockSpec((nfb, 8, w), lambda i: (0, 0, 0))] * 4
        + [pl.BlockSpec((nf // 2, 8, w), lambda i: (0, 0, 0))] * 2,
        out_shape=[jax.ShapeDtypeStruct((nfb, 8, w), f32)] * 4
        + [jax.ShapeDtypeStruct((nf // 2, 8, w), f32)] * 2,
    )(theta, stream_speed)

    xb = lax.ppermute(xr, "gx", [(i, i + 1) for i in range(ngx - 1)])
    xa = lax.ppermute(xl, "gx", [(i + 1, i) for i in range(ngx - 1)])
    zb = lax.ppermute(zl, "gz", [(i, (i + 1) % ngz) for i in range(ngz)])
    za = lax.ppermute(zr, "gz", [((i + 1) % ngz, i) for i in range(ngz)])

    shifted_inverse = jnp.pad(block_inverse, ((0, 0), (1, 0), (1, 0)))

    sn_part, interior, mine = pl.pallas_call(
        lambda *refs: layer_kernel(False, 0, *refs),
        grid=(nsb,),
        in_specs=[smem, smem, smem, blk(0), prev_spec(0), next_spec(0), blk(0),
                  pl.BlockSpec((LB, cz, cz), lambda i: (i, 0, 0)),
                  pl.BlockSpec(memory_space=pl.ANY)],
        out_specs=[blk(0), blk(0), pl.BlockSpec((3, LB, w), lambda i: (0, i, 0))],
        out_shape=[
            jax.ShapeDtypeStruct((ny, cz, w), f32),
            jax.ShapeDtypeStruct((ns, cz, w), f32),
            jax.ShapeDtypeStruct((3, ns, w), f32),
        ],
        scratch_shapes=[pltpu.VMEM((cz, w), jnp.int32), pltpu.VMEM((cz, w), f32)],
    )(faces, wall_layers, contact, theta, theta, theta, section_store, shifted_inverse, zr)

    number = spanwise_number
    spread = jnp.broadcast_to(mine[None], (ngz,) + mine.shape)
    blocks = lax.all_to_all(spread, "gz", 0, 0, tiled=True)
    left = jnp.roll(blocks[:, 2], 1, axis=0)
    targets = blocks[:, 0] + number[None, :, None] * left + number[None, :, None] * blocks[:, 1]

    square = number * number
    diagonal = 1.0 + 2.0 * number - square * (block_inverse[:, 0, 0] + block_inverse[:, -1, -1])
    beside = square * block_inverse[:, 0, -1]
    q = jnp.arange(ngz, dtype=jnp.int32)
    angle = (2.0 * math.pi / ngz) * q.astype(f32)
    denominator = diagonal[:, None] - 2.0 * beside[:, None] * jnp.cos(angle)[None, :]
    k = lax.axis_index("gz")

    def weights(shift):
        m = (q - shift) % ngz
        phase = (2.0 * math.pi / ngz) * ((q[:, None] * m[None, :]) % ngz).astype(f32)
        return jnp.sum(jnp.cos(phase)[None, :, :] / denominator[:, :, None], axis=1) / ngz

    head_values = jnp.sum(weights(k).T[:, :, None] * targets, axis=0)
    following = jnp.sum(weights(k + 1).T[:, :, None] * targets, axis=0)

    fluid_sn, fluid_tn = pl.pallas_call(
        lambda *refs: layer_kernel(True, nsb, *refs),
        grid=(nfb,),
        in_specs=[smem, smem, smem, blk(nsb), prev_spec(nsb), next_spec(nsb), blk(nsb),
                  blk(nsb), blk(nsb), rows_spec, rows_spec, edge_spec, edge_spec,
                  edge_spec, edge_spec, edge_spec, edge_spec,
                  pl.BlockSpec(memory_space=pl.ANY)],
        out_specs=[blk(nsb), blk(nsb)],
        out_shape=[
            jax.ShapeDtypeStruct((ny, cz, w), f32),
            jax.ShapeDtypeStruct((ny, cz, w), f32),
        ],
        scratch_shapes=[pltpu.VMEM((cz, w), jnp.int32), pltpu.VMEM((cz, w), f32),
                        pltpu.VMEM((cz + 16, w), f32)],
        input_output_aliases={17: 0},
    )(faces, wall_layers, contact, theta, theta, theta, section_store,
      stream_speed, span_speed, zb, za, xb, xa, xl, xr, ul, ur, sn_part)

    row = jnp.arange(cz, dtype=jnp.int32)
    col0 = jnp.zeros((ns, cz), f32).at[:, 1:].set(block_inverse[:, :, 0])
    col_last = jnp.zeros((ns, cz), f32).at[:, 1:].set(block_inverse[:, :, -1])
    scale = number[:, None, None]
    solved = interior + scale * (col0[:, :, None] * head_values[:, None, :]
                                 + col_last[:, :, None] * following[:, None, :])
    solved = jnp.where((row == 0)[None, :, None], head_values[:, None, :], solved)
    theta_new = lax.dynamic_update_slice_in_dim(fluid_tn, solved, 0, 0)
    return (theta_new, fluid_sn)


def solution(mesh):
    return jax.shard_map(
        local,
        mesh=mesh,
        in_specs=(
            P(None, "gz", "gx"),
            P(None, "gz", "gx"),
            P(None, "gz", "gx"),
            P(None, "gz", "gx"),
            P(),
            P("gz"),
            P("gx"),
            P(),
            P(),
        ),
        out_specs=(P(None, "gz", "gx"), P(None, "gz", "gx")),
        check_vma=False,
    )
```

```python
import math

import jax
import jax.numpy as jnp
from jax import lax
from jax.experimental import pallas as pl
from jax.experimental.pallas import tpu as pltpu
from jax.sharding import PartitionSpec as P

keep_factor = -5.0 / 9.0
section_weight = 15.0 / 16.0
stream_courant = 0.4
span_courant = 0.4
damping = 1.0 / 256.0

LB = 8


def pack_kernel(th_ref, u_ref, xl_ref, xr_ref, ul_ref, ur_ref, zl_ref, zr_ref):
    ny, cz, w = th_ref.shape
    nblocks = xl_ref.shape[0]
    skip = ny - nblocks * LB
    lane8 = lax.broadcasted_iota(jnp.int32, (8, w), 1)
    sub8 = lax.broadcasted_iota(jnp.int32, (8, w), 0)

    def block(b, carry):
        first = skip + b * LB
        acc_l = jnp.zeros((8, w), jnp.float32)
        acc_r = jnp.zeros((8, w), jnp.float32)
        uacc_l = jnp.zeros((8, w), jnp.float32)
        uacc_r = jnp.zeros((8, w), jnp.float32)
        for s in range(LB):
            speed = u_ref[first + s].astype(jnp.float32)
            for v in range(cz // 8):
                t = th_ref[first + s, 8 * v:8 * v + 8, :]
                pos = 4 * LB * v + 4 * s
                moved = pltpu.roll(t, pos % w, 1)
                umoved = pltpu.roll(speed[8 * v:8 * v + 8], pos % w, 1)
                pick_l = jnp.logical_and(lane8 >= pos, lane8 < pos + 4)
                pick_r = jnp.logical_and(lane8 >= (pos - 4) % w, lane8 < (pos - 4) % w + 4)
                acc_l = jnp.where(pick_l, moved, acc_l)
                acc_r = jnp.where(pick_r, moved, acc_r)
                uacc_l = jnp.where(pick_l, umoved, uacc_l)
                uacc_r = jnp.where(pick_r, umoved, uacc_r)
        xl_ref[b] = acc_l
        xr_ref[b] = acc_r
        ul_ref[b] = uacc_l
        ur_ref[b] = uacc_r
        for p in range(LB // 2):
            a_hi = th_ref[first + 2 * p, cz - 8:cz, :]
            b_hi = th_ref[first + 2 * p + 1, cz - 8:cz, :]
            zl_ref[b * (LB // 2) + p] = jnp.where(sub8 < 4, pltpu.roll(a_hi, 4, 0), b_hi)
            a_lo = th_ref[first + 2 * p, 0:8, :]
            b_lo = th_ref[first + 2 * p + 1, 0:8, :]
            zr_ref[b * (LB // 2) + p] = jnp.where(sub8 < 4, a_lo, pltpu.roll(b_lo, 4, 0))
        return carry

    lax.fori_loop(0, nblocks, block, 0)


def layer_kernel(fluid, block_offset, lb, *refs):
    if fluid:
        (face_ref, wall_ref, contact_ref, th_ref, prev_ref, next_ref, st_ref,
         u_ref, v_ref, zb_ref, za_ref, xb_ref, xa_ref, xl_ref, xr_ref, ul_ref, ur_ref,
         _alias_ref, sn_ref, tn_ref, wallv_ref, contv_ref, ext_ref) = refs
    else:
        (face_ref, wall_ref, contact_ref, th_ref, prev_ref, next_ref, st_ref,
         bs_ref, _order_ref, sn_ref, int_ref, mine_ref, wallv_ref, contv_ref) = refs
    _, cz, w = th_ref.shape
    base = (pl.program_id(0) + block_offset) * lb

    @pl.when(pl.program_id(0) == 0)
    def _():
        sub = lax.broadcasted_iota(jnp.int32, (cz, w), 0)
        acc = jnp.zeros((cz, w), jnp.int32)
        for z in range(cz):
            acc = jnp.where(sub == z, wall_ref[z], acc)
        wallv_ref[...] = acc
        lane = lax.broadcasted_iota(jnp.int32, (cz, w), 1)
        cacc = jnp.zeros((cz, w), jnp.float32)
        for x in range(w):
            cacc = jnp.where(lane == x, contact_ref[x].astype(jnp.float32), cacc)
        contv_ref[...] = cacc

    wall = wallv_ref[...]
    contact = contv_ref[...]

    def face(y):
        both_solid = face_ref[0, y + 1]
        both_fluid = face_ref[2, y + 1]
        at_wall = face_ref[1, y + 1] * contact
        return jnp.where(y + 1 < wall, both_solid, jnp.where(y >= wall, both_fluid, at_wall))

    if fluid:
        lane = lax.broadcasted_iota(jnp.int32, (8, w), 1)
        nv = cz // 8
        slope_scale = -stream_courant / 60.0
        quarter = lane % 4
        miss_l = xb_ref[0] - xr_ref[0]
        miss_r = xa_ref[0] - xl_ref[0]

        def edge(miss, weights, left):
            acc = jnp.zeros((8, w), jnp.float32)
            for j, c in weights:
                if left:
                    term = jnp.where(quarter < j, pltpu.roll(miss, j, 1), 0.0)
                else:
                    term = jnp.where(quarter >= 4 - j, pltpu.roll(miss, w - j, 1), 0.0)
                acc = acc + c * term
            return acc

        fix_l = (slope_scale * ul_ref[0] * edge(miss_l, ((1, -45.0), (2, 9.0), (3, -1.0)), True)
                 - damping * edge(miss_l, ((1, -56.0), (2, 28.0), (3, -8.0), (4, 1.0)), True))
        fix_r = (slope_scale * ur_ref[0] * edge(miss_r, ((1, 45.0), (2, -9.0), (3, 1.0)), False)
                 - damping * edge(miss_r, ((1, -56.0), (2, 28.0), (3, -8.0), (4, 1.0)), False))

    heads = []
    face_dn = face(base - 1)
    for s in range(lb):
        y = base + s
        t = th_ref[s]
        tp = th_ref[s - 1] if s > 0 else prev_ref[0]
        tn = th_ref[s + 1] if s < lb - 1 else next_ref[0]
        face_up = face(y)
        normal = face_up * (tn - t) - face_dn * (t - tp)
        face_dn = face_up
        if fluid:
            u = u_ref[s].astype(jnp.float32)
            v = v_ref[s].astype(jnp.float32)
            xm = [None] + [pltpu.roll(t, j, 1) for j in range(1, 5)]
            xp = [None] + [pltpu.roll(t, w - j, 1) for j in range(1, 5)]
            fixes = []
            for g in range(nv):
                pos = 4 * LB * g + 4 * s
                at_l = jnp.logical_and(lane >= pos, lane < pos + 4)
                at_r = jnp.logical_and(lane >= (pos - 4) % w, lane < (pos - 4) % w + 4)
                picked = jnp.where(at_l, fix_l, jnp.where(at_r, fix_r, 0.0))
                fixes.append(pltpu.roll(picked, (w - pos) % w, 1))
            fix = jnp.concatenate(fixes, axis=0)
            packed_b = zb_ref[s // 2]
            packed_a = za_ref[s // 2]
            if s % 2 == 0:
                packed_b = pltpu.roll(packed_b, 4, 0)
            else:
                packed_a = pltpu.roll(packed_a, 4, 0)
            ext_ref[0:8, :] = packed_b
            ext_ref[8:8 + cz, :] = t
            ext_ref[8 + cz:16 + cz, :] = packed_a
            zm = [None] + [ext_ref[8 - j:8 - j + cz, :] for j in range(1, 5)]
            zp = [None] + [ext_ref[8 + j:8 + j + cz, :] for j in range(1, 5)]

            def slope(m, p):
                return 45.0 * (p[1] - m[1]) - 9.0 * (p[2] - m[2]) + (p[3] - m[3])

            def smooth(m, p):
                return ((p[4] + m[4]) - 8.0 * (p[3] + m[3]) + 28.0 * (p[2] + m[2])
                        - 56.0 * (p[1] + m[1]))

            smoothing = smooth(zm, zp) + smooth(xm, xp) + 140.0 * t
            horiz = (slope_scale * (u * slope(xm, xp) + v * slope(zm, zp))
                     - damping * smoothing) + fix
            across = jnp.where(y >= wall, horiz, 0.0)
            rate = normal + across
        else:
            rate = normal
        sn = keep_factor * st_ref[s] + rate
        adv = t + section_weight * sn
        sn_ref[s] = sn
        if fluid:
            tn_ref[s] = adv
        else:
            inner = jnp.dot(bs_ref[s], adv[1:], precision=lax.Precision.HIGHEST,
                            preferred_element_type=jnp.float32)
            inner = jnp.concatenate([jnp.zeros((1, w), jnp.float32), inner], axis=0)
            int_ref[s] = inner
            heads.append((adv[0:1, :], inner[1:2, :], inner[cz - 1:cz, :]))
    if not fluid:
        for part in range(3):
            rows = jnp.concatenate([h[part] for h in heads], axis=0)
            for n in range(mine_ref.shape[0]):
                mine_ref[n, part] = rows


def local(theta, section_store, stream_speed, span_speed, conductivity, wall_layers,
          contact, spanwise_number, block_inverse):
    f32 = jnp.float32
    ny, cz, w = theta.shape
    ns = block_inverse.shape[0]
    nf = ny - ns
    nsb = ns // LB
    nfb = nf // LB
    ngz = lax.axis_size("gz")
    ngx = lax.axis_size("gx")


    solid_c = conductivity[0]
    fluid_c = conductivity[1]

    def harmonic(a, b):
        return 2.0 * a * b / (a + b)

    zero = jnp.zeros((1,), f32)
    faces = jnp.stack([
        jnp.concatenate([zero, harmonic(solid_c[:-1], solid_c[1:]), zero]),
        jnp.concatenate([zero, harmonic(solid_c[:-1], fluid_c[1:]), zero]),
        jnp.concatenate([zero, harmonic(fluid_c[:-1], fluid_c[1:]), zero]),
    ])

    smem = pl.BlockSpec(memory_space=pltpu.SMEM)
    blk = lambda off: pl.BlockSpec((LB, cz, w), lambda i: (i + off, 0, 0))
    prev_spec = lambda off: pl.BlockSpec((1, cz, w), lambda i: (jnp.maximum((i + off) * LB - 1, 0), 0, 0))
    next_spec = lambda off: pl.BlockSpec((1, cz, w), lambda i: (jnp.minimum((i + off) * LB + LB, ny - 1), 0, 0))
    edge_spec = pl.BlockSpec((1, 8, w), lambda i: (i, 0, 0))
    rows_spec = pl.BlockSpec((LB // 2, 8, w), lambda i: (i, 0, 0))

    xl, xr, ul, ur, zl, zr = pl.pallas_call(
        pack_kernel,
        grid=(1,),
        in_specs=[pl.BlockSpec((ny, cz, w), lambda i: (0, 0, 0))] * 2,
        out_specs=[pl.BlockSpec((nfb, 8, w), lambda i: (0, 0, 0))] * 4
        + [pl.BlockSpec((nf // 2, 8, w), lambda i: (0, 0, 0))] * 2,
        out_shape=[jax.ShapeDtypeStruct((nfb, 8, w), f32)] * 4
        + [jax.ShapeDtypeStruct((nf // 2, 8, w), f32)] * 2,
    )(theta, stream_speed)

    xb = lax.ppermute(xr, "gx", [(i, i + 1) for i in range(ngx - 1)])
    xa = lax.ppermute(xl, "gx", [(i + 1, i) for i in range(ngx - 1)])
    zb = lax.ppermute(zl, "gz", [(i, (i + 1) % ngz) for i in range(ngz)])
    za = lax.ppermute(zr, "gz", [((i + 1) % ngz, i) for i in range(ngz)])


    sb = 2 * LB if ns % (2 * LB) == 0 else LB
    sblk = pl.BlockSpec((sb, cz, w), lambda i: (i, 0, 0))
    sn_part, interior, spread = pl.pallas_call(
        lambda *refs: layer_kernel(False, 0, sb, *refs),
        grid=(ns // sb,),
        in_specs=[smem, smem, smem, sblk,
                  pl.BlockSpec((1, cz, w), lambda i: (jnp.maximum(i * sb - 1, 0), 0, 0)),
                  pl.BlockSpec((1, cz, w), lambda i: (jnp.minimum(i * sb + sb, ny - 1), 0, 0)),
                  sblk,
                  pl.BlockSpec((sb, cz - 1, cz - 1), lambda i: (i, 0, 0)),
                  pl.BlockSpec(memory_space=pl.ANY)],
        out_specs=[sblk, sblk, pl.BlockSpec((ngz, 3, sb, w), lambda i: (0, 0, i, 0))],
        out_shape=[
            jax.ShapeDtypeStruct((ny, cz, w), f32),
            jax.ShapeDtypeStruct((ns, cz, w), f32),
            jax.ShapeDtypeStruct((ngz, 3, ns, w), f32),
        ],
        scratch_shapes=[pltpu.VMEM((cz, w), jnp.int32), pltpu.VMEM((cz, w), f32)],
    )(faces, wall_layers, contact, theta, theta, theta, section_store, block_inverse, zr)

    number = spanwise_number
    blocks = lax.all_to_all(spread, "gz", 0, 0, tiled=True)
    left = jnp.roll(blocks[:, 2], 1, axis=0)
    targets = blocks[:, 0] + number[None, :, None] * left + number[None, :, None] * blocks[:, 1]

    square = number * number
    diagonal = 1.0 + 2.0 * number - square * (block_inverse[:, 0, 0] + block_inverse[:, -1, -1])
    beside = square * block_inverse[:, 0, -1]
    q = jnp.arange(ngz, dtype=jnp.int32)
    angle = (2.0 * math.pi / ngz) * q.astype(f32)
    denominator = diagonal[:, None] - 2.0 * beside[:, None] * jnp.cos(angle)[None, :]
    k = lax.axis_index("gz")

    def weights(shift):
        m = (q - shift) % ngz
        phase = (2.0 * math.pi / ngz) * ((q[:, None] * m[None, :]) % ngz).astype(f32)
        return jnp.sum(jnp.cos(phase)[None, :, :] / denominator[:, :, None], axis=1) / ngz

    head_values = jnp.sum(weights(k).T[:, :, None] * targets, axis=0)
    following = jnp.sum(weights(k + 1).T[:, :, None] * targets, axis=0)

    fluid_sn, fluid_tn = pl.pallas_call(
        lambda *refs: layer_kernel(True, nsb, LB, *refs),
        grid=(nfb,),
        in_specs=[smem, smem, smem, blk(nsb), prev_spec(nsb), next_spec(nsb), blk(nsb),
                  blk(nsb), blk(nsb), rows_spec, rows_spec, edge_spec, edge_spec,
                  edge_spec, edge_spec, edge_spec, edge_spec,
                  pl.BlockSpec(memory_space=pl.ANY)],
        out_specs=[blk(nsb), blk(nsb)],
        out_shape=[
            jax.ShapeDtypeStruct((ny, cz, w), f32),
            jax.ShapeDtypeStruct((ny, cz, w), f32),
        ],
        scratch_shapes=[pltpu.VMEM((cz, w), jnp.int32), pltpu.VMEM((cz, w), f32),
                        pltpu.VMEM((cz + 16, w), f32)],
        input_output_aliases={17: 0},
    )(faces, wall_layers, contact, theta, theta, theta, section_store,
      stream_speed, span_speed, zb, za, xb, xa, xl, xr, ul, ur, sn_part)

    row = jnp.arange(cz, dtype=jnp.int32)
    col0 = jnp.zeros((ns, cz), f32).at[:, 1:].set(block_inverse[:, :, 0])
    col_last = jnp.zeros((ns, cz), f32).at[:, 1:].set(block_inverse[:, :, -1])
    scale = number[:, None, None]
    solved = interior + scale * (col0[:, :, None] * head_values[:, None, :]
                                 + col_last[:, :, None] * following[:, None, :])
    solved = jnp.where((row == 0)[None, :, None], head_values[:, None, :], solved)
    theta_new = lax.dynamic_update_slice_in_dim(fluid_tn, solved, 0, 0)
    return (theta_new, fluid_sn)


def solution(mesh):
    return jax.shard_map(
        local,
        mesh=mesh,
        in_specs=(
            P(None, "gz", "gx"),
            P(None, "gz", "gx"),
            P(None, "gz", "gx"),
            P(None, "gz", "gx"),
            P(),
            P("gz"),
            P("gx"),
            P(),
            P(),
        ),
        out_specs=(P(None, "gz", "gx"), P(None, "gz", "gx")),
        check_vma=False,
    )
```

```python
import math

import jax
import jax.numpy as jnp
from jax import lax
from jax.experimental import pallas as pl
from jax.experimental.pallas import tpu as pltpu
from jax.sharding import PartitionSpec as P

keep_factor = -5.0 / 9.0
section_weight = 15.0 / 16.0
stream_courant = 0.4
span_courant = 0.4
damping = 1.0 / 256.0

LB = 8


def pack_kernel(th_ref, u_ref, xl_ref, xr_ref, ul_ref, ur_ref):
    ny, cz, w = th_ref.shape
    nblocks = xl_ref.shape[0]
    skip = ny - nblocks * LB
    lane8 = lax.broadcasted_iota(jnp.int32, (8, w), 1)

    def block(b, carry):
        first = skip + b * LB
        acc_l = jnp.zeros((8, w), jnp.float32)
        acc_r = jnp.zeros((8, w), jnp.float32)
        uacc_l = jnp.zeros((8, w), jnp.float32)
        uacc_r = jnp.zeros((8, w), jnp.float32)
        for s in range(LB):
            speed = u_ref[first + s].astype(jnp.float32)
            for v in range(cz // 8):
                t = th_ref[first + s, 8 * v:8 * v + 8, :]
                pos = 4 * LB * v + 4 * s
                moved = pltpu.roll(t, pos % w, 1)
                umoved = pltpu.roll(speed[8 * v:8 * v + 8], pos % w, 1)
                pick_l = jnp.logical_and(lane8 >= pos, lane8 < pos + 4)
                pick_r = jnp.logical_and(lane8 >= (pos - 4) % w, lane8 < (pos - 4) % w + 4)
                acc_l = jnp.where(pick_l, moved, acc_l)
                acc_r = jnp.where(pick_r, moved, acc_r)
                uacc_l = jnp.where(pick_l, umoved, uacc_l)
                uacc_r = jnp.where(pick_r, umoved, uacc_r)
        xl_ref[b] = acc_l
        xr_ref[b] = acc_r
        ul_ref[b] = uacc_l
        ur_ref[b] = uacc_r
        return carry

    lax.fori_loop(0, nblocks, block, 0)


def layer_kernel(fluid, block_offset, lb, *refs):
    if fluid:
        (face_ref, wall_ref, contact_ref, th_ref, prev_ref, next_ref, st_ref,
         u_ref, v_ref, zb_ref, za_ref, xb_ref, xa_ref, xl_ref, xr_ref, ul_ref, ur_ref,
         _alias_ref, sn_ref, tn_ref, wallv_ref, contv_ref, ext_ref) = refs
    else:
        (face_ref, wall_ref, contact_ref, th_ref, prev_ref, next_ref, st_ref,
         bs_ref, _order_ref, sn_ref, int_ref, mine_ref, wallv_ref, contv_ref) = refs
    _, cz, w = th_ref.shape
    base = (pl.program_id(0) + block_offset) * lb

    @pl.when(pl.program_id(0) == 0)
    def _():
        sub = lax.broadcasted_iota(jnp.int32, (cz, w), 0)
        acc = jnp.zeros((cz, w), jnp.int32)
        for z in range(cz):
            acc = jnp.where(sub == z, wall_ref[z], acc)
        wallv_ref[...] = acc
        lane = lax.broadcasted_iota(jnp.int32, (cz, w), 1)
        cacc = jnp.zeros((cz, w), jnp.float32)
        for x in range(w):
            cacc = jnp.where(lane == x, contact_ref[x].astype(jnp.float32), cacc)
        contv_ref[...] = cacc

    wall = wallv_ref[...]
    contact = contv_ref[...]

    def face(y):
        both_solid = face_ref[0, y + 1]
        both_fluid = face_ref[2, y + 1]
        at_wall = face_ref[1, y + 1] * contact
        return jnp.where(y + 1 < wall, both_solid, jnp.where(y >= wall, both_fluid, at_wall))

    if fluid:
        lane = lax.broadcasted_iota(jnp.int32, (8, w), 1)
        nv = cz // 8
        slope_scale = -stream_courant / 60.0
        quarter = lane % 4
        miss_l = xb_ref[0] - xr_ref[0]
        miss_r = xa_ref[0] - xl_ref[0]

        def edge(miss, weights, left):
            acc = jnp.zeros((8, w), jnp.float32)
            for j, c in weights:
                if left:
                    term = jnp.where(quarter < j, pltpu.roll(miss, j, 1), 0.0)
                else:
                    term = jnp.where(quarter >= 4 - j, pltpu.roll(miss, w - j, 1), 0.0)
                acc = acc + c * term
            return acc

        fix_l = (slope_scale * ul_ref[0] * edge(miss_l, ((1, -45.0), (2, 9.0), (3, -1.0)), True)
                 - damping * edge(miss_l, ((1, -56.0), (2, 28.0), (3, -8.0), (4, 1.0)), True))
        fix_r = (slope_scale * ur_ref[0] * edge(miss_r, ((1, 45.0), (2, -9.0), (3, 1.0)), False)
                 - damping * edge(miss_r, ((1, -56.0), (2, 28.0), (3, -8.0), (4, 1.0)), False))

    heads = []
    face_dn = face(base - 1)
    for s in range(lb):
        y = base + s
        t = th_ref[s]
        tp = th_ref[s - 1] if s > 0 else prev_ref[0]
        tn = th_ref[s + 1] if s < lb - 1 else next_ref[0]
        face_up = face(y)
        normal = face_up * (tn - t) - face_dn * (t - tp)
        face_dn = face_up
        if fluid:
            u = u_ref[s].astype(jnp.float32)
            v = v_ref[s].astype(jnp.float32)
            xm = [None] + [pltpu.roll(t, j, 1) for j in range(1, 5)]
            xp = [None] + [pltpu.roll(t, w - j, 1) for j in range(1, 5)]
            fixes = []
            for g in range(nv):
                pos = 4 * LB * g + 4 * s
                at_l = jnp.logical_and(lane >= pos, lane < pos + 4)
                at_r = jnp.logical_and(lane >= (pos - 4) % w, lane < (pos - 4) % w + 4)
                picked = jnp.where(at_l, fix_l, jnp.where(at_r, fix_r, 0.0))
                fixes.append(pltpu.roll(picked, (w - pos) % w, 1))
            fix = jnp.concatenate(fixes, axis=0)
            ext_ref[0:8, :] = zb_ref[s]
            ext_ref[8:8 + cz, :] = t
            ext_ref[8 + cz:16 + cz, :] = za_ref[s]
            zm = [None] + [ext_ref[8 - j:8 - j + cz, :] for j in range(1, 5)]
            zp = [None] + [ext_ref[8 + j:8 + j + cz, :] for j in range(1, 5)]

            def slope(m, p):
                return 45.0 * (p[1] - m[1]) - 9.0 * (p[2] - m[2]) + (p[3] - m[3])

            def smooth(m, p):
                return ((p[4] + m[4]) - 8.0 * (p[3] + m[3]) + 28.0 * (p[2] + m[2])
                        - 56.0 * (p[1] + m[1]))

            smoothing = smooth(zm, zp) + smooth(xm, xp) + 140.0 * t
            horiz = (slope_scale * (u * slope(xm, xp) + v * slope(zm, zp))
                     - damping * smoothing) + fix
            across = jnp.where(y >= wall, horiz, 0.0)
            rate = normal + across
        else:
            rate = normal
        sn = keep_factor * st_ref[s] + rate
        adv = t + section_weight * sn
        sn_ref[s] = sn
        if fluid:
            tn_ref[s] = adv
        else:
            inner = jnp.dot(bs_ref[s], adv[1:], precision=lax.Precision.HIGHEST,
                            preferred_element_type=jnp.float32)
            inner = jnp.concatenate([jnp.zeros((1, w), jnp.float32), inner], axis=0)
            int_ref[s] = inner
            heads.append((adv[0:1, :], inner[1:2, :], inner[cz - 1:cz, :]))
    if not fluid:
        for part in range(3):
            rows = jnp.concatenate([h[part] for h in heads], axis=0)
            for n in range(mine_ref.shape[0]):
                mine_ref[n, part] = rows


def local(theta, section_store, stream_speed, span_speed, conductivity, wall_layers,
          contact, spanwise_number, block_inverse):
    f32 = jnp.float32
    ny, cz, w = theta.shape
    ns = block_inverse.shape[0]
    nf = ny - ns
    nsb = ns // LB
    nfb = nf // LB
    ngz = lax.axis_size("gz")
    ngx = lax.axis_size("gx")


    solid_c = conductivity[0]
    fluid_c = conductivity[1]

    def harmonic(a, b):
        return 2.0 * a * b / (a + b)

    zero = jnp.zeros((1,), f32)
    faces = jnp.stack([
        jnp.concatenate([zero, harmonic(solid_c[:-1], solid_c[1:]), zero]),
        jnp.concatenate([zero, harmonic(solid_c[:-1], fluid_c[1:]), zero]),
        jnp.concatenate([zero, harmonic(fluid_c[:-1], fluid_c[1:]), zero]),
    ])

    smem = pl.BlockSpec(memory_space=pltpu.SMEM)
    blk = lambda off: pl.BlockSpec((LB, cz, w), lambda i: (i + off, 0, 0))
    prev_spec = lambda off: pl.BlockSpec((1, cz, w), lambda i: (jnp.maximum((i + off) * LB - 1, 0), 0, 0))
    next_spec = lambda off: pl.BlockSpec((1, cz, w), lambda i: (jnp.minimum((i + off) * LB + LB, ny - 1), 0, 0))
    edge_spec = pl.BlockSpec((1, 8, w), lambda i: (i, 0, 0))
    rows_spec = pl.BlockSpec((LB, 8, w), lambda i: (i, 0, 0))

    zb = lax.ppermute(theta[ns:, cz - 8:, :], "gz", [(i, (i + 1) % ngz) for i in range(ngz)])
    za = lax.ppermute(theta[ns:, :8, :], "gz", [((i + 1) % ngz, i) for i in range(ngz)])

    xl, xr, ul, ur = pl.pallas_call(
        pack_kernel,
        grid=(1,),
        in_specs=[pl.BlockSpec((ny, cz, w), lambda i: (0, 0, 0))] * 2,
        out_specs=[pl.BlockSpec((nfb, 8, w), lambda i: (0, 0, 0))] * 4,
        out_shape=[jax.ShapeDtypeStruct((nfb, 8, w), f32)] * 4,
    )(theta, stream_speed)

    xb = lax.ppermute(xr, "gx", [(i, i + 1) for i in range(ngx - 1)])
    xa = lax.ppermute(xl, "gx", [(i + 1, i) for i in range(ngx - 1)])

    sb = 2 * LB if ns % (2 * LB) == 0 else LB
    sblk = pl.BlockSpec((sb, cz, w), lambda i: (i, 0, 0))
    sn_part, interior, spread = pl.pallas_call(
        lambda *refs: layer_kernel(False, 0, sb, *refs),
        grid=(ns // sb,),
        in_specs=[smem, smem, smem, sblk,
                  pl.BlockSpec((1, cz, w), lambda i: (jnp.maximum(i * sb - 1, 0), 0, 0)),
                  pl.BlockSpec((1, cz, w), lambda i: (jnp.minimum(i * sb + sb, ny - 1), 0, 0)),
                  sblk,
                  pl.BlockSpec((sb, cz - 1, cz - 1), lambda i: (i, 0, 0)),
                  pl.BlockSpec(memory_space=pl.ANY)],
        out_specs=[sblk, sblk, pl.BlockSpec((ngz, 3, sb, w), lambda i: (0, 0, i, 0))],
        out_shape=[
            jax.ShapeDtypeStruct((ny, cz, w), f32),
            jax.ShapeDtypeStruct((ns, cz, w), f32),
            jax.ShapeDtypeStruct((ngz, 3, ns, w), f32),
        ],
        scratch_shapes=[pltpu.VMEM((cz, w), jnp.int32), pltpu.VMEM((cz, w), f32)],
    )(faces, wall_layers, contact, theta, theta, theta, section_store, block_inverse, xr)

    number = spanwise_number
    blocks = lax.all_to_all(spread, "gz", 0, 0, tiled=True)
    left = jnp.roll(blocks[:, 2], 1, axis=0)
    targets = blocks[:, 0] + number[None, :, None] * left + number[None, :, None] * blocks[:, 1]

    square = number * number
    diagonal = 1.0 + 2.0 * number - square * (block_inverse[:, 0, 0] + block_inverse[:, -1, -1])
    beside = square * block_inverse[:, 0, -1]
    q = jnp.arange(ngz, dtype=jnp.int32)
    angle = (2.0 * math.pi / ngz) * q.astype(f32)
    denominator = diagonal[:, None] - 2.0 * beside[:, None] * jnp.cos(angle)[None, :]
    k = lax.axis_index("gz")

    def weights(shift):
        m = (q - shift) % ngz
        phase = (2.0 * math.pi / ngz) * ((q[:, None] * m[None, :]) % ngz).astype(f32)
        return jnp.sum(jnp.cos(phase)[None, :, :] / denominator[:, :, None], axis=1) / ngz

    head_values = jnp.sum(weights(k).T[:, :, None] * targets, axis=0)
    following = jnp.sum(weights(k + 1).T[:, :, None] * targets, axis=0)

    fluid_sn, fluid_tn = pl.pallas_call(
        lambda *refs: layer_kernel(True, nsb, LB, *refs),
        grid=(nfb,),
        in_specs=[smem, smem, smem, blk(nsb), prev_spec(nsb), next_spec(nsb), blk(nsb),
                  blk(nsb), blk(nsb), rows_spec, rows_spec, edge_spec, edge_spec,
                  edge_spec, edge_spec, edge_spec, edge_spec,
                  pl.BlockSpec(memory_space=pl.ANY)],
        out_specs=[blk(nsb), blk(nsb)],
        out_shape=[
            jax.ShapeDtypeStruct((ny, cz, w), f32),
            jax.ShapeDtypeStruct((ny, cz, w), f32),
        ],
        scratch_shapes=[pltpu.VMEM((cz, w), jnp.int32), pltpu.VMEM((cz, w), f32),
                        pltpu.VMEM((cz + 16, w), f32)],
        input_output_aliases={17: 0},
    )(faces, wall_layers, contact, theta, theta, theta, section_store,
      stream_speed, span_speed, zb, za, xb, xa, xl, xr, ul, ur, sn_part)

    row = jnp.arange(cz, dtype=jnp.int32)
    col0 = jnp.zeros((ns, cz), f32).at[:, 1:].set(block_inverse[:, :, 0])
    col_last = jnp.zeros((ns, cz), f32).at[:, 1:].set(block_inverse[:, :, -1])
    scale = number[:, None, None]
    solved = interior + scale * (col0[:, :, None] * head_values[:, None, :]
                                 + col_last[:, :, None] * following[:, None, :])
    solved = jnp.where((row == 0)[None, :, None], head_values[:, None, :], solved)
    theta_new = lax.dynamic_update_slice_in_dim(fluid_tn, solved, 0, 0)
    return (theta_new, fluid_sn)


def solution(mesh):
    return jax.shard_map(
        local,
        mesh=mesh,
        in_specs=(
            P(None, "gz", "gx"),
            P(None, "gz", "gx"),
            P(None, "gz", "gx"),
            P(None, "gz", "gx"),
            P(),
            P("gz"),
            P("gx"),
            P(),
            P(),
        ),
        out_specs=(P(None, "gz", "gx"), P(None, "gz", "gx")),
        check_vma=False,
    )
```

```python
import math

import jax
import jax.numpy as jnp
from jax import lax
from jax.experimental import pallas as pl
from jax.experimental.pallas import tpu as pltpu
from jax.sharding import PartitionSpec as P

keep_factor = -5.0 / 9.0
section_weight = 15.0 / 16.0
stream_courant = 0.4
span_courant = 0.4
damping = 1.0 / 256.0

LB = 8


def pack_kernel(th_ref, u_ref, xl_ref, xr_ref, ul_ref, ur_ref, zl_ref, zr_ref):
    ny, cz, w = th_ref.shape
    nblocks = xl_ref.shape[0]
    skip = ny - nblocks * LB
    lane8 = lax.broadcasted_iota(jnp.int32, (8, w), 1)
    sub8 = lax.broadcasted_iota(jnp.int32, (8, w), 0)

    def block(b, carry):
        first = skip + b * LB
        acc_l = jnp.zeros((8, w), jnp.float32)
        acc_r = jnp.zeros((8, w), jnp.float32)
        uacc_l = jnp.zeros((8, w), jnp.float32)
        uacc_r = jnp.zeros((8, w), jnp.float32)
        for s in range(LB):
            speed = u_ref[first + s].astype(jnp.float32)
            for v in range(cz // 8):
                t = th_ref[first + s, 8 * v:8 * v + 8, :]
                pos = 4 * LB * v + 4 * s
                moved = pltpu.roll(t, pos % w, 1)
                umoved = pltpu.roll(speed[8 * v:8 * v + 8], pos % w, 1)
                pick_l = jnp.logical_and(lane8 >= pos, lane8 < pos + 4)
                pick_r = jnp.logical_and(lane8 >= (pos - 4) % w, lane8 < (pos - 4) % w + 4)
                acc_l = jnp.where(pick_l, moved, acc_l)
                acc_r = jnp.where(pick_r, moved, acc_r)
                uacc_l = jnp.where(pick_l, umoved, uacc_l)
                uacc_r = jnp.where(pick_r, umoved, uacc_r)
        xl_ref[b] = acc_l
        xr_ref[b] = acc_r
        ul_ref[b] = uacc_l
        ur_ref[b] = uacc_r
        for p in range(LB // 2):
            a_hi = th_ref[first + 2 * p, cz - 8:cz, :]
            b_hi = th_ref[first + 2 * p + 1, cz - 8:cz, :]
            zl_ref[b * (LB // 2) + p] = jnp.where(sub8 < 4, pltpu.roll(a_hi, 4, 0), b_hi)
            a_lo = th_ref[first + 2 * p, 0:8, :]
            b_lo = th_ref[first + 2 * p + 1, 0:8, :]
            zr_ref[b * (LB // 2) + p] = jnp.where(sub8 < 4, a_lo, pltpu.roll(b_lo, 4, 0))
        return carry

    lax.fori_loop(0, nblocks, block, 0)


def layer_kernel(fluid, block_offset, lb, *refs):
    if fluid:
        (face_ref, wall_ref, contact_ref, th_ref, prev_ref, next_ref, st_ref,
         u_ref, v_ref, xb_ref, xa_ref, xl_ref, xr_ref, ul_ref, ur_ref,
         _alias_ref, sn_ref, tn_ref, wallv_ref, contv_ref, ext_ref) = refs
    else:
        (face_ref, wall_ref, contact_ref, th_ref, prev_ref, next_ref, st_ref,
         bs_ref, _order_ref, sn_ref, int_ref, mine_ref, wallv_ref, contv_ref) = refs
    _, cz, w = th_ref.shape
    base = (pl.program_id(0) + block_offset) * lb

    @pl.when(pl.program_id(0) == 0)
    def _():
        sub = lax.broadcasted_iota(jnp.int32, (cz, w), 0)
        acc = jnp.zeros((cz, w), jnp.int32)
        for z in range(cz):
            acc = jnp.where(sub == z, wall_ref[z], acc)
        wallv_ref[...] = acc
        lane = lax.broadcasted_iota(jnp.int32, (cz, w), 1)
        cacc = jnp.zeros((cz, w), jnp.float32)
        for x in range(w):
            cacc = jnp.where(lane == x, contact_ref[x].astype(jnp.float32), cacc)
        contv_ref[...] = cacc

    wall = wallv_ref[...]
    contact = contv_ref[...]

    def face(y):
        both_solid = face_ref[0, y + 1]
        both_fluid = face_ref[2, y + 1]
        at_wall = face_ref[1, y + 1] * contact
        return jnp.where(y + 1 < wall, both_solid, jnp.where(y >= wall, both_fluid, at_wall))

    if fluid:
        lane = lax.broadcasted_iota(jnp.int32, (8, w), 1)
        nv = cz // 8
        slope_scale = -stream_courant / 60.0
        quarter = lane % 4
        miss_l = xb_ref[0] - xr_ref[0]
        miss_r = xa_ref[0] - xl_ref[0]

        def edge(miss, weights, left):
            acc = jnp.zeros((8, w), jnp.float32)
            for j, c in weights:
                if left:
                    term = jnp.where(quarter < j, pltpu.roll(miss, j, 1), 0.0)
                else:
                    term = jnp.where(quarter >= 4 - j, pltpu.roll(miss, w - j, 1), 0.0)
                acc = acc + c * term
            return acc

        fix_l = (slope_scale * ul_ref[0] * edge(miss_l, ((1, -45.0), (2, 9.0), (3, -1.0)), True)
                 - damping * edge(miss_l, ((1, -56.0), (2, 28.0), (3, -8.0), (4, 1.0)), True))
        fix_r = (slope_scale * ur_ref[0] * edge(miss_r, ((1, 45.0), (2, -9.0), (3, 1.0)), False)
                 - damping * edge(miss_r, ((1, -56.0), (2, 28.0), (3, -8.0), (4, 1.0)), False))

    heads = []
    face_dn = face(base - 1)
    for s in range(lb):
        y = base + s
        t = th_ref[s]
        tp = th_ref[s - 1] if s > 0 else prev_ref[0]
        tn = th_ref[s + 1] if s < lb - 1 else next_ref[0]
        face_up = face(y)
        normal = face_up * (tn - t) - face_dn * (t - tp)
        face_dn = face_up
        if fluid:
            u = u_ref[s].astype(jnp.float32)
            v = v_ref[s].astype(jnp.float32)
            xm = [None] + [pltpu.roll(t, j, 1) for j in range(1, 5)]
            xp = [None] + [pltpu.roll(t, w - j, 1) for j in range(1, 5)]
            fixes = []
            for g in range(nv):
                pos = 4 * LB * g + 4 * s
                at_l = jnp.logical_and(lane >= pos, lane < pos + 4)
                at_r = jnp.logical_and(lane >= (pos - 4) % w, lane < (pos - 4) % w + 4)
                picked = jnp.where(at_l, fix_l, jnp.where(at_r, fix_r, 0.0))
                fixes.append(pltpu.roll(picked, (w - pos) % w, 1))
            fix = jnp.concatenate(fixes, axis=0)
            ext_ref[0:8, :] = t[cz - 8:]
            ext_ref[8:8 + cz, :] = t
            ext_ref[8 + cz:16 + cz, :] = t[:8]
            zm = [None] + [ext_ref[8 - j:8 - j + cz, :] for j in range(1, 5)]
            zp = [None] + [ext_ref[8 + j:8 + j + cz, :] for j in range(1, 5)]

            def slope(m, p):
                return 45.0 * (p[1] - m[1]) - 9.0 * (p[2] - m[2]) + (p[3] - m[3])

            def smooth(m, p):
                return ((p[4] + m[4]) - 8.0 * (p[3] + m[3]) + 28.0 * (p[2] + m[2])
                        - 56.0 * (p[1] + m[1]))

            smoothing = smooth(zm, zp) + smooth(xm, xp) + 140.0 * t
            horiz = (slope_scale * (u * slope(xm, xp) + v * slope(zm, zp))
                     - damping * smoothing) + fix
            across = jnp.where(y >= wall, horiz, 0.0)
            rate = normal + across
        else:
            rate = normal
        sn = keep_factor * st_ref[s] + rate
        adv = t + section_weight * sn
        sn_ref[s] = sn
        if fluid:
            tn_ref[s] = adv
        else:
            inner = jnp.dot(bs_ref[s], adv[1:], precision=lax.Precision.HIGHEST,
                            preferred_element_type=jnp.float32)
            inner = jnp.concatenate([jnp.zeros((1, w), jnp.float32), inner], axis=0)
            int_ref[s] = inner
            heads.append((adv[0:1, :], inner[1:2, :], inner[cz - 1:cz, :]))
    if not fluid:
        for part in range(3):
            rows = jnp.concatenate([h[part] for h in heads], axis=0)
            for n in range(mine_ref.shape[0]):
                mine_ref[n, part] = rows


def span_fix_kernel(wall_ref, zb_ref, za_ref, zl_ref, zr_ref, v_ref, sn_in, tn_in,
                    sn_out, tn_out, top_sn, bot_sn, top_tn, bot_tn, sems):
    ny, cz, w = v_ref.shape
    nf = top_sn.shape[0]
    ns = ny - nf
    loads = [
        pltpu.make_async_copy(sn_in.at[pl.ds(ns, nf), pl.ds(0, 8), :], top_sn, sems.at[0]),
        pltpu.make_async_copy(sn_in.at[pl.ds(ns, nf), pl.ds(cz - 8, 8), :], bot_sn, sems.at[1]),
        pltpu.make_async_copy(tn_in.at[pl.ds(ns, nf), pl.ds(0, 8), :], top_tn, sems.at[2]),
        pltpu.make_async_copy(tn_in.at[pl.ds(ns, nf), pl.ds(cz - 8, 8), :], bot_tn, sems.at[3]),
    ]
    for c in loads:
        c.start()
    sub = lax.broadcasted_iota(jnp.int32, (8, w), 0)
    wall_top = jnp.zeros((8, w), jnp.int32)
    wall_bot = jnp.zeros((8, w), jnp.int32)
    for z in range(8):
        wall_top = jnp.where(sub == z, wall_ref[z], wall_top)
        wall_bot = jnp.where(sub == z, wall_ref[cz - 8 + z], wall_bot)
    slope_scale = -span_courant / 60.0
    for c in loads:
        c.wait()

    def pair(p, carry):
        miss_top = zb_ref[p] - zl_ref[p]
        miss_bot = za_ref[p] - zr_ref[p]
        for h in range(2):
            f = 2 * p + h
            y = ns + f
            d_top = pltpu.roll(miss_top, 4, 0) if h == 0 else miss_top
            d_top = jnp.where(sub >= 4, d_top, 0.0)
            d_bot = miss_bot if h == 0 else pltpu.roll(miss_bot, 4, 0)
            d_bot = jnp.where(sub < 4, d_bot, 0.0)
            s_top = jnp.zeros((8, w), jnp.float32)
            m_top = jnp.zeros((8, w), jnp.float32)
            s_bot = jnp.zeros((8, w), jnp.float32)
            m_bot = jnp.zeros((8, w), jnp.float32)
            for j, cs, cm in ((1, -45.0, -56.0), (2, 9.0, 28.0), (3, -1.0, -8.0), (4, 0.0, 1.0)):
                lo = jnp.where(sub < j, pltpu.roll(d_top, j, 0), 0.0)
                hi = jnp.where(sub >= 8 - j, pltpu.roll(d_bot, 8 - j, 0), 0.0)
                if cs != 0.0:
                    s_top = s_top + cs * lo
                    s_bot = s_bot - cs * hi
                m_top = m_top + cm * lo
                m_bot = m_bot + cm * hi
            v_top = v_ref[y, 0:8, :].astype(jnp.float32)
            v_bot = v_ref[y, cz - 8:cz, :].astype(jnp.float32)
            fix_top = jnp.where(y >= wall_top, slope_scale * v_top * s_top - damping * m_top, 0.0)
            fix_bot = jnp.where(y >= wall_bot, slope_scale * v_bot * s_bot - damping * m_bot, 0.0)
            top_sn[f] = top_sn[f] + fix_top
            bot_sn[f] = bot_sn[f] + fix_bot
            top_tn[f] = top_tn[f] + section_weight * fix_top
            bot_tn[f] = bot_tn[f] + section_weight * fix_bot
        return carry

    lax.fori_loop(0, nf // 2, pair, 0)
    stores = [
        pltpu.make_async_copy(top_sn, sn_out.at[pl.ds(ns, nf), pl.ds(0, 8), :], sems.at[4]),
        pltpu.make_async_copy(bot_sn, sn_out.at[pl.ds(ns, nf), pl.ds(cz - 8, 8), :], sems.at[5]),
        pltpu.make_async_copy(top_tn, tn_out.at[pl.ds(ns, nf), pl.ds(0, 8), :], sems.at[6]),
        pltpu.make_async_copy(bot_tn, tn_out.at[pl.ds(ns, nf), pl.ds(cz - 8, 8), :], sems.at[7]),
    ]
    for c in stores:
        c.start()
    for c in stores:
        c.wait()


def local(theta, section_store, stream_speed, span_speed, conductivity, wall_layers,
          contact, spanwise_number, block_inverse):
    f32 = jnp.float32
    ny, cz, w = theta.shape
    ns = block_inverse.shape[0]
    nf = ny - ns
    nsb = ns // LB
    nfb = nf // LB
    ngz = lax.axis_size("gz")
    ngx = lax.axis_size("gx")


    solid_c = conductivity[0]
    fluid_c = conductivity[1]

    def harmonic(a, b):
        return 2.0 * a * b / (a + b)

    zero = jnp.zeros((1,), f32)
    faces = jnp.stack([
        jnp.concatenate([zero, harmonic(solid_c[:-1], solid_c[1:]), zero]),
        jnp.concatenate([zero, harmonic(solid_c[:-1], fluid_c[1:]), zero]),
        jnp.concatenate([zero, harmonic(fluid_c[:-1], fluid_c[1:]), zero]),
    ])

    smem = pl.BlockSpec(memory_space=pltpu.SMEM)
    blk = lambda off: pl.BlockSpec((LB, cz, w), lambda i: (i + off, 0, 0))
    prev_spec = lambda off: pl.BlockSpec((1, cz, w), lambda i: (jnp.maximum((i + off) * LB - 1, 0), 0, 0))
    next_spec = lambda off: pl.BlockSpec((1, cz, w), lambda i: (jnp.minimum((i + off) * LB + LB, ny - 1), 0, 0))
    edge_spec = pl.BlockSpec((1, 8, w), lambda i: (i, 0, 0))
    rows_spec = pl.BlockSpec((LB // 2, 8, w), lambda i: (i, 0, 0))

    xl, xr, ul, ur, zl, zr = pl.pallas_call(
        pack_kernel,
        grid=(1,),
        in_specs=[pl.BlockSpec((ny, cz, w), lambda i: (0, 0, 0))] * 2,
        out_specs=[pl.BlockSpec((nfb, 8, w), lambda i: (0, 0, 0))] * 4
        + [pl.BlockSpec((nf // 2, 8, w), lambda i: (0, 0, 0))] * 2,
        out_shape=[jax.ShapeDtypeStruct((nfb, 8, w), f32)] * 4
        + [jax.ShapeDtypeStruct((nf // 2, 8, w), f32)] * 2,
    )(theta, stream_speed)

    xb = lax.ppermute(xr, "gx", [(i, i + 1) for i in range(ngx - 1)])
    xa = lax.ppermute(xl, "gx", [(i + 1, i) for i in range(ngx - 1)])
    zb = lax.ppermute(zl, "gz", [(i, (i + 1) % ngz) for i in range(ngz)])
    za = lax.ppermute(zr, "gz", [((i + 1) % ngz, i) for i in range(ngz)])


    sb = 2 * LB if ns % (2 * LB) == 0 else LB
    sblk = pl.BlockSpec((sb, cz, w), lambda i: (i, 0, 0))
    sn_part, interior, spread = pl.pallas_call(
        lambda *refs: layer_kernel(False, 0, sb, *refs),
        grid=(ns // sb,),
        in_specs=[smem, smem, smem, sblk,
                  pl.BlockSpec((1, cz, w), lambda i: (jnp.maximum(i * sb - 1, 0), 0, 0)),
                  pl.BlockSpec((1, cz, w), lambda i: (jnp.minimum(i * sb + sb, ny - 1), 0, 0)),
                  sblk,
                  pl.BlockSpec((sb, cz - 1, cz - 1), lambda i: (i, 0, 0)),
                  pl.BlockSpec(memory_space=pl.ANY)],
        out_specs=[sblk, sblk, pl.BlockSpec((ngz, 3, sb, w), lambda i: (0, 0, i, 0))],
        out_shape=[
            jax.ShapeDtypeStruct((ny, cz, w), f32),
            jax.ShapeDtypeStruct((ns, cz, w), f32),
            jax.ShapeDtypeStruct((ngz, 3, ns, w), f32),
        ],
        scratch_shapes=[pltpu.VMEM((cz, w), jnp.int32), pltpu.VMEM((cz, w), f32)],
    )(faces, wall_layers, contact, theta, theta, theta, section_store, block_inverse, zr)

    number = spanwise_number
    blocks = lax.all_to_all(spread, "gz", 0, 0, tiled=True)
    left = jnp.roll(blocks[:, 2], 1, axis=0)
    targets = blocks[:, 0] + number[None, :, None] * left + number[None, :, None] * blocks[:, 1]

    square = number * number
    diagonal = 1.0 + 2.0 * number - square * (block_inverse[:, 0, 0] + block_inverse[:, -1, -1])
    beside = square * block_inverse[:, 0, -1]
    q = jnp.arange(ngz, dtype=jnp.int32)
    angle = (2.0 * math.pi / ngz) * q.astype(f32)
    denominator = diagonal[:, None] - 2.0 * beside[:, None] * jnp.cos(angle)[None, :]
    k = lax.axis_index("gz")

    def weights(shift):
        m = (q - shift) % ngz
        phase = (2.0 * math.pi / ngz) * ((q[:, None] * m[None, :]) % ngz).astype(f32)
        return jnp.sum(jnp.cos(phase)[None, :, :] / denominator[:, :, None], axis=1) / ngz

    head_values = jnp.sum(weights(k).T[:, :, None] * targets, axis=0)
    following = jnp.sum(weights(k + 1).T[:, :, None] * targets, axis=0)

    fluid_sn, fluid_tn = pl.pallas_call(
        lambda *refs: layer_kernel(True, nsb, LB, *refs),
        grid=(nfb,),
        in_specs=[smem, smem, smem, blk(nsb), prev_spec(nsb), next_spec(nsb), blk(nsb),
                  blk(nsb), blk(nsb), edge_spec, edge_spec,
                  edge_spec, edge_spec, edge_spec, edge_spec,
                  pl.BlockSpec(memory_space=pl.ANY)],
        out_specs=[blk(nsb), blk(nsb)],
        out_shape=[
            jax.ShapeDtypeStruct((ny, cz, w), f32),
            jax.ShapeDtypeStruct((ny, cz, w), f32),
        ],
        scratch_shapes=[pltpu.VMEM((cz, w), jnp.int32), pltpu.VMEM((cz, w), f32),
                        pltpu.VMEM((cz + 16, w), f32)],
        input_output_aliases={15: 0},
    )(faces, wall_layers, contact, theta, theta, theta, section_store,
      stream_speed, span_speed, xb, xa, xl, xr, ul, ur, sn_part)

    anyspec = pl.BlockSpec(memory_space=pl.ANY)
    whole = lambda shape: pl.BlockSpec(shape, lambda i: (0,) * len(shape))
    fluid_sn, fluid_tn = pl.pallas_call(
        span_fix_kernel,
        grid=(1,),
        in_specs=[smem] + [whole((nf // 2, 8, w))] * 4 + [whole((ny, cz, w)), anyspec, anyspec],
        out_specs=[anyspec, anyspec],
        out_shape=[jax.ShapeDtypeStruct((ny, cz, w), f32)] * 2,
        scratch_shapes=[pltpu.VMEM((nf, 8, w), f32)] * 4 + [pltpu.SemaphoreType.DMA((8,))],
        input_output_aliases={6: 0, 7: 1},
    )(wall_layers, zb, za, zl, zr, span_speed, fluid_sn, fluid_tn)

    row = jnp.arange(cz, dtype=jnp.int32)
    col0 = jnp.zeros((ns, cz), f32).at[:, 1:].set(block_inverse[:, :, 0])
    col_last = jnp.zeros((ns, cz), f32).at[:, 1:].set(block_inverse[:, :, -1])
    scale = number[:, None, None]
    solved = interior + scale * (col0[:, :, None] * head_values[:, None, :]
                                 + col_last[:, :, None] * following[:, None, :])
    solved = jnp.where((row == 0)[None, :, None], head_values[:, None, :], solved)
    theta_new = lax.dynamic_update_slice_in_dim(fluid_tn, solved, 0, 0)
    return (theta_new, fluid_sn)


def solution(mesh):
    return jax.shard_map(
        local,
        mesh=mesh,
        in_specs=(
            P(None, "gz", "gx"),
            P(None, "gz", "gx"),
            P(None, "gz", "gx"),
            P(None, "gz", "gx"),
            P(),
            P("gz"),
            P("gx"),
            P(),
            P(),
        ),
        out_specs=(P(None, "gz", "gx"), P(None, "gz", "gx")),
        check_vma=False,
    )
```

```python
import math

import jax
import jax.numpy as jnp
from jax import lax
from jax.experimental import pallas as pl
from jax.experimental.pallas import tpu as pltpu
from jax.sharding import PartitionSpec as P

keep_factor = -5.0 / 9.0
section_weight = 15.0 / 16.0
stream_courant = 0.4
span_courant = 0.4
damping = 1.0 / 256.0

LB = 8


def pack_kernel(th_ref, u_ref, xl_ref, xr_ref, ul_ref, ur_ref, zl_ref, zr_ref):
    ny, cz, w = th_ref.shape
    nblocks = xl_ref.shape[0]
    skip = ny - nblocks * LB
    lane8 = lax.broadcasted_iota(jnp.int32, (8, w), 1)
    sub8 = lax.broadcasted_iota(jnp.int32, (8, w), 0)

    def block(b, carry):
        first = skip + b * LB
        acc_l = jnp.zeros((8, w), jnp.float32)
        acc_r = jnp.zeros((8, w), jnp.float32)
        uacc_l = jnp.zeros((8, w), jnp.float32)
        uacc_r = jnp.zeros((8, w), jnp.float32)
        for s in range(LB):
            speed = u_ref[first + s].astype(jnp.float32)
            for v in range(cz // 8):
                t = th_ref[first + s, 8 * v:8 * v + 8, :]
                pos = 4 * LB * v + 4 * s
                moved = pltpu.roll(t, pos % w, 1)
                umoved = pltpu.roll(speed[8 * v:8 * v + 8], pos % w, 1)
                pick_l = jnp.logical_and(lane8 >= pos, lane8 < pos + 4)
                pick_r = jnp.logical_and(lane8 >= (pos - 4) % w, lane8 < (pos - 4) % w + 4)
                acc_l = jnp.where(pick_l, moved, acc_l)
                acc_r = jnp.where(pick_r, moved, acc_r)
                uacc_l = jnp.where(pick_l, umoved, uacc_l)
                uacc_r = jnp.where(pick_r, umoved, uacc_r)
        xl_ref[b] = acc_l
        xr_ref[b] = acc_r
        ul_ref[b] = uacc_l
        ur_ref[b] = uacc_r
        for p in range(LB // 2):
            a_hi = th_ref[first + 2 * p, cz - 8:cz, :]
            b_hi = th_ref[first + 2 * p + 1, cz - 8:cz, :]
            zl_ref[b * (LB // 2) + p] = jnp.where(sub8 < 4, pltpu.roll(a_hi, 4, 0), b_hi)
            a_lo = th_ref[first + 2 * p, 0:8, :]
            b_lo = th_ref[first + 2 * p + 1, 0:8, :]
            zr_ref[b * (LB // 2) + p] = jnp.where(sub8 < 4, a_lo, pltpu.roll(b_lo, 4, 0))
        return carry

    lax.fori_loop(0, nblocks, block, 0)


def layer_kernel(fluid, block_offset, lb, *refs):
    if fluid:
        (face_ref, wall_ref, contact_ref, th_ref, prev_ref, next_ref, st_ref,
         u_ref, v_ref, xb_ref, xa_ref, xl_ref, xr_ref, ul_ref, ur_ref,
         _alias_ref, sn_ref, tn_ref, wallv_ref, contv_ref, ext_ref) = refs
    else:
        (face_ref, wall_ref, contact_ref, th_ref, prev_ref, next_ref, st_ref,
         bs_ref, _order_ref, sn_ref, int_ref, mine_ref, wallv_ref, contv_ref) = refs
    _, cz, w = th_ref.shape
    base = (pl.program_id(0) + block_offset) * lb

    @pl.when(pl.program_id(0) == 0)
    def _():
        sub = lax.broadcasted_iota(jnp.int32, (cz, w), 0)
        acc = jnp.zeros((cz, w), jnp.int32)
        for z in range(cz):
            acc = jnp.where(sub == z, wall_ref[z], acc)
        wallv_ref[...] = acc
        lane = lax.broadcasted_iota(jnp.int32, (cz, w), 1)
        cacc = jnp.zeros((cz, w), jnp.float32)
        for x in range(w):
            cacc = jnp.where(lane == x, contact_ref[x].astype(jnp.float32), cacc)
        contv_ref[...] = cacc

    wall = wallv_ref[...]
    contact = contv_ref[...]

    def face(y):
        both_solid = face_ref[0, y + 1]
        both_fluid = face_ref[2, y + 1]
        at_wall = face_ref[1, y + 1] * contact
        return jnp.where(y + 1 < wall, both_solid, jnp.where(y >= wall, both_fluid, at_wall))

    if fluid:
        lane = lax.broadcasted_iota(jnp.int32, (8, w), 1)
        nv = cz // 8
        slope_scale = -stream_courant / 60.0
        quarter = lane % 4
        miss_l = xb_ref[0] - xr_ref[0]
        miss_r = xa_ref[0] - xl_ref[0]

        def edge(miss, weights, left):
            acc = jnp.zeros((8, w), jnp.float32)
            for j, c in weights:
                if left:
                    term = jnp.where(quarter < j, pltpu.roll(miss, j, 1), 0.0)
                else:
                    term = jnp.where(quarter >= 4 - j, pltpu.roll(miss, w - j, 1), 0.0)
                acc = acc + c * term
            return acc

        fix_l = (slope_scale * ul_ref[0] * edge(miss_l, ((1, -45.0), (2, 9.0), (3, -1.0)), True)
                 - damping * edge(miss_l, ((1, -56.0), (2, 28.0), (3, -8.0), (4, 1.0)), True))
        fix_r = (slope_scale * ur_ref[0] * edge(miss_r, ((1, 45.0), (2, -9.0), (3, 1.0)), False)
                 - damping * edge(miss_r, ((1, -56.0), (2, 28.0), (3, -8.0), (4, 1.0)), False))

    heads = []
    face_dn = face(base - 1)
    for s in range(lb):
        y = base + s
        t = th_ref[s]
        tp = th_ref[s - 1] if s > 0 else prev_ref[0]
        tn = th_ref[s + 1] if s < lb - 1 else next_ref[0]
        face_up = face(y)
        normal = face_up * (tn - t) - face_dn * (t - tp)
        face_dn = face_up
        if fluid:
            u = u_ref[s].astype(jnp.float32)
            v = v_ref[s].astype(jnp.float32)
            xm = [None] + [pltpu.roll(t, j, 1) for j in range(1, 5)]
            xp = [None] + [pltpu.roll(t, w - j, 1) for j in range(1, 5)]
            fixes = []
            for g in range(nv):
                pos = 4 * LB * g + 4 * s
                at_l = jnp.logical_and(lane >= pos, lane < pos + 4)
                at_r = jnp.logical_and(lane >= (pos - 4) % w, lane < (pos - 4) % w + 4)
                picked = jnp.where(at_l, fix_l, jnp.where(at_r, fix_r, 0.0))
                fixes.append(pltpu.roll(picked, (w - pos) % w, 1))
            fix = jnp.concatenate(fixes, axis=0)
            ext_ref[0:8, :] = t[cz - 8:]
            ext_ref[8:8 + cz, :] = t
            ext_ref[8 + cz:16 + cz, :] = t[:8]
            zm = [None] + [ext_ref[8 - j:8 - j + cz, :] for j in range(1, 5)]
            zp = [None] + [ext_ref[8 + j:8 + j + cz, :] for j in range(1, 5)]

            def slope(m, p):
                return 45.0 * (p[1] - m[1]) - 9.0 * (p[2] - m[2]) + (p[3] - m[3])

            def smooth(m, p):
                return ((p[4] + m[4]) - 8.0 * (p[3] + m[3]) + 28.0 * (p[2] + m[2])
                        - 56.0 * (p[1] + m[1]))

            smoothing = smooth(zm, zp) + smooth(xm, xp) + 140.0 * t
            horiz = (slope_scale * (u * slope(xm, xp) + v * slope(zm, zp))
                     - damping * smoothing) + fix
            across = jnp.where(y >= wall, horiz, 0.0)
            rate = normal + across
        else:
            rate = normal
        sn = keep_factor * st_ref[s] + rate
        adv = t + section_weight * sn
        sn_ref[s] = sn
        if fluid:
            tn_ref[s] = adv
        else:
            inner = jnp.dot(bs_ref[s], adv[1:], precision=lax.Precision.HIGHEST,
                            preferred_element_type=jnp.float32)
            inner = jnp.concatenate([jnp.zeros((1, w), jnp.float32), inner], axis=0)
            int_ref[s] = inner
            heads.append((adv[0:1, :], inner[1:2, :], inner[cz - 1:cz, :]))
    if not fluid:
        for part in range(3):
            rows = jnp.concatenate([h[part] for h in heads], axis=0)
            for n in range(mine_ref.shape[0]):
                mine_ref[n, part] = rows


def span_fix_kernel(wall_ref, zb_ref, za_ref, zl_ref, zr_ref, v_ref, sn_in, tn_in,
                    sn_out, tn_out, top_sn, bot_sn, top_tn, bot_tn, sems):
    ny, cz, w = v_ref.shape
    nf = top_sn.shape[0]
    ns = ny - nf
    loads = [
        pltpu.make_async_copy(sn_in.at[pl.ds(ns, nf), pl.ds(0, 8), :], top_sn, sems.at[0]),
        pltpu.make_async_copy(sn_in.at[pl.ds(ns, nf), pl.ds(cz - 8, 8), :], bot_sn, sems.at[1]),
        pltpu.make_async_copy(tn_in.at[pl.ds(ns, nf), pl.ds(0, 8), :], top_tn, sems.at[2]),
        pltpu.make_async_copy(tn_in.at[pl.ds(ns, nf), pl.ds(cz - 8, 8), :], bot_tn, sems.at[3]),
    ]
    for c in loads:
        c.start()
    sub = lax.broadcasted_iota(jnp.int32, (8, w), 0)
    wall_top = jnp.zeros((8, w), jnp.int32)
    wall_bot = jnp.zeros((8, w), jnp.int32)
    for z in range(8):
        wall_top = jnp.where(sub == z, wall_ref[z], wall_top)
        wall_bot = jnp.where(sub == z, wall_ref[cz - 8 + z], wall_bot)
    slope_scale = -span_courant / 60.0
    for c in loads:
        c.wait()

    def pair(p, carry):
        miss_top = zb_ref[p] - zl_ref[p]
        miss_bot = za_ref[p] - zr_ref[p]
        for h in range(2):
            f = 2 * p + h
            y = ns + f
            d_top = pltpu.roll(miss_top, 4, 0) if h == 0 else miss_top
            d_top = jnp.where(sub >= 4, d_top, 0.0)
            d_bot = miss_bot if h == 0 else pltpu.roll(miss_bot, 4, 0)
            d_bot = jnp.where(sub < 4, d_bot, 0.0)
            s_top = jnp.zeros((8, w), jnp.float32)
            m_top = jnp.zeros((8, w), jnp.float32)
            s_bot = jnp.zeros((8, w), jnp.float32)
            m_bot = jnp.zeros((8, w), jnp.float32)
            for j, cs, cm in ((1, -45.0, -56.0), (2, 9.0, 28.0), (3, -1.0, -8.0), (4, 0.0, 1.0)):
                lo = jnp.where(sub < j, pltpu.roll(d_top, j, 0), 0.0)
                hi = jnp.where(sub >= 8 - j, pltpu.roll(d_bot, 8 - j, 0), 0.0)
                if cs != 0.0:
                    s_top = s_top + cs * lo
                    s_bot = s_bot - cs * hi
                m_top = m_top + cm * lo
                m_bot = m_bot + cm * hi
            v_top = v_ref[y, 0:8, :].astype(jnp.float32)
            v_bot = v_ref[y, cz - 8:cz, :].astype(jnp.float32)
            fix_top = jnp.where(y >= wall_top, slope_scale * v_top * s_top - damping * m_top, 0.0)
            fix_bot = jnp.where(y >= wall_bot, slope_scale * v_bot * s_bot - damping * m_bot, 0.0)
            top_sn[f] = top_sn[f] + fix_top
            bot_sn[f] = bot_sn[f] + fix_bot
            top_tn[f] = top_tn[f] + section_weight * fix_top
            bot_tn[f] = bot_tn[f] + section_weight * fix_bot
        return carry

    lax.fori_loop(0, nf // 2, pair, 0, unroll=10)
    stores = [
        pltpu.make_async_copy(top_sn, sn_out.at[pl.ds(ns, nf), pl.ds(0, 8), :], sems.at[4]),
        pltpu.make_async_copy(bot_sn, sn_out.at[pl.ds(ns, nf), pl.ds(cz - 8, 8), :], sems.at[5]),
        pltpu.make_async_copy(top_tn, tn_out.at[pl.ds(ns, nf), pl.ds(0, 8), :], sems.at[6]),
        pltpu.make_async_copy(bot_tn, tn_out.at[pl.ds(ns, nf), pl.ds(cz - 8, 8), :], sems.at[7]),
    ]
    for c in stores:
        c.start()
    for c in stores:
        c.wait()


def local(theta, section_store, stream_speed, span_speed, conductivity, wall_layers,
          contact, spanwise_number, block_inverse):
    f32 = jnp.float32
    ny, cz, w = theta.shape
    ns = block_inverse.shape[0]
    nf = ny - ns
    nsb = ns // LB
    nfb = nf // LB
    ngz = lax.axis_size("gz")
    ngx = lax.axis_size("gx")


    solid_c = conductivity[0]
    fluid_c = conductivity[1]

    def harmonic(a, b):
        return 2.0 * a * b / (a + b)

    zero = jnp.zeros((1,), f32)
    faces = jnp.stack([
        jnp.concatenate([zero, harmonic(solid_c[:-1], solid_c[1:]), zero]),
        jnp.concatenate([zero, harmonic(solid_c[:-1], fluid_c[1:]), zero]),
        jnp.concatenate([zero, harmonic(fluid_c[:-1], fluid_c[1:]), zero]),
    ])

    smem = pl.BlockSpec(memory_space=pltpu.SMEM)
    blk = lambda off: pl.BlockSpec((LB, cz, w), lambda i: (i + off, 0, 0))
    prev_spec = lambda off: pl.BlockSpec((1, cz, w), lambda i: (jnp.maximum((i + off) * LB - 1, 0), 0, 0))
    next_spec = lambda off: pl.BlockSpec((1, cz, w), lambda i: (jnp.minimum((i + off) * LB + LB, ny - 1), 0, 0))
    edge_spec = pl.BlockSpec((1, 8, w), lambda i: (i, 0, 0))
    rows_spec = pl.BlockSpec((LB // 2, 8, w), lambda i: (i, 0, 0))

    xl, xr, ul, ur, zl, zr = pl.pallas_call(
        pack_kernel,
        grid=(1,),
        in_specs=[pl.BlockSpec((ny, cz, w), lambda i: (0, 0, 0))] * 2,
        out_specs=[pl.BlockSpec((nfb, 8, w), lambda i: (0, 0, 0))] * 4
        + [pl.BlockSpec((nf // 2, 8, w), lambda i: (0, 0, 0))] * 2,
        out_shape=[jax.ShapeDtypeStruct((nfb, 8, w), f32)] * 4
        + [jax.ShapeDtypeStruct((nf // 2, 8, w), f32)] * 2,
    )(theta, stream_speed)

    xb = lax.ppermute(xr, "gx", [(i, i + 1) for i in range(ngx - 1)])
    xa = lax.ppermute(xl, "gx", [(i + 1, i) for i in range(ngx - 1)])
    zb = lax.ppermute(zl, "gz", [(i, (i + 1) % ngz) for i in range(ngz)])
    za = lax.ppermute(zr, "gz", [((i + 1) % ngz, i) for i in range(ngz)])


    sb = 2 * LB if ns % (2 * LB) == 0 else LB
    sblk = pl.BlockSpec((sb, cz, w), lambda i: (i, 0, 0))
    sn_part, interior, spread = pl.pallas_call(
        lambda *refs: layer_kernel(False, 0, sb, *refs),
        grid=(ns // sb,),
        in_specs=[smem, smem, smem, sblk,
                  pl.BlockSpec((1, cz, w), lambda i: (jnp.maximum(i * sb - 1, 0), 0, 0)),
                  pl.BlockSpec((1, cz, w), lambda i: (jnp.minimum(i * sb + sb, ny - 1), 0, 0)),
                  sblk,
                  pl.BlockSpec((sb, cz - 1, cz - 1), lambda i: (i, 0, 0)),
                  pl.BlockSpec(memory_space=pl.ANY)],
        out_specs=[sblk, sblk, pl.BlockSpec((ngz, 3, sb, w), lambda i: (0, 0, i, 0))],
        out_shape=[
            jax.ShapeDtypeStruct((ny, cz, w), f32),
            jax.ShapeDtypeStruct((ns, cz, w), f32),
            jax.ShapeDtypeStruct((ngz, 3, ns, w), f32),
        ],
        scratch_shapes=[pltpu.VMEM((cz, w), jnp.int32), pltpu.VMEM((cz, w), f32)],
    )(faces, wall_layers, contact, theta, theta, theta, section_store, block_inverse, zr)

    number = spanwise_number
    blocks = lax.all_to_all(spread, "gz", 0, 0, tiled=True)
    left = jnp.roll(blocks[:, 2], 1, axis=0)
    targets = blocks[:, 0] + number[None, :, None] * left + number[None, :, None] * blocks[:, 1]

    square = number * number
    diagonal = 1.0 + 2.0 * number - square * (block_inverse[:, 0, 0] + block_inverse[:, -1, -1])
    beside = square * block_inverse[:, 0, -1]
    q = jnp.arange(ngz, dtype=jnp.int32)
    angle = (2.0 * math.pi / ngz) * q.astype(f32)
    denominator = diagonal[:, None] - 2.0 * beside[:, None] * jnp.cos(angle)[None, :]
    k = lax.axis_index("gz")

    def weights(shift):
        m = (q - shift) % ngz
        phase = (2.0 * math.pi / ngz) * ((q[:, None] * m[None, :]) % ngz).astype(f32)
        return jnp.sum(jnp.cos(phase)[None, :, :] / denominator[:, :, None], axis=1) / ngz

    head_values = jnp.sum(weights(k).T[:, :, None] * targets, axis=0)
    following = jnp.sum(weights(k + 1).T[:, :, None] * targets, axis=0)

    fluid_sn, fluid_tn = pl.pallas_call(
        lambda *refs: layer_kernel(True, nsb, LB, *refs),
        grid=(nfb,),
        in_specs=[smem, smem, smem, blk(nsb), prev_spec(nsb), next_spec(nsb), blk(nsb),
                  blk(nsb), blk(nsb), edge_spec, edge_spec,
                  edge_spec, edge_spec, edge_spec, edge_spec,
                  pl.BlockSpec(memory_space=pl.ANY)],
        out_specs=[blk(nsb), blk(nsb)],
        out_shape=[
            jax.ShapeDtypeStruct((ny, cz, w), f32),
            jax.ShapeDtypeStruct((ny, cz, w), f32),
        ],
        scratch_shapes=[pltpu.VMEM((cz, w), jnp.int32), pltpu.VMEM((cz, w), f32),
                        pltpu.VMEM((cz + 16, w), f32)],
        input_output_aliases={15: 0},
    )(faces, wall_layers, contact, theta, theta, theta, section_store,
      stream_speed, span_speed, xb, xa, xl, xr, ul, ur, sn_part)

    anyspec = pl.BlockSpec(memory_space=pl.ANY)
    whole = lambda shape: pl.BlockSpec(shape, lambda i: (0,) * len(shape))
    fluid_sn, fluid_tn = pl.pallas_call(
        span_fix_kernel,
        grid=(1,),
        in_specs=[smem] + [whole((nf // 2, 8, w))] * 4 + [whole((ny, cz, w)), anyspec, anyspec],
        out_specs=[anyspec, anyspec],
        out_shape=[jax.ShapeDtypeStruct((ny, cz, w), f32)] * 2,
        scratch_shapes=[pltpu.VMEM((nf, 8, w), f32)] * 4 + [pltpu.SemaphoreType.DMA((8,))],
        input_output_aliases={6: 0, 7: 1},
    )(wall_layers, zb, za, zl, zr, span_speed, fluid_sn, fluid_tn)

    row = jnp.arange(cz, dtype=jnp.int32)
    col0 = jnp.zeros((ns, cz), f32).at[:, 1:].set(block_inverse[:, :, 0])
    col_last = jnp.zeros((ns, cz), f32).at[:, 1:].set(block_inverse[:, :, -1])
    scale = number[:, None, None]
    solved = interior + scale * (col0[:, :, None] * head_values[:, None, :]
                                 + col_last[:, :, None] * following[:, None, :])
    solved = jnp.where((row == 0)[None, :, None], head_values[:, None, :], solved)
    theta_new = lax.dynamic_update_slice_in_dim(fluid_tn, solved, 0, 0)
    return (theta_new, fluid_sn)


def solution(mesh):
    return jax.shard_map(
        local,
        mesh=mesh,
        in_specs=(
            P(None, "gz", "gx"),
            P(None, "gz", "gx"),
            P(None, "gz", "gx"),
            P(None, "gz", "gx"),
            P(),
            P("gz"),
            P("gx"),
            P(),
            P(),
        ),
        out_specs=(P(None, "gz", "gx"), P(None, "gz", "gx")),
        check_vma=False,
    )
```

```python
import math

import jax
import jax.numpy as jnp
from jax import lax
from jax.experimental import pallas as pl
from jax.experimental.pallas import tpu as pltpu
from jax.sharding import PartitionSpec as P

keep_factor = -5.0 / 9.0
section_weight = 15.0 / 16.0
stream_courant = 0.4
span_courant = 0.4
damping = 1.0 / 256.0

LB = 8


def pack_kernel(th_ref, u_ref, xl_ref, xr_ref, ul_ref, ur_ref, zl_ref, zr_ref):
    ny, cz, w = th_ref.shape
    nblocks = xl_ref.shape[0]
    skip = ny - nblocks * LB
    lane8 = lax.broadcasted_iota(jnp.int32, (8, w), 1)
    sub8 = lax.broadcasted_iota(jnp.int32, (8, w), 0)

    def block(b, carry):
        first = skip + b * LB
        acc_l = jnp.zeros((8, w), jnp.float32)
        acc_r = jnp.zeros((8, w), jnp.float32)
        uacc_l = jnp.zeros((8, w), jnp.float32)
        uacc_r = jnp.zeros((8, w), jnp.float32)
        for s in range(LB):
            speed = u_ref[first + s].astype(jnp.float32)
            for v in range(cz // 8):
                t = th_ref[first + s, 8 * v:8 * v + 8, :]
                pos = 4 * LB * v + 4 * s
                moved = pltpu.roll(t, pos % w, 1)
                umoved = pltpu.roll(speed[8 * v:8 * v + 8], pos % w, 1)
                pick_l = jnp.logical_and(lane8 >= pos, lane8 < pos + 4)
                pick_r = jnp.logical_and(lane8 >= (pos - 4) % w, lane8 < (pos - 4) % w + 4)
                acc_l = jnp.where(pick_l, moved, acc_l)
                acc_r = jnp.where(pick_r, moved, acc_r)
                uacc_l = jnp.where(pick_l, umoved, uacc_l)
                uacc_r = jnp.where(pick_r, umoved, uacc_r)
        xl_ref[b] = acc_l
        xr_ref[b] = acc_r
        ul_ref[b] = uacc_l
        ur_ref[b] = uacc_r
        for p in range(LB // 2):
            a_hi = th_ref[first + 2 * p, cz - 8:cz, :]
            b_hi = th_ref[first + 2 * p + 1, cz - 8:cz, :]
            zl_ref[b * (LB // 2) + p] = jnp.where(sub8 < 4, pltpu.roll(a_hi, 4, 0), b_hi)
            a_lo = th_ref[first + 2 * p, 0:8, :]
            b_lo = th_ref[first + 2 * p + 1, 0:8, :]
            zr_ref[b * (LB // 2) + p] = jnp.where(sub8 < 4, a_lo, pltpu.roll(b_lo, 4, 0))
        return carry

    lax.fori_loop(0, nblocks, block, 0)


def layer_kernel(fluid, block_offset, lb, *refs):
    if fluid:
        (face_ref, wall_ref, contact_ref, th_ref, prev_ref, next_ref, st_ref,
         u_ref, v_ref, xb_ref, xa_ref, xl_ref, xr_ref, ul_ref, ur_ref,
         _alias_ref, sn_ref, tn_ref, wallv_ref, contv_ref, ext_ref) = refs
    else:
        (face_ref, wall_ref, contact_ref, th_ref, prev_ref, next_ref, st_ref,
         bs_ref, _order_ref, sn_ref, int_ref, mine_ref, wallv_ref, contv_ref) = refs
    _, cz, w = th_ref.shape
    base = (pl.program_id(0) + block_offset) * lb

    @pl.when(pl.program_id(0) == 0)
    def _():
        sub = lax.broadcasted_iota(jnp.int32, (cz, w), 0)
        acc = jnp.zeros((cz, w), jnp.int32)
        for z in range(cz):
            acc = jnp.where(sub == z, wall_ref[z], acc)
        wallv_ref[...] = acc
        lane = lax.broadcasted_iota(jnp.int32, (cz, w), 1)
        cacc = jnp.zeros((cz, w), jnp.float32)
        for x in range(w):
            cacc = jnp.where(lane == x, contact_ref[x].astype(jnp.float32), cacc)
        contv_ref[...] = cacc

    wall = wallv_ref[...]
    contact = contv_ref[...]

    def face(y):
        both_solid = face_ref[0, y + 1]
        both_fluid = face_ref[2, y + 1]
        at_wall = face_ref[1, y + 1] * contact
        return jnp.where(y + 1 < wall, both_solid, jnp.where(y >= wall, both_fluid, at_wall))

    if fluid:
        lane = lax.broadcasted_iota(jnp.int32, (8, w), 1)
        nv = cz // 8
        slope_scale = -stream_courant / 60.0
        quarter = lane % 4
        miss_l = xb_ref[0] - xr_ref[0]
        miss_r = xa_ref[0] - xl_ref[0]

        def edge(miss, weights, left):
            acc = jnp.zeros((8, w), jnp.float32)
            for j, c in weights:
                if left:
                    term = jnp.where(quarter < j, pltpu.roll(miss, j, 1), 0.0)
                else:
                    term = jnp.where(quarter >= 4 - j, pltpu.roll(miss, w - j, 1), 0.0)
                acc = acc + c * term
            return acc

        fix_l = (slope_scale * ul_ref[0] * edge(miss_l, ((1, -45.0), (2, 9.0), (3, -1.0)), True)
                 - damping * edge(miss_l, ((1, -56.0), (2, 28.0), (3, -8.0), (4, 1.0)), True))
        fix_r = (slope_scale * ur_ref[0] * edge(miss_r, ((1, 45.0), (2, -9.0), (3, 1.0)), False)
                 - damping * edge(miss_r, ((1, -56.0), (2, 28.0), (3, -8.0), (4, 1.0)), False))

    heads = []
    face_dn = face(base - 1)
    for s in range(lb):
        y = base + s
        t = th_ref[s]
        tp = th_ref[s - 1] if s > 0 else prev_ref[0]
        tn = th_ref[s + 1] if s < lb - 1 else next_ref[0]
        face_up = face(y)
        normal = face_up * (tn - t) - face_dn * (t - tp)
        face_dn = face_up
        if fluid:
            u = u_ref[s].astype(jnp.float32)
            v = v_ref[s].astype(jnp.float32)
            xm = [None] + [pltpu.roll(t, j, 1) for j in range(1, 5)]
            xp = [None] + [pltpu.roll(t, w - j, 1) for j in range(1, 5)]
            fixes = []
            for g in range(nv):
                pos = 4 * LB * g + 4 * s
                at_l = jnp.logical_and(lane >= pos, lane < pos + 4)
                at_r = jnp.logical_and(lane >= (pos - 4) % w, lane < (pos - 4) % w + 4)
                picked = jnp.where(at_l, fix_l, jnp.where(at_r, fix_r, 0.0))
                fixes.append(pltpu.roll(picked, (w - pos) % w, 1))
            fix = jnp.concatenate(fixes, axis=0)
            ext_ref[0:8, :] = t[cz - 8:]
            ext_ref[8:8 + cz, :] = t
            ext_ref[8 + cz:16 + cz, :] = t[:8]
            zm = [None] + [ext_ref[8 - j:8 - j + cz, :] for j in range(1, 5)]
            zp = [None] + [ext_ref[8 + j:8 + j + cz, :] for j in range(1, 5)]

            def slope(m, p):
                return 45.0 * (p[1] - m[1]) - 9.0 * (p[2] - m[2]) + (p[3] - m[3])

            def smooth(m, p):
                return ((p[4] + m[4]) - 8.0 * (p[3] + m[3]) + 28.0 * (p[2] + m[2])
                        - 56.0 * (p[1] + m[1]))

            smoothing = smooth(zm, zp) + smooth(xm, xp) + 140.0 * t
            horiz = (slope_scale * (u * slope(xm, xp) + v * slope(zm, zp))
                     - damping * smoothing) + fix
            across = jnp.where(y >= wall, horiz, 0.0)
            rate = normal + across
        else:
            rate = normal
        sn = keep_factor * st_ref[s] + rate
        adv = t + section_weight * sn
        sn_ref[s] = sn
        if fluid:
            tn_ref[s] = adv
        else:
            inner = jnp.dot(bs_ref[s], adv[1:], precision=lax.Precision.HIGHEST,
                            preferred_element_type=jnp.float32)
            inner = jnp.concatenate([jnp.zeros((1, w), jnp.float32), inner], axis=0)
            int_ref[s] = inner
            heads.append((adv[0:1, :], inner[1:2, :], inner[cz - 1:cz, :]))
    if not fluid:
        for part in range(3):
            rows = jnp.concatenate([h[part] for h in heads], axis=0)
            for n in range(mine_ref.shape[0]):
                mine_ref[n, part] = rows


def span_fix_kernel(wall_ref, zb_ref, za_ref, zl_ref, zr_ref, v_ref, sn_in, tn_in,
                    sn_out, tn_out, top_sn, bot_sn, top_tn, bot_tn, sems):
    ny, cz, w = v_ref.shape
    nf = top_sn.shape[0]
    ns = ny - nf
    loads = [
        pltpu.make_async_copy(sn_in.at[pl.ds(ns, nf), pl.ds(0, 8), :], top_sn, sems.at[0]),
        pltpu.make_async_copy(sn_in.at[pl.ds(ns, nf), pl.ds(cz - 8, 8), :], bot_sn, sems.at[1]),
        pltpu.make_async_copy(tn_in.at[pl.ds(ns, nf), pl.ds(0, 8), :], top_tn, sems.at[2]),
        pltpu.make_async_copy(tn_in.at[pl.ds(ns, nf), pl.ds(cz - 8, 8), :], bot_tn, sems.at[3]),
    ]
    for c in loads:
        c.start()
    sub = lax.broadcasted_iota(jnp.int32, (8, w), 0)
    wall_top = jnp.zeros((8, w), jnp.int32)
    wall_bot = jnp.zeros((8, w), jnp.int32)
    for z in range(8):
        wall_top = jnp.where(sub == z, wall_ref[z], wall_top)
        wall_bot = jnp.where(sub == z, wall_ref[cz - 8 + z], wall_bot)
    slope_scale = -span_courant / 60.0

    def side(top, sn_buf, tn_buf):
        def pair(p, carry):
            if top:
                miss = zb_ref[p] - zl_ref[p]
            else:
                miss = za_ref[p] - zr_ref[p]
            for h in range(2):
                f = 2 * p + h
                y = ns + f
                if top:
                    d = pltpu.roll(miss, 4, 0) if h == 0 else miss
                    d = jnp.where(sub >= 4, d, 0.0)
                else:
                    d = miss if h == 0 else pltpu.roll(miss, 4, 0)
                    d = jnp.where(sub < 4, d, 0.0)
                s_acc = jnp.zeros((8, w), jnp.float32)
                m_acc = jnp.zeros((8, w), jnp.float32)
                for j, cs, cm in ((1, -45.0, -56.0), (2, 9.0, 28.0), (3, -1.0, -8.0), (4, 0.0, 1.0)):
                    if top:
                        term = jnp.where(sub < j, pltpu.roll(d, j, 0), 0.0)
                    else:
                        term = jnp.where(sub >= 8 - j, pltpu.roll(d, 8 - j, 0), 0.0)
                        cs = -cs
                    if cs != 0.0:
                        s_acc = s_acc + cs * term
                    m_acc = m_acc + cm * term
                rows = slice(0, 8) if top else slice(cz - 8, cz)
                speed = v_ref[y, rows, :].astype(jnp.float32)
                wall = wall_top if top else wall_bot
                fix = jnp.where(y >= wall, slope_scale * speed * s_acc - damping * m_acc, 0.0)
                sn_buf[f] = sn_buf[f] + fix
                tn_buf[f] = tn_buf[f] + section_weight * fix
            return carry

        lax.fori_loop(0, nf // 2, pair, 0, unroll=10)

    targets = [
        (top_sn, sn_out.at[pl.ds(ns, nf), pl.ds(0, 8), :], sems.at[4]),
        (top_tn, tn_out.at[pl.ds(ns, nf), pl.ds(0, 8), :], sems.at[5]),
        (bot_sn, sn_out.at[pl.ds(ns, nf), pl.ds(cz - 8, 8), :], sems.at[6]),
        (bot_tn, tn_out.at[pl.ds(ns, nf), pl.ds(cz - 8, 8), :], sems.at[7]),
    ]
    stores = [pltpu.make_async_copy(*t) for t in targets]
    loads[0].wait()
    loads[2].wait()
    side(True, top_sn, top_tn)
    stores[0].start()
    stores[1].start()
    loads[1].wait()
    loads[3].wait()
    side(False, bot_sn, bot_tn)
    stores[2].start()
    stores[3].start()
    for c in stores:
        c.wait()


def local(theta, section_store, stream_speed, span_speed, conductivity, wall_layers,
          contact, spanwise_number, block_inverse):
    f32 = jnp.float32
    ny, cz, w = theta.shape
    ns = block_inverse.shape[0]
    nf = ny - ns
    nsb = ns // LB
    nfb = nf // LB
    ngz = lax.axis_size("gz")
    ngx = lax.axis_size("gx")


    solid_c = conductivity[0]
    fluid_c = conductivity[1]

    def harmonic(a, b):
        return 2.0 * a * b / (a + b)

    zero = jnp.zeros((1,), f32)
    faces = jnp.stack([
        jnp.concatenate([zero, harmonic(solid_c[:-1], solid_c[1:]), zero]),
        jnp.concatenate([zero, harmonic(solid_c[:-1], fluid_c[1:]), zero]),
        jnp.concatenate([zero, harmonic(fluid_c[:-1], fluid_c[1:]), zero]),
    ])

    smem = pl.BlockSpec(memory_space=pltpu.SMEM)
    blk = lambda off: pl.BlockSpec((LB, cz, w), lambda i: (i + off, 0, 0))
    prev_spec = lambda off: pl.BlockSpec((1, cz, w), lambda i: (jnp.maximum((i + off) * LB - 1, 0), 0, 0))
    next_spec = lambda off: pl.BlockSpec((1, cz, w), lambda i: (jnp.minimum((i + off) * LB + LB, ny - 1), 0, 0))
    edge_spec = pl.BlockSpec((1, 8, w), lambda i: (i, 0, 0))
    rows_spec = pl.BlockSpec((LB // 2, 8, w), lambda i: (i, 0, 0))

    xl, xr, ul, ur, zl, zr = pl.pallas_call(
        pack_kernel,
        grid=(1,),
        in_specs=[pl.BlockSpec((ny, cz, w), lambda i: (0, 0, 0))] * 2,
        out_specs=[pl.BlockSpec((nfb, 8, w), lambda i: (0, 0, 0))] * 4
        + [pl.BlockSpec((nf // 2, 8, w), lambda i: (0, 0, 0))] * 2,
        out_shape=[jax.ShapeDtypeStruct((nfb, 8, w), f32)] * 4
        + [jax.ShapeDtypeStruct((nf // 2, 8, w), f32)] * 2,
    )(theta, stream_speed)

    xb = lax.ppermute(xr, "gx", [(i, i + 1) for i in range(ngx - 1)])
    xa = lax.ppermute(xl, "gx", [(i + 1, i) for i in range(ngx - 1)])
    zb = lax.ppermute(zl, "gz", [(i, (i + 1) % ngz) for i in range(ngz)])
    za = lax.ppermute(zr, "gz", [((i + 1) % ngz, i) for i in range(ngz)])


    sb = 2 * LB if ns % (2 * LB) == 0 else LB
    sblk = pl.BlockSpec((sb, cz, w), lambda i: (i, 0, 0))
    sn_part, interior, spread = pl.pallas_call(
        lambda *refs: layer_kernel(False, 0, sb, *refs),
        grid=(ns // sb,),
        in_specs=[smem, smem, smem, sblk,
                  pl.BlockSpec((1, cz, w), lambda i: (jnp.maximum(i * sb - 1, 0), 0, 0)),
                  pl.BlockSpec((1, cz, w), lambda i: (jnp.minimum(i * sb + sb, ny - 1), 0, 0)),
                  sblk,
                  pl.BlockSpec((sb, cz - 1, cz - 1), lambda i: (i, 0, 0)),
                  pl.BlockSpec(memory_space=pl.ANY)],
        out_specs=[sblk, sblk, pl.BlockSpec((ngz, 3, sb, w), lambda i: (0, 0, i, 0))],
        out_shape=[
            jax.ShapeDtypeStruct((ny, cz, w), f32),
            jax.ShapeDtypeStruct((ns, cz, w), f32),
            jax.ShapeDtypeStruct((ngz, 3, ns, w), f32),
        ],
        scratch_shapes=[pltpu.VMEM((cz, w), jnp.int32), pltpu.VMEM((cz, w), f32)],
    )(faces, wall_layers, contact, theta, theta, theta, section_store, block_inverse, zr)

    number = spanwise_number
    blocks = lax.all_to_all(spread, "gz", 0, 0, tiled=True)
    left = jnp.roll(blocks[:, 2], 1, axis=0)
    targets = blocks[:, 0] + number[None, :, None] * left + number[None, :, None] * blocks[:, 1]

    square = number * number
    diagonal = 1.0 + 2.0 * number - square * (block_inverse[:, 0, 0] + block_inverse[:, -1, -1])
    beside = square * block_inverse[:, 0, -1]
    q = jnp.arange(ngz, dtype=jnp.int32)
    angle = (2.0 * math.pi / ngz) * q.astype(f32)
    denominator = diagonal[:, None] - 2.0 * beside[:, None] * jnp.cos(angle)[None, :]
    k = lax.axis_index("gz")

    def weights(shift):
        m = (q - shift) % ngz
        phase = (2.0 * math.pi / ngz) * ((q[:, None] * m[None, :]) % ngz).astype(f32)
        return jnp.sum(jnp.cos(phase)[None, :, :] / denominator[:, :, None], axis=1) / ngz

    head_values = jnp.sum(weights(k).T[:, :, None] * targets, axis=0)
    following = jnp.sum(weights(k + 1).T[:, :, None] * targets, axis=0)

    fluid_sn, fluid_tn = pl.pallas_call(
        lambda *refs: layer_kernel(True, nsb, LB, *refs),
        grid=(nfb,),
        in_specs=[smem, smem, smem, blk(nsb), prev_spec(nsb), next_spec(nsb), blk(nsb),
                  blk(nsb), blk(nsb), edge_spec, edge_spec,
                  edge_spec, edge_spec, edge_spec, edge_spec,
                  pl.BlockSpec(memory_space=pl.ANY)],
        out_specs=[blk(nsb), blk(nsb)],
        out_shape=[
            jax.ShapeDtypeStruct((ny, cz, w), f32),
            jax.ShapeDtypeStruct((ny, cz, w), f32),
        ],
        scratch_shapes=[pltpu.VMEM((cz, w), jnp.int32), pltpu.VMEM((cz, w), f32),
                        pltpu.VMEM((cz + 16, w), f32)],
        input_output_aliases={15: 0},
    )(faces, wall_layers, contact, theta, theta, theta, section_store,
      stream_speed, span_speed, xb, xa, xl, xr, ul, ur, sn_part)

    anyspec = pl.BlockSpec(memory_space=pl.ANY)
    whole = lambda shape: pl.BlockSpec(shape, lambda i: (0,) * len(shape))
    fluid_sn, fluid_tn = pl.pallas_call(
        span_fix_kernel,
        grid=(1,),
        in_specs=[smem] + [whole((nf // 2, 8, w))] * 4 + [whole((ny, cz, w)), anyspec, anyspec],
        out_specs=[anyspec, anyspec],
        out_shape=[jax.ShapeDtypeStruct((ny, cz, w), f32)] * 2,
        scratch_shapes=[pltpu.VMEM((nf, 8, w), f32)] * 4 + [pltpu.SemaphoreType.DMA((8,))],
        input_output_aliases={6: 0, 7: 1},
    )(wall_layers, zb, za, zl, zr, span_speed, fluid_sn, fluid_tn)

    row = jnp.arange(cz, dtype=jnp.int32)
    col0 = jnp.zeros((ns, cz), f32).at[:, 1:].set(block_inverse[:, :, 0])
    col_last = jnp.zeros((ns, cz), f32).at[:, 1:].set(block_inverse[:, :, -1])
    scale = number[:, None, None]
    solved = interior + scale * (col0[:, :, None] * head_values[:, None, :]
                                 + col_last[:, :, None] * following[:, None, :])
    solved = jnp.where((row == 0)[None, :, None], head_values[:, None, :], solved)
    theta_new = lax.dynamic_update_slice_in_dim(fluid_tn, solved, 0, 0)
    return (theta_new, fluid_sn)


def solution(mesh):
    return jax.shard_map(
        local,
        mesh=mesh,
        in_specs=(
            P(None, "gz", "gx"),
            P(None, "gz", "gx"),
            P(None, "gz", "gx"),
            P(None, "gz", "gx"),
            P(),
            P("gz"),
            P("gx"),
            P(),
            P(),
        ),
        out_specs=(P(None, "gz", "gx"), P(None, "gz", "gx")),
        check_vma=False,
    )
```

```python
import math

import jax
import jax.numpy as jnp
from jax import lax
from jax.experimental import pallas as pl
from jax.experimental.pallas import tpu as pltpu
from jax.sharding import PartitionSpec as P

keep_factor = -5.0 / 9.0
section_weight = 15.0 / 16.0
stream_courant = 0.4
span_courant = 0.4
damping = 1.0 / 256.0

LB = 8


def pack_kernel(th_ref, u_ref, xl_ref, xr_ref, ul_ref, ur_ref, zl_ref, zr_ref):
    ny, cz, w = th_ref.shape
    nblocks = xl_ref.shape[0]
    skip = ny - nblocks * LB
    lane8 = lax.broadcasted_iota(jnp.int32, (8, w), 1)
    sub8 = lax.broadcasted_iota(jnp.int32, (8, w), 0)

    def block(b, carry):
        first = skip + b * LB
        acc_l = jnp.zeros((8, w), jnp.float32)
        acc_r = jnp.zeros((8, w), jnp.float32)
        uacc_l = jnp.zeros((8, w), jnp.float32)
        uacc_r = jnp.zeros((8, w), jnp.float32)
        for s in range(LB):
            speed = u_ref[first + s].astype(jnp.float32)
            for v in range(cz // 8):
                t = th_ref[first + s, 8 * v:8 * v + 8, :]
                pos = 4 * LB * v + 4 * s
                moved = pltpu.roll(t, pos % w, 1)
                umoved = pltpu.roll(speed[8 * v:8 * v + 8], pos % w, 1)
                pick_l = jnp.logical_and(lane8 >= pos, lane8 < pos + 4)
                pick_r = jnp.logical_and(lane8 >= (pos - 4) % w, lane8 < (pos - 4) % w + 4)
                acc_l = jnp.where(pick_l, moved, acc_l)
                acc_r = jnp.where(pick_r, moved, acc_r)
                uacc_l = jnp.where(pick_l, umoved, uacc_l)
                uacc_r = jnp.where(pick_r, umoved, uacc_r)
        xl_ref[b] = acc_l
        xr_ref[b] = acc_r
        ul_ref[b] = uacc_l
        ur_ref[b] = uacc_r
        for p in range(LB // 2):
            a_hi = th_ref[first + 2 * p, cz - 8:cz, :]
            b_hi = th_ref[first + 2 * p + 1, cz - 8:cz, :]
            zl_ref[b * (LB // 2) + p] = jnp.where(sub8 < 4, pltpu.roll(a_hi, 4, 0), b_hi)
            a_lo = th_ref[first + 2 * p, 0:8, :]
            b_lo = th_ref[first + 2 * p + 1, 0:8, :]
            zr_ref[b * (LB // 2) + p] = jnp.where(sub8 < 4, a_lo, pltpu.roll(b_lo, 4, 0))
        return carry

    lax.fori_loop(0, nblocks, block, 0)


def layer_kernel(fluid, block_offset, lb, *refs):
    if fluid:
        (face_ref, wall_ref, contact_ref, th_ref, prev_ref, next_ref, st_ref,
         u_ref, v_ref, xb_ref, xa_ref, xl_ref, xr_ref, ul_ref, ur_ref,
         _alias_ref, sn_ref, tn_ref, tsn_ref, bsn_ref, ttn_ref, btn_ref,
         wallv_ref, contv_ref, ext_ref) = refs
    else:
        (face_ref, wall_ref, contact_ref, th_ref, prev_ref, next_ref, st_ref,
         bs_ref, _order_ref, sn_ref, int_ref, mine_ref, wallv_ref, contv_ref) = refs
    _, cz, w = th_ref.shape
    base = (pl.program_id(0) + block_offset) * lb

    @pl.when(pl.program_id(0) == 0)
    def _():
        sub = lax.broadcasted_iota(jnp.int32, (cz, w), 0)
        acc = jnp.zeros((cz, w), jnp.int32)
        for z in range(cz):
            acc = jnp.where(sub == z, wall_ref[z], acc)
        wallv_ref[...] = acc
        lane = lax.broadcasted_iota(jnp.int32, (cz, w), 1)
        cacc = jnp.zeros((cz, w), jnp.float32)
        for x in range(w):
            cacc = jnp.where(lane == x, contact_ref[x].astype(jnp.float32), cacc)
        contv_ref[...] = cacc

    wall = wallv_ref[...]
    contact = contv_ref[...]

    def face(y):
        both_solid = face_ref[0, y + 1]
        both_fluid = face_ref[2, y + 1]
        at_wall = face_ref[1, y + 1] * contact
        return jnp.where(y + 1 < wall, both_solid, jnp.where(y >= wall, both_fluid, at_wall))

    if fluid:
        lane = lax.broadcasted_iota(jnp.int32, (8, w), 1)
        nv = cz // 8
        slope_scale = -stream_courant / 60.0
        quarter = lane % 4
        miss_l = xb_ref[0] - xr_ref[0]
        miss_r = xa_ref[0] - xl_ref[0]

        def edge(miss, weights, left):
            acc = jnp.zeros((8, w), jnp.float32)
            for j, c in weights:
                if left:
                    term = jnp.where(quarter < j, pltpu.roll(miss, j, 1), 0.0)
                else:
                    term = jnp.where(quarter >= 4 - j, pltpu.roll(miss, w - j, 1), 0.0)
                acc = acc + c * term
            return acc

        fix_l = (slope_scale * ul_ref[0] * edge(miss_l, ((1, -45.0), (2, 9.0), (3, -1.0)), True)
                 - damping * edge(miss_l, ((1, -56.0), (2, 28.0), (3, -8.0), (4, 1.0)), True))
        fix_r = (slope_scale * ur_ref[0] * edge(miss_r, ((1, 45.0), (2, -9.0), (3, 1.0)), False)
                 - damping * edge(miss_r, ((1, -56.0), (2, 28.0), (3, -8.0), (4, 1.0)), False))

    heads = []
    face_dn = face(base - 1)
    for s in range(lb):
        y = base + s
        t = th_ref[s]
        tp = th_ref[s - 1] if s > 0 else prev_ref[0]
        tn = th_ref[s + 1] if s < lb - 1 else next_ref[0]
        face_up = face(y)
        normal = face_up * (tn - t) - face_dn * (t - tp)
        face_dn = face_up
        if fluid:
            u = u_ref[s].astype(jnp.float32)
            v = v_ref[s].astype(jnp.float32)
            xm = [None] + [pltpu.roll(t, j, 1) for j in range(1, 5)]
            xp = [None] + [pltpu.roll(t, w - j, 1) for j in range(1, 5)]
            fixes = []
            for g in range(nv):
                pos = 4 * LB * g + 4 * s
                at_l = jnp.logical_and(lane >= pos, lane < pos + 4)
                at_r = jnp.logical_and(lane >= (pos - 4) % w, lane < (pos - 4) % w + 4)
                picked = jnp.where(at_l, fix_l, jnp.where(at_r, fix_r, 0.0))
                fixes.append(pltpu.roll(picked, (w - pos) % w, 1))
            fix = jnp.concatenate(fixes, axis=0)
            ext_ref[0:8, :] = t[cz - 8:]
            ext_ref[8:8 + cz, :] = t
            ext_ref[8 + cz:16 + cz, :] = t[:8]
            zm = [None] + [ext_ref[8 - j:8 - j + cz, :] for j in range(1, 5)]
            zp = [None] + [ext_ref[8 + j:8 + j + cz, :] for j in range(1, 5)]

            def slope(m, p):
                return 45.0 * (p[1] - m[1]) - 9.0 * (p[2] - m[2]) + (p[3] - m[3])

            def smooth(m, p):
                return ((p[4] + m[4]) - 8.0 * (p[3] + m[3]) + 28.0 * (p[2] + m[2])
                        - 56.0 * (p[1] + m[1]))

            smoothing = smooth(zm, zp) + smooth(xm, xp) + 140.0 * t
            horiz = (slope_scale * (u * slope(xm, xp) + v * slope(zm, zp))
                     - damping * smoothing) + fix
            across = jnp.where(y >= wall, horiz, 0.0)
            rate = normal + across
        else:
            rate = normal
        sn = keep_factor * st_ref[s] + rate
        adv = t + section_weight * sn
        sn_ref[s] = sn
        if fluid:
            tn_ref[s] = adv
            tsn_ref[s] = sn[0:8]
            bsn_ref[s] = sn[cz - 8:]
            ttn_ref[s] = adv[0:8]
            btn_ref[s] = adv[cz - 8:]
        else:
            inner = jnp.dot(bs_ref[s], adv[1:], precision=lax.Precision.HIGHEST,
                            preferred_element_type=jnp.float32)
            inner = jnp.concatenate([jnp.zeros((1, w), jnp.float32), inner], axis=0)
            int_ref[s] = inner
            heads.append((adv[0:1, :], inner[1:2, :], inner[cz - 1:cz, :]))
    if not fluid:
        for part in range(3):
            rows = jnp.concatenate([h[part] for h in heads], axis=0)
            for n in range(mine_ref.shape[0]):
                mine_ref[n, part] = rows


def span_fix_kernel(wall_ref, zb_ref, za_ref, zl_ref, zr_ref, v_ref, ta_ref, tb_ref, tc_ref,
                    td_ref, sn_in, tn_in, sn_out, tn_out, top_sn, bot_sn, top_tn, bot_tn, sems):
    ny, cz, w = v_ref.shape
    nf = top_sn.shape[0]
    ns = ny - nf
    del sn_in, tn_in
    top_sn[...] = ta_ref[...]
    bot_sn[...] = tb_ref[...]
    top_tn[...] = tc_ref[...]
    bot_tn[...] = td_ref[...]
    sub = lax.broadcasted_iota(jnp.int32, (8, w), 0)
    wall_top = jnp.zeros((8, w), jnp.int32)
    wall_bot = jnp.zeros((8, w), jnp.int32)
    for z in range(8):
        wall_top = jnp.where(sub == z, wall_ref[z], wall_top)
        wall_bot = jnp.where(sub == z, wall_ref[cz - 8 + z], wall_bot)
    slope_scale = -span_courant / 60.0

    def side(top, sn_buf, tn_buf):
        def pair(p, carry):
            if top:
                miss = zb_ref[p] - zl_ref[p]
            else:
                miss = za_ref[p] - zr_ref[p]
            for h in range(2):
                f = 2 * p + h
                y = ns + f
                if top:
                    d = pltpu.roll(miss, 4, 0) if h == 0 else miss
                    d = jnp.where(sub >= 4, d, 0.0)
                else:
                    d = miss if h == 0 else pltpu.roll(miss, 4, 0)
                    d = jnp.where(sub < 4, d, 0.0)
                s_acc = jnp.zeros((8, w), jnp.float32)
                m_acc = jnp.zeros((8, w), jnp.float32)
                for j, cs, cm in ((1, -45.0, -56.0), (2, 9.0, 28.0), (3, -1.0, -8.0), (4, 0.0, 1.0)):
                    if top:
                        term = jnp.where(sub < j, pltpu.roll(d, j, 0), 0.0)
                    else:
                        term = jnp.where(sub >= 8 - j, pltpu.roll(d, 8 - j, 0), 0.0)
                        cs = -cs
                    if cs != 0.0:
                        s_acc = s_acc + cs * term
                    m_acc = m_acc + cm * term
                rows = slice(0, 8) if top else slice(cz - 8, cz)
                speed = v_ref[y, rows, :].astype(jnp.float32)
                wall = wall_top if top else wall_bot
                fix = jnp.where(y >= wall, slope_scale * speed * s_acc - damping * m_acc, 0.0)
                sn_buf[f] = sn_buf[f] + fix
                tn_buf[f] = tn_buf[f] + section_weight * fix
            return carry

        lax.fori_loop(0, nf // 2, pair, 0, unroll=10)

    targets = [
        (top_sn, sn_out.at[pl.ds(ns, nf), pl.ds(0, 8), :], sems.at[4]),
        (top_tn, tn_out.at[pl.ds(ns, nf), pl.ds(0, 8), :], sems.at[5]),
        (bot_sn, sn_out.at[pl.ds(ns, nf), pl.ds(cz - 8, 8), :], sems.at[6]),
        (bot_tn, tn_out.at[pl.ds(ns, nf), pl.ds(cz - 8, 8), :], sems.at[7]),
    ]
    stores = [pltpu.make_async_copy(*t) for t in targets]
    side(True, top_sn, top_tn)
    stores[0].start()
    stores[1].start()
    side(False, bot_sn, bot_tn)
    stores[2].start()
    stores[3].start()
    for c in stores:
        c.wait()


def local(theta, section_store, stream_speed, span_speed, conductivity, wall_layers,
          contact, spanwise_number, block_inverse):
    f32 = jnp.float32
    ny, cz, w = theta.shape
    ns = block_inverse.shape[0]
    nf = ny - ns
    nsb = ns // LB
    nfb = nf // LB
    ngz = lax.axis_size("gz")
    ngx = lax.axis_size("gx")


    solid_c = conductivity[0]
    fluid_c = conductivity[1]

    def harmonic(a, b):
        return 2.0 * a * b / (a + b)

    zero = jnp.zeros((1,), f32)
    faces = jnp.stack([
        jnp.concatenate([zero, harmonic(solid_c[:-1], solid_c[1:]), zero]),
        jnp.concatenate([zero, harmonic(solid_c[:-1], fluid_c[1:]), zero]),
        jnp.concatenate([zero, harmonic(fluid_c[:-1], fluid_c[1:]), zero]),
    ])

    smem = pl.BlockSpec(memory_space=pltpu.SMEM)
    blk = lambda off: pl.BlockSpec((LB, cz, w), lambda i: (i + off, 0, 0))
    prev_spec = lambda off: pl.BlockSpec((1, cz, w), lambda i: (jnp.maximum((i + off) * LB - 1, 0), 0, 0))
    next_spec = lambda off: pl.BlockSpec((1, cz, w), lambda i: (jnp.minimum((i + off) * LB + LB, ny - 1), 0, 0))
    edge_spec = pl.BlockSpec((1, 8, w), lambda i: (i, 0, 0))
    rows_spec = pl.BlockSpec((LB // 2, 8, w), lambda i: (i, 0, 0))

    xl, xr, ul, ur, zl, zr = pl.pallas_call(
        pack_kernel,
        grid=(1,),
        in_specs=[pl.BlockSpec((ny, cz, w), lambda i: (0, 0, 0))] * 2,
        out_specs=[pl.BlockSpec((nfb, 8, w), lambda i: (0, 0, 0))] * 4
        + [pl.BlockSpec((nf // 2, 8, w), lambda i: (0, 0, 0))] * 2,
        out_shape=[jax.ShapeDtypeStruct((nfb, 8, w), f32)] * 4
        + [jax.ShapeDtypeStruct((nf // 2, 8, w), f32)] * 2,
    )(theta, stream_speed)

    xb = lax.ppermute(xr, "gx", [(i, i + 1) for i in range(ngx - 1)])
    xa = lax.ppermute(xl, "gx", [(i + 1, i) for i in range(ngx - 1)])
    zb = lax.ppermute(zl, "gz", [(i, (i + 1) % ngz) for i in range(ngz)])
    za = lax.ppermute(zr, "gz", [((i + 1) % ngz, i) for i in range(ngz)])


    sb = 2 * LB if ns % (2 * LB) == 0 else LB
    sblk = pl.BlockSpec((sb, cz, w), lambda i: (i, 0, 0))
    sn_part, interior, spread = pl.pallas_call(
        lambda *refs: layer_kernel(False, 0, sb, *refs),
        grid=(ns // sb,),
        in_specs=[smem, smem, smem, sblk,
                  pl.BlockSpec((1, cz, w), lambda i: (jnp.maximum(i * sb - 1, 0), 0, 0)),
                  pl.BlockSpec((1, cz, w), lambda i: (jnp.minimum(i * sb + sb, ny - 1), 0, 0)),
                  sblk,
                  pl.BlockSpec((sb, cz - 1, cz - 1), lambda i: (i, 0, 0)),
                  pl.BlockSpec(memory_space=pl.ANY)],
        out_specs=[sblk, sblk, pl.BlockSpec((ngz, 3, sb, w), lambda i: (0, 0, i, 0))],
        out_shape=[
            jax.ShapeDtypeStruct((ny, cz, w), f32),
            jax.ShapeDtypeStruct((ns, cz, w), f32),
            jax.ShapeDtypeStruct((ngz, 3, ns, w), f32),
        ],
        scratch_shapes=[pltpu.VMEM((cz, w), jnp.int32), pltpu.VMEM((cz, w), f32)],
    )(faces, wall_layers, contact, theta, theta, theta, section_store, block_inverse, zr)

    number = spanwise_number
    blocks = lax.all_to_all(spread, "gz", 0, 0, tiled=True)
    left = jnp.roll(blocks[:, 2], 1, axis=0)
    targets = blocks[:, 0] + number[None, :, None] * left + number[None, :, None] * blocks[:, 1]

    square = number * number
    diagonal = 1.0 + 2.0 * number - square * (block_inverse[:, 0, 0] + block_inverse[:, -1, -1])
    beside = square * block_inverse[:, 0, -1]
    q = jnp.arange(ngz, dtype=jnp.int32)
    angle = (2.0 * math.pi / ngz) * q.astype(f32)
    denominator = diagonal[:, None] - 2.0 * beside[:, None] * jnp.cos(angle)[None, :]
    k = lax.axis_index("gz")

    def weights(shift):
        m = (q - shift) % ngz
        phase = (2.0 * math.pi / ngz) * ((q[:, None] * m[None, :]) % ngz).astype(f32)
        return jnp.sum(jnp.cos(phase)[None, :, :] / denominator[:, :, None], axis=1) / ngz

    head_values = jnp.sum(weights(k).T[:, :, None] * targets, axis=0)
    following = jnp.sum(weights(k + 1).T[:, :, None] * targets, axis=0)

    fluid_sn, fluid_tn, tiles_a, tiles_b, tiles_c, tiles_d = pl.pallas_call(
        lambda *refs: layer_kernel(True, nsb, LB, *refs),
        grid=(nfb,),
        in_specs=[smem, smem, smem, blk(nsb), prev_spec(nsb), next_spec(nsb), blk(nsb),
                  blk(nsb), blk(nsb), edge_spec, edge_spec,
                  edge_spec, edge_spec, edge_spec, edge_spec,
                  pl.BlockSpec(memory_space=pl.ANY)],
        out_specs=[blk(nsb), blk(nsb)] + [pl.BlockSpec((LB, 8, w), lambda i: (i, 0, 0))] * 4,
        out_shape=[
            jax.ShapeDtypeStruct((ny, cz, w), f32),
            jax.ShapeDtypeStruct((ny, cz, w), f32),
        ] + [jax.ShapeDtypeStruct((nf, 8, w), f32)] * 4,
        scratch_shapes=[pltpu.VMEM((cz, w), jnp.int32), pltpu.VMEM((cz, w), f32),
                        pltpu.VMEM((cz + 16, w), f32)],
        input_output_aliases={15: 0},
    )(faces, wall_layers, contact, theta, theta, theta, section_store,
      stream_speed, span_speed, xb, xa, xl, xr, ul, ur, sn_part)

    anyspec = pl.BlockSpec(memory_space=pl.ANY)
    whole = lambda shape: pl.BlockSpec(shape, lambda i: (0,) * len(shape))
    fluid_sn, fluid_tn = pl.pallas_call(
        span_fix_kernel,
        grid=(1,),
        in_specs=[smem] + [whole((nf // 2, 8, w))] * 4 + [whole((ny, cz, w))]
        + [whole((nf, 8, w))] * 4 + [anyspec, anyspec],
        out_specs=[anyspec, anyspec],
        out_shape=[jax.ShapeDtypeStruct((ny, cz, w), f32)] * 2,
        scratch_shapes=[pltpu.VMEM((nf, 8, w), f32)] * 4 + [pltpu.SemaphoreType.DMA((8,))],
        input_output_aliases={10: 0, 11: 1},
    )(wall_layers, zb, za, zl, zr, span_speed, tiles_a, tiles_b, tiles_c, tiles_d,
      fluid_sn, fluid_tn)

    row = jnp.arange(cz, dtype=jnp.int32)
    col0 = jnp.zeros((ns, cz), f32).at[:, 1:].set(block_inverse[:, :, 0])
    col_last = jnp.zeros((ns, cz), f32).at[:, 1:].set(block_inverse[:, :, -1])
    scale = number[:, None, None]
    solved = interior + scale * (col0[:, :, None] * head_values[:, None, :]
                                 + col_last[:, :, None] * following[:, None, :])
    solved = jnp.where((row == 0)[None, :, None], head_values[:, None, :], solved)
    theta_new = lax.dynamic_update_slice_in_dim(fluid_tn, solved, 0, 0)
    return (theta_new, fluid_sn)


def solution(mesh):
    return jax.shard_map(
        local,
        mesh=mesh,
        in_specs=(
            P(None, "gz", "gx"),
            P(None, "gz", "gx"),
            P(None, "gz", "gx"),
            P(None, "gz", "gx"),
            P(),
            P("gz"),
            P("gx"),
            P(),
            P(),
        ),
        out_specs=(P(None, "gz", "gx"), P(None, "gz", "gx")),
        check_vma=False,
    )
```

```python
import math

import jax
import jax.numpy as jnp
from jax import lax
from jax.experimental import pallas as pl
from jax.experimental.pallas import tpu as pltpu
from jax.sharding import PartitionSpec as P

keep_factor = -5.0 / 9.0
section_weight = 15.0 / 16.0
stream_courant = 0.4
span_courant = 0.4
damping = 1.0 / 256.0

LB = 8


def pack_kernel(th_ref, u_ref, xl_ref, xr_ref, ul_ref, ur_ref, zl_ref, zr_ref):
    ny, cz, w = th_ref.shape
    nblocks = xl_ref.shape[0]
    skip = ny - nblocks * LB
    lane8 = lax.broadcasted_iota(jnp.int32, (8, w), 1)
    sub8 = lax.broadcasted_iota(jnp.int32, (8, w), 0)

    def block(b, carry):
        first = skip + b * LB
        acc_l = jnp.zeros((8, w), jnp.float32)
        acc_r = jnp.zeros((8, w), jnp.float32)
        uacc_l = jnp.zeros((8, w), jnp.float32)
        uacc_r = jnp.zeros((8, w), jnp.float32)
        for s in range(LB):
            speed = u_ref[first + s].astype(jnp.float32)
            for v in range(cz // 8):
                t = th_ref[first + s, 8 * v:8 * v + 8, :]
                pos = 4 * LB * v + 4 * s
                moved = pltpu.roll(t, pos % w, 1)
                umoved = pltpu.roll(speed[8 * v:8 * v + 8], pos % w, 1)
                pick_l = jnp.logical_and(lane8 >= pos, lane8 < pos + 4)
                pick_r = jnp.logical_and(lane8 >= (pos - 4) % w, lane8 < (pos - 4) % w + 4)
                acc_l = jnp.where(pick_l, moved, acc_l)
                acc_r = jnp.where(pick_r, moved, acc_r)
                uacc_l = jnp.where(pick_l, umoved, uacc_l)
                uacc_r = jnp.where(pick_r, umoved, uacc_r)
        xl_ref[b] = acc_l
        xr_ref[b] = acc_r
        ul_ref[b] = uacc_l
        ur_ref[b] = uacc_r
        for p in range(LB // 2):
            a_hi = th_ref[first + 2 * p, cz - 8:cz, :]
            b_hi = th_ref[first + 2 * p + 1, cz - 8:cz, :]
            zl_ref[b * (LB // 2) + p] = jnp.where(sub8 < 4, pltpu.roll(a_hi, 4, 0), b_hi)
            a_lo = th_ref[first + 2 * p, 0:8, :]
            b_lo = th_ref[first + 2 * p + 1, 0:8, :]
            zr_ref[b * (LB // 2) + p] = jnp.where(sub8 < 4, a_lo, pltpu.roll(b_lo, 4, 0))
        return carry

    lax.fori_loop(0, nblocks, block, 0)


def layer_kernel(fluid, block_offset, lb, *refs):
    if fluid:
        (face_ref, wall_ref, contact_ref, th_ref, prev_ref, next_ref, st_ref,
         u_ref, v_ref, xb_ref, xa_ref, xl_ref, xr_ref, ul_ref, ur_ref,
         _alias_ref, sn_ref, tn_ref, tsn_ref, bsn_ref, ttn_ref, btn_ref, tv_ref, bv_ref,
         wallv_ref, contv_ref, ext_ref) = refs
    else:
        (face_ref, wall_ref, contact_ref, th_ref, prev_ref, next_ref, st_ref,
         bs_ref, _order_ref, sn_ref, int_ref, mine_ref, wallv_ref, contv_ref) = refs
    _, cz, w = th_ref.shape
    base = (pl.program_id(0) + block_offset) * lb

    @pl.when(pl.program_id(0) == 0)
    def _():
        sub = lax.broadcasted_iota(jnp.int32, (cz, w), 0)
        acc = jnp.zeros((cz, w), jnp.int32)
        for z in range(cz):
            acc = jnp.where(sub == z, wall_ref[z], acc)
        wallv_ref[...] = acc
        lane = lax.broadcasted_iota(jnp.int32, (cz, w), 1)
        cacc = jnp.zeros((cz, w), jnp.float32)
        for x in range(w):
            cacc = jnp.where(lane == x, contact_ref[x].astype(jnp.float32), cacc)
        contv_ref[...] = cacc

    wall = wallv_ref[...]
    contact = contv_ref[...]

    def face(y):
        both_solid = face_ref[0, y + 1]
        both_fluid = face_ref[2, y + 1]
        at_wall = face_ref[1, y + 1] * contact
        return jnp.where(y + 1 < wall, both_solid, jnp.where(y >= wall, both_fluid, at_wall))

    if fluid:
        lane = lax.broadcasted_iota(jnp.int32, (8, w), 1)
        nv = cz // 8
        slope_scale = -stream_courant / 60.0
        quarter = lane % 4
        miss_l = xb_ref[0] - xr_ref[0]
        miss_r = xa_ref[0] - xl_ref[0]

        def edge(miss, weights, left):
            acc = jnp.zeros((8, w), jnp.float32)
            for j, c in weights:
                if left:
                    term = jnp.where(quarter < j, pltpu.roll(miss, j, 1), 0.0)
                else:
                    term = jnp.where(quarter >= 4 - j, pltpu.roll(miss, w - j, 1), 0.0)
                acc = acc + c * term
            return acc

        fix_l = (slope_scale * ul_ref[0] * edge(miss_l, ((1, -45.0), (2, 9.0), (3, -1.0)), True)
                 - damping * edge(miss_l, ((1, -56.0), (2, 28.0), (3, -8.0), (4, 1.0)), True))
        fix_r = (slope_scale * ur_ref[0] * edge(miss_r, ((1, 45.0), (2, -9.0), (3, 1.0)), False)
                 - damping * edge(miss_r, ((1, -56.0), (2, 28.0), (3, -8.0), (4, 1.0)), False))

    heads = []
    face_dn = face(base - 1)
    for s in range(lb):
        y = base + s
        t = th_ref[s]
        tp = th_ref[s - 1] if s > 0 else prev_ref[0]
        tn = th_ref[s + 1] if s < lb - 1 else next_ref[0]
        face_up = face(y)
        normal = face_up * (tn - t) - face_dn * (t - tp)
        face_dn = face_up
        if fluid:
            u = u_ref[s].astype(jnp.float32)
            v = v_ref[s].astype(jnp.float32)
            xm = [None] + [pltpu.roll(t, j, 1) for j in range(1, 5)]
            xp = [None] + [pltpu.roll(t, w - j, 1) for j in range(1, 5)]
            fixes = []
            for g in range(nv):
                pos = 4 * LB * g + 4 * s
                at_l = jnp.logical_and(lane >= pos, lane < pos + 4)
                at_r = jnp.logical_and(lane >= (pos - 4) % w, lane < (pos - 4) % w + 4)
                picked = jnp.where(at_l, fix_l, jnp.where(at_r, fix_r, 0.0))
                fixes.append(pltpu.roll(picked, (w - pos) % w, 1))
            fix = jnp.concatenate(fixes, axis=0)
            ext_ref[0:8, :] = t[cz - 8:]
            ext_ref[8:8 + cz, :] = t
            ext_ref[8 + cz:16 + cz, :] = t[:8]
            zm = [None] + [ext_ref[8 - j:8 - j + cz, :] for j in range(1, 5)]
            zp = [None] + [ext_ref[8 + j:8 + j + cz, :] for j in range(1, 5)]

            def slope(m, p):
                return 45.0 * (p[1] - m[1]) - 9.0 * (p[2] - m[2]) + (p[3] - m[3])

            def smooth(m, p):
                return ((p[4] + m[4]) - 8.0 * (p[3] + m[3]) + 28.0 * (p[2] + m[2])
                        - 56.0 * (p[1] + m[1]))

            smoothing = smooth(zm, zp) + smooth(xm, xp) + 140.0 * t
            horiz = (slope_scale * (u * slope(xm, xp) + v * slope(zm, zp))
                     - damping * smoothing) + fix
            across = jnp.where(y >= wall, horiz, 0.0)
            rate = normal + across
        else:
            rate = normal
        sn = keep_factor * st_ref[s] + rate
        adv = t + section_weight * sn
        sn_ref[s] = sn
        if fluid:
            tn_ref[s] = adv
            tsn_ref[s] = sn[0:8]
            bsn_ref[s] = sn[cz - 8:]
            ttn_ref[s] = adv[0:8]
            btn_ref[s] = adv[cz - 8:]
            tv_ref[s] = v[0:8]
            bv_ref[s] = v[cz - 8:]
        else:
            inner = jnp.dot(bs_ref[s], adv[1:], precision=lax.Precision.HIGHEST,
                            preferred_element_type=jnp.float32)
            inner = jnp.concatenate([jnp.zeros((1, w), jnp.float32), inner], axis=0)
            int_ref[s] = inner
            heads.append((adv[0:1, :], inner[1:2, :], inner[cz - 1:cz, :]))
    if not fluid:
        for part in range(3):
            rows = jnp.concatenate([h[part] for h in heads], axis=0)
            for n in range(mine_ref.shape[0]):
                mine_ref[n, part] = rows


def span_fix_kernel(wall_ref, zb_ref, za_ref, zl_ref, zr_ref, tv_ref, bv_ref, ta_ref, tb_ref, tc_ref,
                    td_ref, sn_in, tn_in, sn_out, tn_out, top_sn, bot_sn, top_tn, bot_tn, sems):
    ny, cz, w = sn_in.shape
    nf = top_sn.shape[0]
    ns = ny - nf
    del sn_in, tn_in
    top_sn[...] = ta_ref[...]
    bot_sn[...] = tb_ref[...]
    top_tn[...] = tc_ref[...]
    bot_tn[...] = td_ref[...]
    sub = lax.broadcasted_iota(jnp.int32, (8, w), 0)
    wall_top = jnp.zeros((8, w), jnp.int32)
    wall_bot = jnp.zeros((8, w), jnp.int32)
    for z in range(8):
        wall_top = jnp.where(sub == z, wall_ref[z], wall_top)
        wall_bot = jnp.where(sub == z, wall_ref[cz - 8 + z], wall_bot)
    slope_scale = -span_courant / 60.0

    def side(top, sn_buf, tn_buf):
        def pair(p, carry):
            if top:
                miss = zb_ref[p] - zl_ref[p]
            else:
                miss = za_ref[p] - zr_ref[p]
            for h in range(2):
                f = 2 * p + h
                y = ns + f
                if top:
                    d = pltpu.roll(miss, 4, 0) if h == 0 else miss
                    d = jnp.where(sub >= 4, d, 0.0)
                else:
                    d = miss if h == 0 else pltpu.roll(miss, 4, 0)
                    d = jnp.where(sub < 4, d, 0.0)
                s_acc = jnp.zeros((8, w), jnp.float32)
                m_acc = jnp.zeros((8, w), jnp.float32)
                for j, cs, cm in ((1, -45.0, -56.0), (2, 9.0, 28.0), (3, -1.0, -8.0), (4, 0.0, 1.0)):
                    if top:
                        term = jnp.where(sub < j, pltpu.roll(d, j, 0), 0.0)
                    else:
                        term = jnp.where(sub >= 8 - j, pltpu.roll(d, 8 - j, 0), 0.0)
                        cs = -cs
                    if cs != 0.0:
                        s_acc = s_acc + cs * term
                    m_acc = m_acc + cm * term
                speed = tv_ref[f] if top else bv_ref[f]
                wall = wall_top if top else wall_bot
                fix = jnp.where(y >= wall, slope_scale * speed * s_acc - damping * m_acc, 0.0)
                sn_buf[f] = sn_buf[f] + fix
                tn_buf[f] = tn_buf[f] + section_weight * fix
            return carry

        lax.fori_loop(0, nf // 2, pair, 0, unroll=10)

    targets = [
        (top_sn, sn_out.at[pl.ds(ns, nf), pl.ds(0, 8), :], sems.at[4]),
        (top_tn, tn_out.at[pl.ds(ns, nf), pl.ds(0, 8), :], sems.at[5]),
        (bot_sn, sn_out.at[pl.ds(ns, nf), pl.ds(cz - 8, 8), :], sems.at[6]),
        (bot_tn, tn_out.at[pl.ds(ns, nf), pl.ds(cz - 8, 8), :], sems.at[7]),
    ]
    stores = [pltpu.make_async_copy(*t) for t in targets]
    side(True, top_sn, top_tn)
    stores[0].start()
    stores[1].start()
    side(False, bot_sn, bot_tn)
    stores[2].start()
    stores[3].start()
    for c in stores:
        c.wait()


def local(theta, section_store, stream_speed, span_speed, conductivity, wall_layers,
          contact, spanwise_number, block_inverse):
    f32 = jnp.float32
    ny, cz, w = theta.shape
    ns = block_inverse.shape[0]
    nf = ny - ns
    nsb = ns // LB
    nfb = nf // LB
    ngz = lax.axis_size("gz")
    ngx = lax.axis_size("gx")


    solid_c = conductivity[0]
    fluid_c = conductivity[1]

    def harmonic(a, b):
        return 2.0 * a * b / (a + b)

    zero = jnp.zeros((1,), f32)
    faces = jnp.stack([
        jnp.concatenate([zero, harmonic(solid_c[:-1], solid_c[1:]), zero]),
        jnp.concatenate([zero, harmonic(solid_c[:-1], fluid_c[1:]), zero]),
        jnp.concatenate([zero, harmonic(fluid_c[:-1], fluid_c[1:]), zero]),
    ])

    smem = pl.BlockSpec(memory_space=pltpu.SMEM)
    blk = lambda off: pl.BlockSpec((LB, cz, w), lambda i: (i + off, 0, 0))
    prev_spec = lambda off: pl.BlockSpec((1, cz, w), lambda i: (jnp.maximum((i + off) * LB - 1, 0), 0, 0))
    next_spec = lambda off: pl.BlockSpec((1, cz, w), lambda i: (jnp.minimum((i + off) * LB + LB, ny - 1), 0, 0))
    edge_spec = pl.BlockSpec((1, 8, w), lambda i: (i, 0, 0))
    rows_spec = pl.BlockSpec((LB // 2, 8, w), lambda i: (i, 0, 0))

    xl, xr, ul, ur, zl, zr = pl.pallas_call(
        pack_kernel,
        grid=(1,),
        in_specs=[pl.BlockSpec((ny, cz, w), lambda i: (0, 0, 0))] * 2,
        out_specs=[pl.BlockSpec((nfb, 8, w), lambda i: (0, 0, 0))] * 4
        + [pl.BlockSpec((nf // 2, 8, w), lambda i: (0, 0, 0))] * 2,
        out_shape=[jax.ShapeDtypeStruct((nfb, 8, w), f32)] * 4
        + [jax.ShapeDtypeStruct((nf // 2, 8, w), f32)] * 2,
    )(theta, stream_speed)

    xb = lax.ppermute(xr, "gx", [(i, i + 1) for i in range(ngx - 1)])
    xa = lax.ppermute(xl, "gx", [(i + 1, i) for i in range(ngx - 1)])
    zb = lax.ppermute(zl, "gz", [(i, (i + 1) % ngz) for i in range(ngz)])
    za = lax.ppermute(zr, "gz", [((i + 1) % ngz, i) for i in range(ngz)])


    sb = 2 * LB if ns % (2 * LB) == 0 else LB
    sblk = pl.BlockSpec((sb, cz, w), lambda i: (i, 0, 0))
    sn_part, interior, spread = pl.pallas_call(
        lambda *refs: layer_kernel(False, 0, sb, *refs),
        grid=(ns // sb,),
        in_specs=[smem, smem, smem, sblk,
                  pl.BlockSpec((1, cz, w), lambda i: (jnp.maximum(i * sb - 1, 0), 0, 0)),
                  pl.BlockSpec((1, cz, w), lambda i: (jnp.minimum(i * sb + sb, ny - 1), 0, 0)),
                  sblk,
                  pl.BlockSpec((sb, cz - 1, cz - 1), lambda i: (i, 0, 0)),
                  pl.BlockSpec(memory_space=pl.ANY)],
        out_specs=[sblk, sblk, pl.BlockSpec((ngz, 3, sb, w), lambda i: (0, 0, i, 0))],
        out_shape=[
            jax.ShapeDtypeStruct((ny, cz, w), f32),
            jax.ShapeDtypeStruct((ns, cz, w), f32),
            jax.ShapeDtypeStruct((ngz, 3, ns, w), f32),
        ],
        scratch_shapes=[pltpu.VMEM((cz, w), jnp.int32), pltpu.VMEM((cz, w), f32)],
    )(faces, wall_layers, contact, theta, theta, theta, section_store, block_inverse, zr)

    number = spanwise_number
    blocks = lax.all_to_all(spread, "gz", 0, 0, tiled=True)
    left = jnp.roll(blocks[:, 2], 1, axis=0)
    targets = blocks[:, 0] + number[None, :, None] * left + number[None, :, None] * blocks[:, 1]

    square = number * number
    diagonal = 1.0 + 2.0 * number - square * (block_inverse[:, 0, 0] + block_inverse[:, -1, -1])
    beside = square * block_inverse[:, 0, -1]
    q = jnp.arange(ngz, dtype=jnp.int32)
    angle = (2.0 * math.pi / ngz) * q.astype(f32)
    denominator = diagonal[:, None] - 2.0 * beside[:, None] * jnp.cos(angle)[None, :]
    k = lax.axis_index("gz")

    def weights(shift):
        m = (q - shift) % ngz
        phase = (2.0 * math.pi / ngz) * ((q[:, None] * m[None, :]) % ngz).astype(f32)
        return jnp.sum(jnp.cos(phase)[None, :, :] / denominator[:, :, None], axis=1) / ngz

    head_values = jnp.sum(weights(k).T[:, :, None] * targets, axis=0)
    following = jnp.sum(weights(k + 1).T[:, :, None] * targets, axis=0)

    fluid_sn, fluid_tn, tiles_a, tiles_b, tiles_c, tiles_d, speed_top, speed_bot = pl.pallas_call(
        lambda *refs: layer_kernel(True, nsb, LB, *refs),
        grid=(nfb,),
        in_specs=[smem, smem, smem, blk(nsb), prev_spec(nsb), next_spec(nsb), blk(nsb),
                  blk(nsb), blk(nsb), edge_spec, edge_spec,
                  edge_spec, edge_spec, edge_spec, edge_spec,
                  pl.BlockSpec(memory_space=pl.ANY)],
        out_specs=[blk(nsb), blk(nsb)] + [pl.BlockSpec((LB, 8, w), lambda i: (i, 0, 0))] * 6,
        out_shape=[
            jax.ShapeDtypeStruct((ny, cz, w), f32),
            jax.ShapeDtypeStruct((ny, cz, w), f32),
        ] + [jax.ShapeDtypeStruct((nf, 8, w), f32)] * 6,
        scratch_shapes=[pltpu.VMEM((cz, w), jnp.int32), pltpu.VMEM((cz, w), f32),
                        pltpu.VMEM((cz + 16, w), f32)],
        input_output_aliases={15: 0},
    )(faces, wall_layers, contact, theta, theta, theta, section_store,
      stream_speed, span_speed, xb, xa, xl, xr, ul, ur, sn_part)

    anyspec = pl.BlockSpec(memory_space=pl.ANY)
    whole = lambda shape: pl.BlockSpec(shape, lambda i: (0,) * len(shape))
    fluid_sn, fluid_tn = pl.pallas_call(
        span_fix_kernel,
        grid=(1,),
        in_specs=[smem] + [whole((nf // 2, 8, w))] * 4
        + [whole((nf, 8, w))] * 6 + [anyspec, anyspec],
        out_specs=[anyspec, anyspec],
        out_shape=[jax.ShapeDtypeStruct((ny, cz, w), f32)] * 2,
        scratch_shapes=[pltpu.VMEM((nf, 8, w), f32)] * 4 + [pltpu.SemaphoreType.DMA((8,))],
        input_output_aliases={11: 0, 12: 1},
    )(wall_layers, zb, za, zl, zr, speed_top, speed_bot, tiles_a, tiles_b, tiles_c, tiles_d,
      fluid_sn, fluid_tn)

    row = jnp.arange(cz, dtype=jnp.int32)
    col0 = jnp.zeros((ns, cz), f32).at[:, 1:].set(block_inverse[:, :, 0])
    col_last = jnp.zeros((ns, cz), f32).at[:, 1:].set(block_inverse[:, :, -1])
    scale = number[:, None, None]
    solved = interior + scale * (col0[:, :, None] * head_values[:, None, :]
                                 + col_last[:, :, None] * following[:, None, :])
    solved = jnp.where((row == 0)[None, :, None], head_values[:, None, :], solved)
    theta_new = lax.dynamic_update_slice_in_dim(fluid_tn, solved, 0, 0)
    return (theta_new, fluid_sn)


def solution(mesh):
    return jax.shard_map(
        local,
        mesh=mesh,
        in_specs=(
            P(None, "gz", "gx"),
            P(None, "gz", "gx"),
            P(None, "gz", "gx"),
            P(None, "gz", "gx"),
            P(),
            P("gz"),
            P("gx"),
            P(),
            P(),
        ),
        out_specs=(P(None, "gz", "gx"), P(None, "gz", "gx")),
        check_vma=False,
    )
```

```python
import math

import jax
import jax.numpy as jnp
from jax import lax
from jax.experimental import pallas as pl
from jax.experimental.pallas import tpu as pltpu
from jax.sharding import PartitionSpec as P

keep_factor = -5.0 / 9.0
section_weight = 15.0 / 16.0
stream_courant = 0.4
span_courant = 0.4
damping = 1.0 / 256.0

LB = 8


def pack_kernel(th_ref, u_ref, xl_ref, xr_ref, ul_ref, ur_ref, zl_ref, zr_ref):
    ny, cz, w = th_ref.shape
    nblocks = xl_ref.shape[0]
    skip = ny - nblocks * LB
    lane8 = lax.broadcasted_iota(jnp.int32, (8, w), 1)
    sub8 = lax.broadcasted_iota(jnp.int32, (8, w), 0)

    def block(b, carry):
        first = skip + b * LB
        acc_l = jnp.zeros((8, w), jnp.float32)
        acc_r = jnp.zeros((8, w), jnp.float32)
        uacc_l = jnp.zeros((8, w), jnp.float32)
        uacc_r = jnp.zeros((8, w), jnp.float32)
        for s in range(LB):
            speed = u_ref[first + s].astype(jnp.float32)
            for v in range(cz // 8):
                t = th_ref[first + s, 8 * v:8 * v + 8, :]
                pos = 4 * LB * v + 4 * s
                moved = pltpu.roll(t, pos % w, 1)
                umoved = pltpu.roll(speed[8 * v:8 * v + 8], pos % w, 1)
                pick_l = jnp.logical_and(lane8 >= pos, lane8 < pos + 4)
                pick_r = jnp.logical_and(lane8 >= (pos - 4) % w, lane8 < (pos - 4) % w + 4)
                acc_l = jnp.where(pick_l, moved, acc_l)
                acc_r = jnp.where(pick_r, moved, acc_r)
                uacc_l = jnp.where(pick_l, umoved, uacc_l)
                uacc_r = jnp.where(pick_r, umoved, uacc_r)
        xl_ref[b] = acc_l
        xr_ref[b] = acc_r
        ul_ref[b] = uacc_l
        ur_ref[b] = uacc_r
        for p in range(LB // 2):
            a_hi = th_ref[first + 2 * p, cz - 8:cz, :]
            b_hi = th_ref[first + 2 * p + 1, cz - 8:cz, :]
            zl_ref[b * (LB // 2) + p] = jnp.where(sub8 < 4, pltpu.roll(a_hi, 4, 0), b_hi)
            a_lo = th_ref[first + 2 * p, 0:8, :]
            b_lo = th_ref[first + 2 * p + 1, 0:8, :]
            zr_ref[b * (LB // 2) + p] = jnp.where(sub8 < 4, a_lo, pltpu.roll(b_lo, 4, 0))
        return carry

    lax.fori_loop(0, nblocks, block, 0)


def layer_kernel(fluid, block_offset, lb, *refs):
    if fluid:
        (face_ref, wall_ref, contact_ref, th_ref, prev_ref, next_ref, st_ref,
         u_ref, v_ref, xb_ref, xa_ref, xl_ref, xr_ref, ul_ref, ur_ref,
         _alias_ref, sn_ref, tn_ref, tsn_ref, bsn_ref, ttn_ref, btn_ref,
         wallv_ref, contv_ref, ext_ref) = refs
    else:
        (face_ref, wall_ref, contact_ref, th_ref, prev_ref, next_ref, st_ref,
         bs_ref, _order_ref, sn_ref, int_ref, mine_ref, wallv_ref, contv_ref) = refs
    _, cz, w = th_ref.shape
    base = (pl.program_id(0) + block_offset) * lb

    @pl.when(pl.program_id(0) == 0)
    def _():
        sub = lax.broadcasted_iota(jnp.int32, (cz, w), 0)
        acc = jnp.zeros((cz, w), jnp.int32)
        for z in range(cz):
            acc = jnp.where(sub == z, wall_ref[z], acc)
        wallv_ref[...] = acc
        lane = lax.broadcasted_iota(jnp.int32, (cz, w), 1)
        cacc = jnp.zeros((cz, w), jnp.float32)
        for x in range(w):
            cacc = jnp.where(lane == x, contact_ref[x].astype(jnp.float32), cacc)
        contv_ref[...] = cacc

    wall = wallv_ref[...]
    contact = contv_ref[...]

    def face(y):
        both_solid = face_ref[0, y + 1]
        both_fluid = face_ref[2, y + 1]
        at_wall = face_ref[1, y + 1] * contact
        return jnp.where(y + 1 < wall, both_solid, jnp.where(y >= wall, both_fluid, at_wall))

    if fluid:
        lane = lax.broadcasted_iota(jnp.int32, (8, w), 1)
        nv = cz // 8
        slope_scale = -stream_courant / 60.0
        quarter = lane % 4
        miss_l = xb_ref[0] - xr_ref[0]
        miss_r = xa_ref[0] - xl_ref[0]

        def edge(miss, weights, left):
            acc = jnp.zeros((8, w), jnp.float32)
            for j, c in weights:
                if left:
                    term = jnp.where(quarter < j, pltpu.roll(miss, j, 1), 0.0)
                else:
                    term = jnp.where(quarter >= 4 - j, pltpu.roll(miss, w - j, 1), 0.0)
                acc = acc + c * term
            return acc

        fix_l = (slope_scale * ul_ref[0] * edge(miss_l, ((1, -45.0), (2, 9.0), (3, -1.0)), True)
                 - damping * edge(miss_l, ((1, -56.0), (2, 28.0), (3, -8.0), (4, 1.0)), True))
        fix_r = (slope_scale * ur_ref[0] * edge(miss_r, ((1, 45.0), (2, -9.0), (3, 1.0)), False)
                 - damping * edge(miss_r, ((1, -56.0), (2, 28.0), (3, -8.0), (4, 1.0)), False))

    heads = []
    face_dn = face(base - 1)
    for s in range(lb):
        y = base + s
        t = th_ref[s]
        tp = th_ref[s - 1] if s > 0 else prev_ref[0]
        tn = th_ref[s + 1] if s < lb - 1 else next_ref[0]
        face_up = face(y)
        normal = face_up * (tn - t) - face_dn * (t - tp)
        face_dn = face_up
        if fluid:
            u = u_ref[s].astype(jnp.float32)
            v = v_ref[s].astype(jnp.float32)
            xm = [None] + [pltpu.roll(t, j, 1) for j in range(1, 5)]
            xp = [None] + [pltpu.roll(t, w - j, 1) for j in range(1, 5)]
            fixes = []
            for g in range(nv):
                pos = 4 * LB * g + 4 * s
                at_l = jnp.logical_and(lane >= pos, lane < pos + 4)
                at_r = jnp.logical_and(lane >= (pos - 4) % w, lane < (pos - 4) % w + 4)
                picked = jnp.where(at_l, fix_l, jnp.where(at_r, fix_r, 0.0))
                fixes.append(pltpu.roll(picked, (w - pos) % w, 1))
            fix = jnp.concatenate(fixes, axis=0)
            ext_ref[0:8, :] = t[cz - 8:]
            ext_ref[8:8 + cz, :] = t
            ext_ref[8 + cz:16 + cz, :] = t[:8]
            zm = [None] + [ext_ref[8 - j:8 - j + cz, :] for j in range(1, 5)]
            zp = [None] + [ext_ref[8 + j:8 + j + cz, :] for j in range(1, 5)]

            def slope(m, p):
                return 45.0 * (p[1] - m[1]) - 9.0 * (p[2] - m[2]) + (p[3] - m[3])

            def smooth(m, p):
                return ((p[4] + m[4]) - 8.0 * (p[3] + m[3]) + 28.0 * (p[2] + m[2])
                        - 56.0 * (p[1] + m[1]))

            smoothing = smooth(zm, zp) + smooth(xm, xp) + 140.0 * t
            horiz = (slope_scale * (u * slope(xm, xp) + v * slope(zm, zp))
                     - damping * smoothing) + fix
            across = jnp.where(y >= wall, horiz, 0.0)
            rate = normal + across
        else:
            rate = normal
        sn = keep_factor * st_ref[s] + rate
        adv = t + section_weight * sn
        sn_ref[s] = sn
        if fluid:
            tn_ref[s] = adv
            tsn_ref[s] = sn[0:8]
            bsn_ref[s] = sn[cz - 8:]
            ttn_ref[s] = adv[0:8]
            btn_ref[s] = adv[cz - 8:]
        else:
            inner = jnp.dot(bs_ref[s], adv[1:], precision=lax.Precision.HIGHEST,
                            preferred_element_type=jnp.float32)
            inner = jnp.concatenate([jnp.zeros((1, w), jnp.float32), inner], axis=0)
            int_ref[s] = inner
            heads.append((adv[0:1, :], inner[1:2, :], inner[cz - 1:cz, :]))
    if not fluid:
        for part in range(3):
            rows = jnp.concatenate([h[part] for h in heads], axis=0)
            for n in range(mine_ref.shape[0]):
                mine_ref[n, part] = rows


def span_fix_kernel(wall_ref, zb_ref, za_ref, zl_ref, zr_ref, v_ref, ta_ref, tb_ref, tc_ref,
                    td_ref, sn_in, tn_in, sn_out, tn_out, top_sn, bot_sn, top_tn, bot_tn, sems):
    ny, cz, w = v_ref.shape
    nf = top_sn.shape[0]
    ns = ny - nf
    del sn_in, tn_in
    top_sn[...] = ta_ref[...]
    bot_sn[...] = tb_ref[...]
    top_tn[...] = tc_ref[...]
    bot_tn[...] = td_ref[...]
    sub = lax.broadcasted_iota(jnp.int32, (8, w), 0)
    wall_top = jnp.zeros((8, w), jnp.int32)
    wall_bot = jnp.zeros((8, w), jnp.int32)
    for z in range(8):
        wall_top = jnp.where(sub == z, wall_ref[z], wall_top)
        wall_bot = jnp.where(sub == z, wall_ref[cz - 8 + z], wall_bot)
    slope_scale = -span_courant / 60.0

    def side(top, sn_buf, tn_buf):
        def pair(p, carry):
            if top:
                miss = zb_ref[p] - zl_ref[p]
            else:
                miss = za_ref[p] - zr_ref[p]
            for h in range(2):
                f = 2 * p + h
                y = ns + f
                if top:
                    d = pltpu.roll(miss, 4, 0) if h == 0 else miss
                    d = jnp.where(sub >= 4, d, 0.0)
                else:
                    d = miss if h == 0 else pltpu.roll(miss, 4, 0)
                    d = jnp.where(sub < 4, d, 0.0)
                s_acc = jnp.zeros((8, w), jnp.float32)
                m_acc = jnp.zeros((8, w), jnp.float32)
                for j, cs, cm in ((1, -45.0, -56.0), (2, 9.0, 28.0), (3, -1.0, -8.0), (4, 0.0, 1.0)):
                    if top:
                        term = jnp.where(sub < j, pltpu.roll(d, j, 0), 0.0)
                    else:
                        term = jnp.where(sub >= 8 - j, pltpu.roll(d, 8 - j, 0), 0.0)
                        cs = -cs
                    if cs != 0.0:
                        s_acc = s_acc + cs * term
                    m_acc = m_acc + cm * term
                rows = slice(0, 8) if top else slice(cz - 8, cz)
                speed = v_ref[y, rows, :].astype(jnp.float32)
                wall = wall_top if top else wall_bot
                fix = jnp.where(y >= wall, slope_scale * speed * s_acc - damping * m_acc, 0.0)
                sn_buf[f] = sn_buf[f] + fix
                tn_buf[f] = tn_buf[f] + section_weight * fix
            return carry

        lax.fori_loop(0, nf // 2, pair, 0, unroll=20)

    targets = [
        (top_sn, sn_out.at[pl.ds(ns, nf), pl.ds(0, 8), :], sems.at[4]),
        (top_tn, tn_out.at[pl.ds(ns, nf), pl.ds(0, 8), :], sems.at[5]),
        (bot_sn, sn_out.at[pl.ds(ns, nf), pl.ds(cz - 8, 8), :], sems.at[6]),
        (bot_tn, tn_out.at[pl.ds(ns, nf), pl.ds(cz - 8, 8), :], sems.at[7]),
    ]
    stores = [pltpu.make_async_copy(*t) for t in targets]
    side(True, top_sn, top_tn)
    stores[0].start()
    stores[1].start()
    side(False, bot_sn, bot_tn)
    stores[2].start()
    stores[3].start()
    for c in stores:
        c.wait()


def local(theta, section_store, stream_speed, span_speed, conductivity, wall_layers,
          contact, spanwise_number, block_inverse):
    f32 = jnp.float32
    ny, cz, w = theta.shape
    ns = block_inverse.shape[0]
    nf = ny - ns
    nsb = ns // LB
    nfb = nf // LB
    ngz = lax.axis_size("gz")
    ngx = lax.axis_size("gx")


    solid_c = conductivity[0]
    fluid_c = conductivity[1]

    def harmonic(a, b):
        return 2.0 * a * b / (a + b)

    zero = jnp.zeros((1,), f32)
    faces = jnp.stack([
        jnp.concatenate([zero, harmonic(solid_c[:-1], solid_c[1:]), zero]),
        jnp.concatenate([zero, harmonic(solid_c[:-1], fluid_c[1:]), zero]),
        jnp.concatenate([zero, harmonic(fluid_c[:-1], fluid_c[1:]), zero]),
    ])

    smem = pl.BlockSpec(memory_space=pltpu.SMEM)
    blk = lambda off: pl.BlockSpec((LB, cz, w), lambda i: (i + off, 0, 0))
    prev_spec = lambda off: pl.BlockSpec((1, cz, w), lambda i: (jnp.maximum((i + off) * LB - 1, 0), 0, 0))
    next_spec = lambda off: pl.BlockSpec((1, cz, w), lambda i: (jnp.minimum((i + off) * LB + LB, ny - 1), 0, 0))
    edge_spec = pl.BlockSpec((1, 8, w), lambda i: (i, 0, 0))
    rows_spec = pl.BlockSpec((LB // 2, 8, w), lambda i: (i, 0, 0))

    xl, xr, ul, ur, zl, zr = pl.pallas_call(
        pack_kernel,
        grid=(1,),
        in_specs=[pl.BlockSpec((ny, cz, w), lambda i: (0, 0, 0))] * 2,
        out_specs=[pl.BlockSpec((nfb, 8, w), lambda i: (0, 0, 0))] * 4
        + [pl.BlockSpec((nf // 2, 8, w), lambda i: (0, 0, 0))] * 2,
        out_shape=[jax.ShapeDtypeStruct((nfb, 8, w), f32)] * 4
        + [jax.ShapeDtypeStruct((nf // 2, 8, w), f32)] * 2,
    )(theta, stream_speed)

    xb = lax.ppermute(xr, "gx", [(i, i + 1) for i in range(ngx - 1)])
    xa = lax.ppermute(xl, "gx", [(i + 1, i) for i in range(ngx - 1)])
    zb = lax.ppermute(zl, "gz", [(i, (i + 1) % ngz) for i in range(ngz)])
    za = lax.ppermute(zr, "gz", [((i + 1) % ngz, i) for i in range(ngz)])


    sb = 2 * LB if ns % (2 * LB) == 0 else LB
    sblk = pl.BlockSpec((sb, cz, w), lambda i: (i, 0, 0))
    sn_part, interior, spread = pl.pallas_call(
        lambda *refs: layer_kernel(False, 0, sb, *refs),
        grid=(ns // sb,),
        in_specs=[smem, smem, smem, sblk,
                  pl.BlockSpec((1, cz, w), lambda i: (jnp.maximum(i * sb - 1, 0), 0, 0)),
                  pl.BlockSpec((1, cz, w), lambda i: (jnp.minimum(i * sb + sb, ny - 1), 0, 0)),
                  sblk,
                  pl.BlockSpec((sb, cz - 1, cz - 1), lambda i: (i, 0, 0)),
                  pl.BlockSpec(memory_space=pl.ANY)],
        out_specs=[sblk, sblk, pl.BlockSpec((ngz, 3, sb, w), lambda i: (0, 0, i, 0))],
        out_shape=[
            jax.ShapeDtypeStruct((ny, cz, w), f32),
            jax.ShapeDtypeStruct((ns, cz, w), f32),
            jax.ShapeDtypeStruct((ngz, 3, ns, w), f32),
        ],
        scratch_shapes=[pltpu.VMEM((cz, w), jnp.int32), pltpu.VMEM((cz, w), f32)],
    )(faces, wall_layers, contact, theta, theta, theta, section_store, block_inverse, zr)

    number = spanwise_number
    blocks = lax.all_to_all(spread, "gz", 0, 0, tiled=True)
    left = jnp.roll(blocks[:, 2], 1, axis=0)
    targets = blocks[:, 0] + number[None, :, None] * left + number[None, :, None] * blocks[:, 1]

    square = number * number
    diagonal = 1.0 + 2.0 * number - square * (block_inverse[:, 0, 0] + block_inverse[:, -1, -1])
    beside = square * block_inverse[:, 0, -1]
    q = jnp.arange(ngz, dtype=jnp.int32)
    angle = (2.0 * math.pi / ngz) * q.astype(f32)
    denominator = diagonal[:, None] - 2.0 * beside[:, None] * jnp.cos(angle)[None, :]
    k = lax.axis_index("gz")

    def weights(shift):
        m = (q - shift) % ngz
        phase = (2.0 * math.pi / ngz) * ((q[:, None] * m[None, :]) % ngz).astype(f32)
        return jnp.sum(jnp.cos(phase)[None, :, :] / denominator[:, :, None], axis=1) / ngz

    head_values = jnp.sum(weights(k).T[:, :, None] * targets, axis=0)
    following = jnp.sum(weights(k + 1).T[:, :, None] * targets, axis=0)

    fluid_sn, fluid_tn, tiles_a, tiles_b, tiles_c, tiles_d = pl.pallas_call(
        lambda *refs: layer_kernel(True, nsb, LB, *refs),
        grid=(nfb,),
        in_specs=[smem, smem, smem, blk(nsb), prev_spec(nsb), next_spec(nsb), blk(nsb),
                  blk(nsb), blk(nsb), edge_spec, edge_spec,
                  edge_spec, edge_spec, edge_spec, edge_spec,
                  pl.BlockSpec(memory_space=pl.ANY)],
        out_specs=[blk(nsb), blk(nsb)] + [pl.BlockSpec((LB, 8, w), lambda i: (i, 0, 0))] * 4,
        out_shape=[
            jax.ShapeDtypeStruct((ny, cz, w), f32),
            jax.ShapeDtypeStruct((ny, cz, w), f32),
        ] + [jax.ShapeDtypeStruct((nf, 8, w), f32)] * 4,
        scratch_shapes=[pltpu.VMEM((cz, w), jnp.int32), pltpu.VMEM((cz, w), f32),
                        pltpu.VMEM((cz + 16, w), f32)],
        input_output_aliases={15: 0},
    )(faces, wall_layers, contact, theta, theta, theta, section_store,
      stream_speed, span_speed, xb, xa, xl, xr, ul, ur, sn_part)

    anyspec = pl.BlockSpec(memory_space=pl.ANY)
    whole = lambda shape: pl.BlockSpec(shape, lambda i: (0,) * len(shape))
    fluid_sn, fluid_tn = pl.pallas_call(
        span_fix_kernel,
        grid=(1,),
        in_specs=[smem] + [whole((nf // 2, 8, w))] * 4 + [whole((ny, cz, w))]
        + [whole((nf, 8, w))] * 4 + [anyspec, anyspec],
        out_specs=[anyspec, anyspec],
        out_shape=[jax.ShapeDtypeStruct((ny, cz, w), f32)] * 2,
        scratch_shapes=[pltpu.VMEM((nf, 8, w), f32)] * 4 + [pltpu.SemaphoreType.DMA((8,))],
        input_output_aliases={10: 0, 11: 1},
    )(wall_layers, zb, za, zl, zr, span_speed, tiles_a, tiles_b, tiles_c, tiles_d,
      fluid_sn, fluid_tn)

    row = jnp.arange(cz, dtype=jnp.int32)
    col0 = jnp.zeros((ns, cz), f32).at[:, 1:].set(block_inverse[:, :, 0])
    col_last = jnp.zeros((ns, cz), f32).at[:, 1:].set(block_inverse[:, :, -1])
    scale = number[:, None, None]
    solved = interior + scale * (col0[:, :, None] * head_values[:, None, :]
                                 + col_last[:, :, None] * following[:, None, :])
    solved = jnp.where((row == 0)[None, :, None], head_values[:, None, :], solved)
    theta_new = lax.dynamic_update_slice_in_dim(fluid_tn, solved, 0, 0)
    return (theta_new, fluid_sn)


def solution(mesh):
    return jax.shard_map(
        local,
        mesh=mesh,
        in_specs=(
            P(None, "gz", "gx"),
            P(None, "gz", "gx"),
            P(None, "gz", "gx"),
            P(None, "gz", "gx"),
            P(),
            P("gz"),
            P("gx"),
            P(),
            P(),
        ),
        out_specs=(P(None, "gz", "gx"), P(None, "gz", "gx")),
        check_vma=False,
    )
```

```python
import math

import jax
import jax.numpy as jnp
from jax import lax
from jax.experimental import pallas as pl
from jax.experimental.pallas import tpu as pltpu
from jax.sharding import PartitionSpec as P

keep_factor = -5.0 / 9.0
section_weight = 15.0 / 16.0
stream_courant = 0.4
span_courant = 0.4
damping = 1.0 / 256.0

LB = 8


def pack_kernel(th_ref, u_ref, xl_ref, xr_ref, ul_ref, ur_ref, zl_ref, zr_ref):
    ny, cz, w = th_ref.shape
    nblocks = xl_ref.shape[0]
    skip = ny - nblocks * LB
    lane8 = lax.broadcasted_iota(jnp.int32, (8, w), 1)
    sub8 = lax.broadcasted_iota(jnp.int32, (8, w), 0)

    def block(b, carry):
        first = skip + b * LB
        acc_l = jnp.zeros((8, w), jnp.float32)
        acc_r = jnp.zeros((8, w), jnp.float32)
        uacc_l = jnp.zeros((8, w), jnp.float32)
        uacc_r = jnp.zeros((8, w), jnp.float32)
        for s in range(LB):
            speed = u_ref[first + s].astype(jnp.float32)
            for v in range(cz // 8):
                t = th_ref[first + s, 8 * v:8 * v + 8, :]
                pos = 4 * LB * v + 4 * s
                moved = pltpu.roll(t, pos % w, 1)
                umoved = pltpu.roll(speed[8 * v:8 * v + 8], pos % w, 1)
                pick_l = jnp.logical_and(lane8 >= pos, lane8 < pos + 4)
                pick_r = jnp.logical_and(lane8 >= (pos - 4) % w, lane8 < (pos - 4) % w + 4)
                acc_l = jnp.where(pick_l, moved, acc_l)
                acc_r = jnp.where(pick_r, moved, acc_r)
                uacc_l = jnp.where(pick_l, umoved, uacc_l)
                uacc_r = jnp.where(pick_r, umoved, uacc_r)
        xl_ref[b] = acc_l
        xr_ref[b] = acc_r
        ul_ref[b] = uacc_l
        ur_ref[b] = uacc_r
        for p in range(LB // 2):
            a_hi = th_ref[first + 2 * p, cz - 8:cz, :]
            b_hi = th_ref[first + 2 * p + 1, cz - 8:cz, :]
            zl_ref[b * (LB // 2) + p] = jnp.where(sub8 < 4, pltpu.roll(a_hi, 4, 0), b_hi)
            a_lo = th_ref[first + 2 * p, 0:8, :]
            b_lo = th_ref[first + 2 * p + 1, 0:8, :]
            zr_ref[b * (LB // 2) + p] = jnp.where(sub8 < 4, a_lo, pltpu.roll(b_lo, 4, 0))
        return carry

    lax.fori_loop(0, nblocks, block, 0)


def layer_kernel(fluid, block_offset, lb, *refs):
    if fluid:
        (face_ref, wall_ref, contact_ref, th_ref, prev_ref, next_ref, st_ref,
         u_ref, v_ref, xb_ref, xa_ref, xl_ref, xr_ref, ul_ref, ur_ref,
         _alias_ref, sn_ref, tn_ref, tsn_ref, bsn_ref, ttn_ref, btn_ref,
         wallv_ref, contv_ref, ext_ref) = refs
    else:
        (face_ref, wall_ref, contact_ref, th_ref, prev_ref, next_ref, st_ref,
         bs_ref, _order_ref, sn_ref, int_ref, mine_ref, wallv_ref, contv_ref) = refs
    _, cz, w = th_ref.shape
    base = (pl.program_id(0) + block_offset) * lb

    @pl.when(pl.program_id(0) == 0)
    def _():
        sub = lax.broadcasted_iota(jnp.int32, (cz, w), 0)
        acc = jnp.zeros((cz, w), jnp.int32)
        for z in range(cz):
            acc = jnp.where(sub == z, wall_ref[z], acc)
        wallv_ref[...] = acc
        lane = lax.broadcasted_iota(jnp.int32, (cz, w), 1)
        cacc = jnp.zeros((cz, w), jnp.float32)
        for x in range(w):
            cacc = jnp.where(lane == x, contact_ref[x].astype(jnp.float32), cacc)
        contv_ref[...] = cacc

    wall = wallv_ref[...]
    contact = contv_ref[...]

    def face(y):
        both_solid = face_ref[0, y + 1]
        both_fluid = face_ref[2, y + 1]
        at_wall = face_ref[1, y + 1] * contact
        return jnp.where(y + 1 < wall, both_solid, jnp.where(y >= wall, both_fluid, at_wall))

    if fluid:
        lane = lax.broadcasted_iota(jnp.int32, (8, w), 1)
        nv = cz // 8
        slope_scale = -stream_courant / 60.0
        quarter = lane % 4
        miss_l = xb_ref[0] - xr_ref[0]
        miss_r = xa_ref[0] - xl_ref[0]

        def edge(miss, weights, left):
            acc = jnp.zeros((8, w), jnp.float32)
            for j, c in weights:
                if left:
                    term = jnp.where(quarter < j, pltpu.roll(miss, j, 1), 0.0)
                else:
                    term = jnp.where(quarter >= 4 - j, pltpu.roll(miss, w - j, 1), 0.0)
                acc = acc + c * term
            return acc

        fix_l = (slope_scale * ul_ref[0] * edge(miss_l, ((1, -45.0), (2, 9.0), (3, -1.0)), True)
                 - damping * edge(miss_l, ((1, -56.0), (2, 28.0), (3, -8.0), (4, 1.0)), True))
        fix_r = (slope_scale * ur_ref[0] * edge(miss_r, ((1, 45.0), (2, -9.0), (3, 1.0)), False)
                 - damping * edge(miss_r, ((1, -56.0), (2, 28.0), (3, -8.0), (4, 1.0)), False))

    heads = []
    face_dn = face(base - 1)
    for s in range(lb):
        y = base + s
        t = th_ref[s]
        tp = th_ref[s - 1] if s > 0 else prev_ref[0]
        tn = th_ref[s + 1] if s < lb - 1 else next_ref[0]
        face_up = face(y)
        normal = face_up * (tn - t) - face_dn * (t - tp)
        face_dn = face_up
        if fluid:
            u = u_ref[s].astype(jnp.float32)
            v = v_ref[s].astype(jnp.float32)
            xm = [None] + [pltpu.roll(t, j, 1) for j in range(1, 5)]
            xp = [None] + [pltpu.roll(t, w - j, 1) for j in range(1, 5)]
            fixes = []
            for g in range(nv):
                pos = 4 * LB * g + 4 * s
                at_l = jnp.logical_and(lane >= pos, lane < pos + 4)
                at_r = jnp.logical_and(lane >= (pos - 4) % w, lane < (pos - 4) % w + 4)
                picked = jnp.where(at_l, fix_l, jnp.where(at_r, fix_r, 0.0))
                fixes.append(pltpu.roll(picked, (w - pos) % w, 1))
            fix = jnp.concatenate(fixes, axis=0)
            ext_ref[0:8, :] = t[cz - 8:]
            ext_ref[8:8 + cz, :] = t
            ext_ref[8 + cz:16 + cz, :] = t[:8]
            zm = [None] + [ext_ref[8 - j:8 - j + cz, :] for j in range(1, 5)]
            zp = [None] + [ext_ref[8 + j:8 + j + cz, :] for j in range(1, 5)]

            def slope(m, p):
                return 45.0 * (p[1] - m[1]) - 9.0 * (p[2] - m[2]) + (p[3] - m[3])

            def smooth(m, p):
                return ((p[4] + m[4]) - 8.0 * (p[3] + m[3]) + 28.0 * (p[2] + m[2])
                        - 56.0 * (p[1] + m[1]))

            smoothing = smooth(zm, zp) + smooth(xm, xp) + 140.0 * t
            horiz = (slope_scale * (u * slope(xm, xp) + v * slope(zm, zp))
                     - damping * smoothing) + fix
            across = jnp.where(y >= wall, horiz, 0.0)
            rate = normal + across
        else:
            rate = normal
        sn = keep_factor * st_ref[s] + rate
        adv = t + section_weight * sn
        sn_ref[s] = sn
        if fluid:
            tn_ref[s] = adv
            tsn_ref[s] = sn[0:8]
            bsn_ref[s] = sn[cz - 8:]
            ttn_ref[s] = adv[0:8]
            btn_ref[s] = adv[cz - 8:]
        else:
            inner = jnp.dot(bs_ref[s], adv[1:], precision=lax.Precision.HIGHEST,
                            preferred_element_type=jnp.float32)
            inner = jnp.concatenate([jnp.zeros((1, w), jnp.float32), inner], axis=0)
            int_ref[s] = inner
            heads.append((adv[0:1, :], inner[1:2, :], inner[cz - 1:cz, :]))
    if not fluid:
        for part in range(3):
            rows = jnp.concatenate([h[part] for h in heads], axis=0)
            for n in range(mine_ref.shape[0]):
                mine_ref[n, part] = rows


def span_fix_kernel(wall_ref, zb_ref, za_ref, zl_ref, zr_ref, v_ref, ta_ref, tb_ref, tc_ref,
                    td_ref, sn_in, tn_in, sn_out, tn_out, top_sn, bot_sn, top_tn, bot_tn, sems):
    ny, cz, w = v_ref.shape
    nf = top_sn.shape[0]
    ns = ny - nf
    del sn_in, tn_in
    top_sn[...] = ta_ref[...]
    bot_sn[...] = tb_ref[...]
    top_tn[...] = tc_ref[...]
    bot_tn[...] = td_ref[...]
    sub = lax.broadcasted_iota(jnp.int32, (8, w), 0)
    wall_top = jnp.zeros((8, w), jnp.int32)
    wall_bot = jnp.zeros((8, w), jnp.int32)
    for z in range(8):
        wall_top = jnp.where(sub == z, wall_ref[z], wall_top)
        wall_bot = jnp.where(sub == z, wall_ref[cz - 8 + z], wall_bot)
    slope_scale = -span_courant / 60.0

    def side(top, sn_buf, tn_buf):
        def pair(p, carry):
            if top:
                miss = zb_ref[p] - zl_ref[p]
            else:
                miss = za_ref[p] - zr_ref[p]
            for h in range(2):
                f = 2 * p + h
                y = ns + f
                if top:
                    d = pltpu.roll(miss, 4, 0) if h == 0 else miss
                    d = jnp.where(sub >= 4, d, 0.0)
                else:
                    d = miss if h == 0 else pltpu.roll(miss, 4, 0)
                    d = jnp.where(sub < 4, d, 0.0)
                s_acc = jnp.zeros((8, w), jnp.float32)
                m_acc = jnp.zeros((8, w), jnp.float32)
                for j, cs, cm in ((1, -45.0, -56.0), (2, 9.0, 28.0), (3, -1.0, -8.0), (4, 0.0, 1.0)):
                    if top:
                        term = jnp.where(sub < j, pltpu.roll(d, j, 0), 0.0)
                    else:
                        term = jnp.where(sub >= 8 - j, pltpu.roll(d, 8 - j, 0), 0.0)
                        cs = -cs
                    if cs != 0.0:
                        s_acc = s_acc + cs * term
                    m_acc = m_acc + cm * term
                rows = slice(0, 8) if top else slice(cz - 8, cz)
                speed = v_ref[y, rows, :].astype(jnp.float32)
                wall = wall_top if top else wall_bot
                fix = jnp.where(y >= wall, slope_scale * speed * s_acc - damping * m_acc, 0.0)
                sn_buf[f] = sn_buf[f] + fix
                tn_buf[f] = tn_buf[f] + section_weight * fix
            return carry

        lax.fori_loop(0, nf // 2, pair, 0, unroll=30)

    targets = [
        (top_sn, sn_out.at[pl.ds(ns, nf), pl.ds(0, 8), :], sems.at[4]),
        (top_tn, tn_out.at[pl.ds(ns, nf), pl.ds(0, 8), :], sems.at[5]),
        (bot_sn, sn_out.at[pl.ds(ns, nf), pl.ds(cz - 8, 8), :], sems.at[6]),
        (bot_tn, tn_out.at[pl.ds(ns, nf), pl.ds(cz - 8, 8), :], sems.at[7]),
    ]
    stores = [pltpu.make_async_copy(*t) for t in targets]
    side(True, top_sn, top_tn)
    stores[0].start()
    stores[1].start()
    side(False, bot_sn, bot_tn)
    stores[2].start()
    stores[3].start()
    for c in stores:
        c.wait()


def local(theta, section_store, stream_speed, span_speed, conductivity, wall_layers,
          contact, spanwise_number, block_inverse):
    f32 = jnp.float32
    ny, cz, w = theta.shape
    ns = block_inverse.shape[0]
    nf = ny - ns
    nsb = ns // LB
    nfb = nf // LB
    ngz = lax.axis_size("gz")
    ngx = lax.axis_size("gx")


    solid_c = conductivity[0]
    fluid_c = conductivity[1]

    def harmonic(a, b):
        return 2.0 * a * b / (a + b)

    zero = jnp.zeros((1,), f32)
    faces = jnp.stack([
        jnp.concatenate([zero, harmonic(solid_c[:-1], solid_c[1:]), zero]),
        jnp.concatenate([zero, harmonic(solid_c[:-1], fluid_c[1:]), zero]),
        jnp.concatenate([zero, harmonic(fluid_c[:-1], fluid_c[1:]), zero]),
    ])

    smem = pl.BlockSpec(memory_space=pltpu.SMEM)
    blk = lambda off: pl.BlockSpec((LB, cz, w), lambda i: (i + off, 0, 0))
    prev_spec = lambda off: pl.BlockSpec((1, cz, w), lambda i: (jnp.maximum((i + off) * LB - 1, 0), 0, 0))
    next_spec = lambda off: pl.BlockSpec((1, cz, w), lambda i: (jnp.minimum((i + off) * LB + LB, ny - 1), 0, 0))
    edge_spec = pl.BlockSpec((1, 8, w), lambda i: (i, 0, 0))
    rows_spec = pl.BlockSpec((LB // 2, 8, w), lambda i: (i, 0, 0))

    xl, xr, ul, ur, zl, zr = pl.pallas_call(
        pack_kernel,
        grid=(1,),
        in_specs=[pl.BlockSpec((ny, cz, w), lambda i: (0, 0, 0))] * 2,
        out_specs=[pl.BlockSpec((nfb, 8, w), lambda i: (0, 0, 0))] * 4
        + [pl.BlockSpec((nf // 2, 8, w), lambda i: (0, 0, 0))] * 2,
        out_shape=[jax.ShapeDtypeStruct((nfb, 8, w), f32)] * 4
        + [jax.ShapeDtypeStruct((nf // 2, 8, w), f32)] * 2,
    )(theta, stream_speed)

    xb = lax.ppermute(xr, "gx", [(i, i + 1) for i in range(ngx - 1)])
    xa = lax.ppermute(xl, "gx", [(i + 1, i) for i in range(ngx - 1)])
    zb = lax.ppermute(zl, "gz", [(i, (i + 1) % ngz) for i in range(ngz)])
    za = lax.ppermute(zr, "gz", [((i + 1) % ngz, i) for i in range(ngz)])


    sb = 2 * LB if ns % (2 * LB) == 0 else LB
    sblk = pl.BlockSpec((sb, cz, w), lambda i: (i, 0, 0))
    sn_part, interior, spread = pl.pallas_call(
        lambda *refs: layer_kernel(False, 0, sb, *refs),
        grid=(ns // sb,),
        in_specs=[smem, smem, smem, sblk,
                  pl.BlockSpec((1, cz, w), lambda i: (jnp.maximum(i * sb - 1, 0), 0, 0)),
                  pl.BlockSpec((1, cz, w), lambda i: (jnp.minimum(i * sb + sb, ny - 1), 0, 0)),
                  sblk,
                  pl.BlockSpec((sb, cz - 1, cz - 1), lambda i: (i, 0, 0)),
                  pl.BlockSpec(memory_space=pl.ANY)],
        out_specs=[sblk, sblk, pl.BlockSpec((ngz, 3, sb, w), lambda i: (0, 0, i, 0))],
        out_shape=[
            jax.ShapeDtypeStruct((ny, cz, w), f32),
            jax.ShapeDtypeStruct((ns, cz, w), f32),
            jax.ShapeDtypeStruct((ngz, 3, ns, w), f32),
        ],
        scratch_shapes=[pltpu.VMEM((cz, w), jnp.int32), pltpu.VMEM((cz, w), f32)],
    )(faces, wall_layers, contact, theta, theta, theta, section_store, block_inverse, zr)

    number = spanwise_number
    blocks = lax.all_to_all(spread, "gz", 0, 0, tiled=True)
    left = jnp.roll(blocks[:, 2], 1, axis=0)
    targets = blocks[:, 0] + number[None, :, None] * left + number[None, :, None] * blocks[:, 1]

    square = number * number
    diagonal = 1.0 + 2.0 * number - square * (block_inverse[:, 0, 0] + block_inverse[:, -1, -1])
    beside = square * block_inverse[:, 0, -1]
    q = jnp.arange(ngz, dtype=jnp.int32)
    angle = (2.0 * math.pi / ngz) * q.astype(f32)
    denominator = diagonal[:, None] - 2.0 * beside[:, None] * jnp.cos(angle)[None, :]
    k = lax.axis_index("gz")

    def weights(shift):
        m = (q - shift) % ngz
        phase = (2.0 * math.pi / ngz) * ((q[:, None] * m[None, :]) % ngz).astype(f32)
        return jnp.sum(jnp.cos(phase)[None, :, :] / denominator[:, :, None], axis=1) / ngz

    head_values = jnp.sum(weights(k).T[:, :, None] * targets, axis=0)
    following = jnp.sum(weights(k + 1).T[:, :, None] * targets, axis=0)

    fluid_sn, fluid_tn, tiles_a, tiles_b, tiles_c, tiles_d = pl.pallas_call(
        lambda *refs: layer_kernel(True, nsb, LB, *refs),
        grid=(nfb,),
        in_specs=[smem, smem, smem, blk(nsb), prev_spec(nsb), next_spec(nsb), blk(nsb),
                  blk(nsb), blk(nsb), edge_spec, edge_spec,
                  edge_spec, edge_spec, edge_spec, edge_spec,
                  pl.BlockSpec(memory_space=pl.ANY)],
        out_specs=[blk(nsb), blk(nsb)] + [pl.BlockSpec((LB, 8, w), lambda i: (i, 0, 0))] * 4,
        out_shape=[
            jax.ShapeDtypeStruct((ny, cz, w), f32),
            jax.ShapeDtypeStruct((ny, cz, w), f32),
        ] + [jax.ShapeDtypeStruct((nf, 8, w), f32)] * 4,
        scratch_shapes=[pltpu.VMEM((cz, w), jnp.int32), pltpu.VMEM((cz, w), f32),
                        pltpu.VMEM((cz + 16, w), f32)],
        input_output_aliases={15: 0},
    )(faces, wall_layers, contact, theta, theta, theta, section_store,
      stream_speed, span_speed, xb, xa, xl, xr, ul, ur, sn_part)

    anyspec = pl.BlockSpec(memory_space=pl.ANY)
    whole = lambda shape: pl.BlockSpec(shape, lambda i: (0,) * len(shape))
    fluid_sn, fluid_tn = pl.pallas_call(
        span_fix_kernel,
        grid=(1,),
        in_specs=[smem] + [whole((nf // 2, 8, w))] * 4 + [whole((ny, cz, w))]
        + [whole((nf, 8, w))] * 4 + [anyspec, anyspec],
        out_specs=[anyspec, anyspec],
        out_shape=[jax.ShapeDtypeStruct((ny, cz, w), f32)] * 2,
        scratch_shapes=[pltpu.VMEM((nf, 8, w), f32)] * 4 + [pltpu.SemaphoreType.DMA((8,))],
        input_output_aliases={10: 0, 11: 1},
    )(wall_layers, zb, za, zl, zr, span_speed, tiles_a, tiles_b, tiles_c, tiles_d,
      fluid_sn, fluid_tn)

    row = jnp.arange(cz, dtype=jnp.int32)
    col0 = jnp.zeros((ns, cz), f32).at[:, 1:].set(block_inverse[:, :, 0])
    col_last = jnp.zeros((ns, cz), f32).at[:, 1:].set(block_inverse[:, :, -1])
    scale = number[:, None, None]
    solved = interior + scale * (col0[:, :, None] * head_values[:, None, :]
                                 + col_last[:, :, None] * following[:, None, :])
    solved = jnp.where((row == 0)[None, :, None], head_values[:, None, :], solved)
    theta_new = lax.dynamic_update_slice_in_dim(fluid_tn, solved, 0, 0)
    return (theta_new, fluid_sn)


def solution(mesh):
    return jax.shard_map(
        local,
        mesh=mesh,
        in_specs=(
            P(None, "gz", "gx"),
            P(None, "gz", "gx"),
            P(None, "gz", "gx"),
            P(None, "gz", "gx"),
            P(),
            P("gz"),
            P("gx"),
            P(),
            P(),
        ),
        out_specs=(P(None, "gz", "gx"), P(None, "gz", "gx")),
        check_vma=False,
    )
```
